32 devices in a mesh: row: 4 (over z), col: 8 (over y, x, core).
Axes of the slice: x: 2, y: 2, z: 4, core: 2. Of those that a mesh axis runs over, the one named last changes fastest.
Arguments:
- latent: bfloat16 [128, 256, 512], P('row', 'col'), may hold values from -6 to 6
- bn_scale: float32 [512], replicated, may hold values from 0.5 to 2
- bn_shift: float32 [512], replicated, may hold values from -3 to 3
- w_expand: bfloat16 [512, 2048], replicated, may hold values from -0.25 to 0.25
- b_expand: float32 [2048], replicated, may hold values from -3 to 3
- dw_kernel: bfloat16 [3, 3, 2048], replicated, may hold values from -2 to 2
- dw_bias: float32 [2048], replicated, may hold values from -3 to 3
- w_project: bfloat16 [2048, 512], replicated, may hold values from -0.125 to 0.125
- b_project: float32 [512], replicated, may hold values from -3 to 3
- ln_gain: float32 [512], replicated, may hold values from 0.5 to 1.5
- ln_bias: float32 [512], replicated, may hold values from -3 to 3
- w_qkv: bfloat16 [512, 1536], replicated, may hold values from -0.25 to 0.25
- pos_bias: float32 [16, 64, 64], replicated, may hold values from -400 to 400
- w_out: bfloat16 [512, 512], replicated, may hold values from -0.25 to 0.25
- b_out: float32 [512], replicated, may hold values from -3 to 3
Outputs:
- block_out: bfloat16 [128, 256, 512], P('row', 'col')
The draws below stay inside these ranges and needn't reach their ends.
All inputs are finite; a program needn't handle non-finite values.
Results may differ from the reference program's by a relative error of at most 0.0065.
Values may be sent and summed in bfloat16 or wider, within the bound.
No kernel may reach another device: no remote copies, remote signals or barrier semaphores. Data moves between devices by JAX's collectives and lax.ppermute only.
A program may use at most 64 MiB of HBM per device.

```python
import math
import jax
import jax.numpy as jnp
from jax import lax

WIDTH = 512
HEADS = 16
INNER = 2048
GRID = 8
GROUP_TOK = 64
TILE_H = 32
IMG_H = 128
IMG_W = 256
STRIDE_H = 16
STRIDE_W = 32


def draw_pos_bias(key, part):
    keys = jax.random.split(key, 1)
    shape = (HEADS, GROUP_TOK, GROUP_TOK)
    return jnp.clip(1.5 * jax.random.normal(keys[0], shape, jnp.float32), -6.0, 6.0)


def block_levels(rng, extent, shards, low, largest):
    loudness, own = 1.0, jax.random.fold_in(rng, 6)
    for position, blocks in shards:
        steps = jnp.exp(jax.random.uniform(jax.random.fold_in(own, position), (blocks,), jnp.float32, low / len(shards), largest / len(shards)))
        loudness = loudness * jnp.repeat(steps, extent[position] // blocks).reshape([-1 if axis == position else 1 for axis in range(len(extent))])
    return loudness


def gaussian(own_key, extent, scale, bound, shards=(), kind=jnp.bfloat16):
    values = jax.random.normal(own_key, extent, jnp.float32) * scale
    if len(shards) > 0:
        values = block_levels(own_key, extent, shards, -0.22, 0.18) * values
    return jnp.clip(values, min=-bound, max=bound).astype(kind)


def setup_inputs(seed: int = 0) -> dict:
    streams_of = jax.random.split(jax.random.key(seed), 16)
    return {
        "latent": gaussian(streams_of[0], (IMG_H, IMG_W, WIDTH), 1.0, 6.0, ((0, 4), (1, 8))),
        "bn_scale": jnp.clip(jnp.exp(jax.random.uniform(streams_of[1], (WIDTH,), jnp.float32, math.log(0.5), math.log(2.0))), 0.5, 2.0),
        "bn_shift": gaussian(streams_of[2], (WIDTH,), 0.5, 3.0, (), jnp.float32),
        "w_expand": gaussian(streams_of[3], (WIDTH, INNER), WIDTH ** -0.5, 0.25),
        "b_expand": gaussian(streams_of[4], (INNER,), 0.5, 3.0, (), jnp.float32),
        "dw_kernel": gaussian(streams_of[5], (3, 3, INNER), 9 ** -0.5, 2.0),
        "dw_bias": gaussian(streams_of[6], (INNER,), 0.5, 3.0, (), jnp.float32),
        "w_project": gaussian(streams_of[7], (INNER, WIDTH), INNER ** -0.5, 0.125),
        "b_project": gaussian(streams_of[8], (WIDTH,), 0.5, 3.0, (), jnp.float32),
        "ln_gain": jnp.clip(jax.random.uniform(streams_of[9], (WIDTH,), jnp.float32, 0.5, 1.5), 0.5, 1.5),
        "ln_bias": gaussian(streams_of[10], (WIDTH,), 0.5, 3.0, (), jnp.float32),
        "w_qkv": gaussian(streams_of[11], (WIDTH, 3 * WIDTH), WIDTH ** -0.5, 0.25),
        "pos_bias": draw_pos_bias(jax.random.fold_in(streams_of[15], 71), 0),
        "w_out": gaussian(streams_of[13], (WIDTH, WIDTH), WIDTH ** -0.5, 0.25),
        "b_out": gaussian(streams_of[14], (WIDTH,), 0.5, 3.0, (), jnp.float32),
    }


def gelu_tanh(v):
    return jax.nn.gelu(v, approximate=True)

def attend(qkv, pos_bias):
    groups, members, three = qkv.shape
    width = three // 3
    head_dim = width // HEADS
    query = qkv[:, :, :width].reshape(groups, members, HEADS, head_dim).astype(jnp.float32)
    keys = qkv[:, :, width:2 * width].reshape(groups, members, HEADS, head_dim).astype(jnp.float32)
    values = qkv[:, :, 2 * width:].reshape(groups, members, HEADS, head_dim).astype(jnp.float32)
    scores = jnp.einsum('gihd,gjhd->ghij', query, keys) * head_dim ** (-0.5) + pos_bias[None]
    top = lax.optimization_barrier(jnp.max(scores, axis=-1, keepdims=True))
    expo = jnp.exp(scores - top)
    probs = (expo / lax.optimization_barrier(jnp.sum(expo, axis=-1, keepdims=True))).astype(jnp.bfloat16)
    mixed = jnp.einsum('ghij,gjhd->gihd', probs.astype(jnp.float32), values)
    return mixed.astype(jnp.bfloat16).reshape(groups, members, width)

def reference(latent, bn_scale, bn_shift, w_expand, b_expand, dw_kernel, dw_bias, w_project, b_project, ln_gain, ln_bias, w_qkv, pos_bias, w_out, b_out):
    padded_in = jnp.pad(latent, ((1, 1), (0, 0), (0, 0)))

    def conv_band(start):
        rows = lax.dynamic_slice_in_dim(padded_in, start, TILE_H + 2, 0)
        normed_in = (rows.astype(jnp.float32) * bn_scale + bn_shift).astype(jnp.bfloat16)
        hidden = jnp.dot(normed_in.reshape(-1, WIDTH), w_expand, preferred_element_type=jnp.float32) + b_expand
        hidden = gelu_tanh(hidden).astype(jnp.bfloat16).reshape(TILE_H + 2, IMG_W, INNER)
        global_rows = start - 1 + jnp.arange(TILE_H + 2, dtype=jnp.int32)
        inside = (global_rows >= 0) & (global_rows < IMG_H)
        hidden = jnp.where(inside[:, None, None], hidden, jnp.zeros_like(hidden))
        hidden = jnp.pad(hidden, ((0, 0), (1, 1), (0, 0)))
        total = jnp.zeros((TILE_H, IMG_W, INNER), jnp.float32)
        for down in range(3):
            for across in range(3):
                total = total + hidden[down:down + TILE_H, across:across + IMG_W].astype(jnp.float32) * dw_kernel[down, across].astype(jnp.float32)
        depth = gelu_tanh(total + dw_bias).astype(jnp.bfloat16)
        proj = jnp.dot(depth.reshape(-1, INNER), w_project, preferred_element_type=jnp.float32).reshape(TILE_H, IMG_W, WIDTH)
        return (rows[1:-1].astype(jnp.float32) + proj + b_project).astype(jnp.bfloat16)
    starts = jnp.arange(IMG_H // TILE_H, dtype=jnp.int32) * TILE_H
    mid = lax.map(conv_band, starts).reshape(IMG_H, IMG_W, WIDTH)
    mid_grid = mid.reshape(GRID, STRIDE_H, IMG_W, WIDTH)

    def grid_rows(offset):
        rows = lax.dynamic_index_in_dim(mid_grid, offset, axis=1, keepdims=False)
        grouped = rows.reshape(GRID, GRID, STRIDE_W, WIDTH).transpose(2, 0, 1, 3).reshape(STRIDE_W, GROUP_TOK, WIDTH)
        values = grouped.astype(jnp.float32)
        mean = lax.optimization_barrier(jnp.mean(values, axis=-1, keepdims=True))
        var = lax.optimization_barrier(jnp.mean(jnp.square(values - mean), axis=-1, keepdims=True))
        normed = ((values - mean) * lax.rsqrt(var + 1e-05) * ln_gain + ln_bias).astype(jnp.bfloat16)
        qkv = jnp.dot(normed.reshape(-1, WIDTH), w_qkv, preferred_element_type=jnp.float32).astype(jnp.bfloat16)
        attended = attend(qkv.reshape(STRIDE_W, GROUP_TOK, 3 * WIDTH), pos_bias)
        result = values.reshape(-1, WIDTH) + jnp.dot(attended.reshape(-1, WIDTH), w_out, preferred_element_type=jnp.float32) + b_out
        result = result.astype(jnp.bfloat16).reshape(STRIDE_W, GRID, GRID, WIDTH)
        return result.transpose(1, 2, 0, 3).reshape(GRID, IMG_W, WIDTH)
    offsets = jnp.arange(STRIDE_H, dtype=jnp.int32)
    stacked = lax.map(grid_rows, offsets)
    return stacked.transpose(1, 0, 2, 3).reshape(IMG_H, IMG_W, WIDTH)
```

```python
import jax
import jax.numpy as jnp
from jax import lax
from jax.sharding import PartitionSpec as P

HEADS = 16
GRID = 8


def extended(block, sides, width):
    for axis, dim in sides:
        count = lax.axis_size(axis)
        forward = [(i, i + 1) for i in range(count - 1)]
        backward = [(target, source) for source, target in forward]
        low = lax.ppermute(
            lax.slice_in_dim(block, block.shape[dim] - width, None, axis=dim), axis, forward
        )
        high = lax.ppermute(lax.slice_in_dim(block, 0, width, axis=dim), axis, backward)
        block = jnp.concatenate([low, block, high], axis=dim)
    return block


def gelu_tanh(v):
    return jax.nn.gelu(v, approximate=True)


def layout_sizes(tile_h, tile_w):
    n_row = lax.axis_size("row")
    n_col = lax.axis_size("col")
    stride_h = tile_h * n_row // GRID
    stride_w = tile_w * n_col // GRID
    part_h = min(tile_h, stride_h)
    part_w = min(tile_w, stride_w)
    return dict(
        n_row=n_row,
        n_col=n_col,
        pr=tile_h // part_h,
        kr=part_h // n_row,
        qr=stride_h // part_h,
        pc=tile_w // part_w,
        kc=part_w // n_col,
        qc=stride_w // part_w,
    )


def to_owner(tile, sizes):
    tile_h, tile_w, feats = tile.shape
    message = sizes["pr"] * sizes["kr"] * sizes["pc"] * sizes["kc"]
    outgoing = tile.reshape(
        sizes["pr"], sizes["n_row"], sizes["kr"], sizes["pc"], sizes["n_col"], sizes["kc"], feats
    ).transpose(1, 4, 0, 2, 3, 5, 6)
    arrived = lax.all_to_all(
        outgoing.reshape(sizes["n_row"] * sizes["n_col"], message, feats),
        ("row", "col"),
        split_axis=0,
        concat_axis=0,
        tiled=True,
    )
    arrived = arrived.reshape(
        sizes["n_row"] // sizes["qr"],
        sizes["qr"],
        sizes["n_col"] // sizes["qc"],
        sizes["qc"],
        sizes["pr"],
        sizes["kr"],
        sizes["pc"],
        sizes["kc"],
        feats,
    )
    arrived = arrived.transpose(1, 5, 3, 7, 0, 4, 2, 6, 8)
    return arrived.reshape(
        sizes["qr"] * sizes["kr"] * sizes["qc"] * sizes["kc"], GRID * GRID, feats
    )


def to_home(grouped, sizes, tile_h, tile_w):
    feats = grouped.shape[-1]
    message = sizes["pr"] * sizes["kr"] * sizes["pc"] * sizes["kc"]
    outgoing = grouped.reshape(
        sizes["qr"],
        sizes["kr"],
        sizes["qc"],
        sizes["kc"],
        sizes["n_row"] // sizes["qr"],
        sizes["pr"],
        sizes["n_col"] // sizes["qc"],
        sizes["pc"],
        feats,
    )
    outgoing = outgoing.transpose(4, 0, 6, 2, 5, 1, 7, 3, 8)
    back = lax.all_to_all(
        outgoing.reshape(sizes["n_row"] * sizes["n_col"], message, feats),
        ("row", "col"),
        split_axis=0,
        concat_axis=0,
        tiled=True,
    )
    back = back.reshape(
        sizes["n_row"], sizes["n_col"], sizes["pr"], sizes["kr"], sizes["pc"], sizes["kc"], feats
    ).transpose(2, 0, 3, 4, 1, 5, 6)
    return back.reshape(tile_h, tile_w, feats)


def attend(qkv, pos_bias):
    groups, members, three = qkv.shape
    width = three // 3
    head_dim = width // HEADS
    query = qkv[:, :, :width].reshape(groups, members, HEADS, head_dim)
    keys = qkv[:, :, width : 2 * width].reshape(groups, members, HEADS, head_dim)
    values = qkv[:, :, 2 * width :].reshape(groups, members, HEADS, head_dim)
    scores = (
        jnp.einsum("gihd,gjhd->ghij", query, keys, preferred_element_type=jnp.float32)
        * head_dim ** (-0.5)
        + pos_bias[None]
    )
    top = jnp.max(scores, axis=-1, keepdims=True)
    expo = jnp.exp(scores - top)
    probs = (expo / jnp.sum(expo, axis=-1, keepdims=True)).astype(jnp.bfloat16)
    mixed = jnp.einsum("ghij,gjhd->gihd", probs, values, preferred_element_type=jnp.float32)
    return mixed.astype(jnp.bfloat16).reshape(groups, members, width)


def on_device(
    latent,
    bn_scale,
    bn_shift,
    w_expand,
    b_expand,
    dw_kernel,
    dw_bias,
    w_project,
    b_project,
    ln_gain,
    ln_bias,
    w_qkv,
    pos_bias,
    w_out,
    b_out,
):
    tile_h, tile_w, width = latent.shape
    hidden_width = w_expand.shape[1]
    rows_here = latent.shape[0]
    cols_here = latent.shape[1]
    normed_in = (latent.astype(jnp.float32) * bn_scale + bn_shift).astype(jnp.bfloat16)
    hidden = (
        jnp.dot(normed_in.reshape(-1, width), w_expand, preferred_element_type=jnp.float32)
        + b_expand
    )
    padded = extended(
        gelu_tanh(hidden).astype(jnp.bfloat16).reshape(rows_here, cols_here, hidden_width),
        (("row", 0), ("col", 1)),
        1,
    )
    total = jnp.zeros((tile_h, tile_w, hidden_width), jnp.float32)
    for down in range(3):
        for across in range(3):
            total = total + padded[down : down + tile_h, across : across + tile_w].astype(
                jnp.float32
            ) * dw_kernel[down, across].astype(jnp.float32)
    depth = gelu_tanh(total + dw_bias).astype(jnp.bfloat16)
    proj = jnp.dot(depth.reshape(-1, hidden_width), w_project, preferred_element_type=jnp.float32)
    mid = (latent.reshape(-1, width).astype(jnp.float32) + proj + b_project).astype(jnp.bfloat16)
    sizes = layout_sizes(tile_h, tile_w)
    grouped_mid = to_owner(mid.reshape(tile_h, tile_w, width), sizes)
    groups_here, members, _ = grouped_mid.shape
    values = grouped_mid.reshape(-1, width).astype(jnp.float32)
    mean = jnp.mean(values, axis=-1, keepdims=True)
    var = jnp.mean(jnp.square(values - mean), axis=-1, keepdims=True)
    normed = ((values - mean) * lax.rsqrt(var + 1e-05) * ln_gain + ln_bias).astype(jnp.bfloat16)
    qkv = jnp.dot(normed, w_qkv, preferred_element_type=jnp.float32).astype(jnp.bfloat16)
    attended = attend(qkv.reshape(groups_here, members, 3 * width), pos_bias).reshape(-1, width)
    result = values + jnp.dot(attended, w_out, preferred_element_type=jnp.float32) + b_out
    result = result.astype(jnp.bfloat16).reshape(groups_here, members, width)
    return to_home(result, sizes, tile_h, tile_w)


def solution(mesh):
    return jax.shard_map(
        on_device,
        mesh=mesh,
        in_specs=(
            P("row", "col", None),
            P(),
            P(),
            P(),
            P(),
            P(),
            P(),
            P(),
            P(),
            P(),
            P(),
            P(),
            P(),
            P(),
            P(),
        ),
        out_specs=P("row", "col", None),
        check_vma=False,
    )
```

```python
import jax
import jax.numpy as jnp
from jax import lax
from jax.sharding import PartitionSpec as P

HEADS = 16
GRID = 8


def shifted(x, down, across):
    n_row = lax.axis_size("row")
    n_col = lax.axis_size("col")
    pairs = []
    for i in range(n_row):
        for j in range(n_col):
            if 0 <= i + down < n_row and 0 <= j + across < n_col:
                pairs.append((i * n_col + j, (i + down) * n_col + j + across))
    return lax.ppermute(x, ("row", "col"), pairs)


def halo(block):
    up = shifted(block[-1:], 1, 0)
    down = shifted(block[:1], -1, 0)
    left = shifted(block[:, -1:], 0, 1)
    right = shifted(block[:, :1], 0, -1)
    up_left = shifted(block[-1:, -1:], 1, 1)
    up_right = shifted(block[-1:, :1], 1, -1)
    down_left = shifted(block[:1, -1:], -1, 1)
    down_right = shifted(block[:1, :1], -1, -1)
    return up, down, left, right, up_left, up_right, down_left, down_right


def gelu_tanh(v):
    return jax.nn.gelu(v, approximate=True)


def layout_sizes(tile_h, tile_w):
    n_row = lax.axis_size("row")
    n_col = lax.axis_size("col")
    stride_h = tile_h * n_row // GRID
    stride_w = tile_w * n_col // GRID
    part_h = min(tile_h, stride_h)
    part_w = min(tile_w, stride_w)
    return dict(
        n_row=n_row,
        n_col=n_col,
        pr=tile_h // part_h,
        kr=part_h // n_row,
        qr=stride_h // part_h,
        pc=tile_w // part_w,
        kc=part_w // n_col,
        qc=stride_w // part_w,
    )


def to_owner(tile, sizes):
    tile_h, tile_w, feats = tile.shape
    message = sizes["pr"] * sizes["kr"] * sizes["pc"] * sizes["kc"]
    outgoing = tile.reshape(
        sizes["pr"], sizes["n_row"], sizes["kr"], sizes["pc"], sizes["n_col"], sizes["kc"], feats
    ).transpose(1, 4, 0, 2, 3, 5, 6)
    arrived = lax.all_to_all(
        outgoing.reshape(sizes["n_row"] * sizes["n_col"], message, feats),
        ("row", "col"),
        split_axis=0,
        concat_axis=0,
        tiled=True,
    )
    arrived = arrived.reshape(
        sizes["n_row"] // sizes["qr"],
        sizes["qr"],
        sizes["n_col"] // sizes["qc"],
        sizes["qc"],
        sizes["pr"],
        sizes["kr"],
        sizes["pc"],
        sizes["kc"],
        feats,
    )
    arrived = arrived.transpose(1, 5, 3, 7, 0, 4, 2, 6, 8)
    return arrived.reshape(
        sizes["qr"] * sizes["kr"] * sizes["qc"] * sizes["kc"], GRID * GRID, feats
    )


def to_home(grouped, sizes, tile_h, tile_w):
    feats = grouped.shape[-1]
    message = sizes["pr"] * sizes["kr"] * sizes["pc"] * sizes["kc"]
    outgoing = grouped.reshape(
        sizes["qr"],
        sizes["kr"],
        sizes["qc"],
        sizes["kc"],
        sizes["n_row"] // sizes["qr"],
        sizes["pr"],
        sizes["n_col"] // sizes["qc"],
        sizes["pc"],
        feats,
    )
    outgoing = outgoing.transpose(4, 0, 6, 2, 5, 1, 7, 3, 8)
    back = lax.all_to_all(
        outgoing.reshape(sizes["n_row"] * sizes["n_col"], message, feats),
        ("row", "col"),
        split_axis=0,
        concat_axis=0,
        tiled=True,
    )
    back = back.reshape(
        sizes["n_row"], sizes["n_col"], sizes["pr"], sizes["kr"], sizes["pc"], sizes["kc"], feats
    ).transpose(2, 0, 3, 4, 1, 5, 6)
    return back.reshape(tile_h, tile_w, feats)


def attend(qkv, pos_bias):
    groups, members, three = qkv.shape
    width = three // 3
    head_dim = width // HEADS
    query = qkv[:, :, :width].reshape(groups, members, HEADS, head_dim)
    keys = qkv[:, :, width : 2 * width].reshape(groups, members, HEADS, head_dim)
    values = qkv[:, :, 2 * width :].reshape(groups, members, HEADS, head_dim)
    scores = (
        jnp.einsum("gihd,gjhd->ghij", query, keys, preferred_element_type=jnp.float32)
        * head_dim ** (-0.5)
        + pos_bias[None]
    )
    top = jnp.max(scores, axis=-1, keepdims=True)
    expo = jnp.exp(scores - top)
    probs = (expo / jnp.sum(expo, axis=-1, keepdims=True)).astype(jnp.bfloat16)
    mixed = jnp.einsum("ghij,gjhd->gihd", probs, values, preferred_element_type=jnp.float32)
    return mixed.astype(jnp.bfloat16).reshape(groups, members, width)


def on_device(
    latent,
    bn_scale,
    bn_shift,
    w_expand,
    b_expand,
    dw_kernel,
    dw_bias,
    w_project,
    b_project,
    ln_gain,
    ln_bias,
    w_qkv,
    pos_bias,
    w_out,
    b_out,
):
    tile_h, tile_w, width = latent.shape
    hidden_width = w_expand.shape[1]
    rows_here = latent.shape[0]
    cols_here = latent.shape[1]
    def expand(pixels):
        normed_in = (pixels.astype(jnp.float32) * bn_scale + bn_shift).astype(jnp.bfloat16)
        hidden = (
            jnp.dot(normed_in.reshape(-1, width), w_expand, preferred_element_type=jnp.float32)
            + b_expand
        )
        return gelu_tanh(hidden).astype(jnp.bfloat16)

    up, down, left, right, up_left, up_right, down_left, down_right = halo(latent)
    inner = expand(latent).reshape(rows_here, cols_here, hidden_width)
    rim = jnp.concatenate(
        [
            jnp.concatenate([up_left, up, up_right], axis=1).reshape(-1, width),
            jnp.concatenate([down_left, down, down_right], axis=1).reshape(-1, width),
            left.reshape(-1, width),
            right.reshape(-1, width),
        ],
        axis=0,
    )
    rim = expand(rim)
    wide = cols_here + 2
    top = rim[:wide].reshape(1, wide, hidden_width)
    bottom = rim[wide : 2 * wide].reshape(1, wide, hidden_width)
    west = rim[2 * wide : 2 * wide + rows_here].reshape(rows_here, 1, hidden_width)
    east = rim[2 * wide + rows_here :].reshape(rows_here, 1, hidden_width)
    padded = jnp.concatenate(
        [top, jnp.concatenate([west, inner, east], axis=1), bottom], axis=0
    )
    row_at = lax.axis_index("row") * rows_here - 1 + jnp.arange(rows_here + 2)
    col_at = lax.axis_index("col") * cols_here - 1 + jnp.arange(wide)
    inside = ((row_at >= 0) & (row_at < lax.axis_size("row") * rows_here))[:, None] & (
        (col_at >= 0) & (col_at < lax.axis_size("col") * cols_here)
    )[None, :]
    padded = jnp.where(inside[:, :, None], padded, jnp.zeros_like(padded))
    total = jnp.zeros((tile_h, tile_w, hidden_width), jnp.float32)
    for down in range(3):
        for across in range(3):
            total = total + padded[down : down + tile_h, across : across + tile_w].astype(
                jnp.float32
            ) * dw_kernel[down, across].astype(jnp.float32)
    depth = gelu_tanh(total + dw_bias).astype(jnp.bfloat16)
    proj = jnp.dot(depth.reshape(-1, hidden_width), w_project, preferred_element_type=jnp.float32)
    mid = (latent.reshape(-1, width).astype(jnp.float32) + proj + b_project).astype(jnp.bfloat16)
    sizes = layout_sizes(tile_h, tile_w)
    grouped_mid = to_owner(mid.reshape(tile_h, tile_w, width), sizes)
    groups_here, members, _ = grouped_mid.shape
    values = grouped_mid.reshape(-1, width).astype(jnp.float32)
    mean = jnp.mean(values, axis=-1, keepdims=True)
    var = jnp.mean(jnp.square(values - mean), axis=-1, keepdims=True)
    normed = ((values - mean) * lax.rsqrt(var + 1e-05) * ln_gain + ln_bias).astype(jnp.bfloat16)
    qkv = jnp.dot(normed, w_qkv, preferred_element_type=jnp.float32).astype(jnp.bfloat16)
    attended = attend(qkv.reshape(groups_here, members, 3 * width), pos_bias).reshape(-1, width)
    result = values + jnp.dot(attended, w_out, preferred_element_type=jnp.float32) + b_out
    result = result.astype(jnp.bfloat16).reshape(groups_here, members, width)
    return to_home(result, sizes, tile_h, tile_w)


def solution(mesh):
    return jax.shard_map(
        on_device,
        mesh=mesh,
        in_specs=(
            P("row", "col", None),
            P(),
            P(),
            P(),
            P(),
            P(),
            P(),
            P(),
            P(),
            P(),
            P(),
            P(),
            P(),
            P(),
            P(),
        ),
        out_specs=P("row", "col", None),
        check_vma=False,
    )
```

```python
import math

import jax
import jax.numpy as jnp
from jax import lax
from jax.sharding import PartitionSpec as P
from jax.experimental import pallas as pl
from jax.experimental.pallas import tpu as pltpu

HEADS = 16
GRID = 8


def extended(block, sides, width):
    for axis, dim in sides:
        count = lax.axis_size(axis)
        forward = [(i, i + 1) for i in range(count - 1)]
        backward = [(target, source) for source, target in forward]
        low = lax.ppermute(
            lax.slice_in_dim(block, block.shape[dim] - width, None, axis=dim), axis, forward
        )
        high = lax.ppermute(lax.slice_in_dim(block, 0, width, axis=dim), axis, backward)
        block = jnp.concatenate([low, block, high], axis=dim)
    return block


def gelu_tanh(v):
    return jax.nn.gelu(v, approximate=True)


def layout_sizes(tile_h, tile_w):
    n_row = lax.axis_size("row")
    n_col = lax.axis_size("col")
    stride_h = tile_h * n_row // GRID
    stride_w = tile_w * n_col // GRID
    part_h = min(tile_h, stride_h)
    part_w = min(tile_w, stride_w)
    return dict(
        n_row=n_row,
        n_col=n_col,
        pr=tile_h // part_h,
        kr=part_h // n_row,
        qr=stride_h // part_h,
        pc=tile_w // part_w,
        kc=part_w // n_col,
        qc=stride_w // part_w,
    )


def to_owner(tile, sizes):
    tile_h, tile_w, feats = tile.shape
    message = sizes["pr"] * sizes["kr"] * sizes["pc"] * sizes["kc"]
    outgoing = tile.reshape(
        sizes["pr"], sizes["n_row"], sizes["kr"], sizes["pc"], sizes["n_col"], sizes["kc"], feats
    ).transpose(1, 4, 0, 2, 3, 5, 6)
    arrived = lax.all_to_all(
        outgoing.reshape(sizes["n_row"] * sizes["n_col"], message, feats),
        ("row", "col"),
        split_axis=0,
        concat_axis=0,
        tiled=True,
    )
    arrived = arrived.reshape(
        sizes["n_row"] // sizes["qr"],
        sizes["qr"],
        sizes["n_col"] // sizes["qc"],
        sizes["qc"],
        sizes["pr"],
        sizes["kr"],
        sizes["pc"],
        sizes["kc"],
        feats,
    )
    arrived = arrived.transpose(1, 5, 3, 7, 0, 4, 2, 6, 8)
    return arrived.reshape(
        sizes["qr"] * sizes["kr"] * sizes["qc"] * sizes["kc"], GRID * GRID, feats
    )


def to_home(grouped, sizes, tile_h, tile_w):
    feats = grouped.shape[-1]
    message = sizes["pr"] * sizes["kr"] * sizes["pc"] * sizes["kc"]
    outgoing = grouped.reshape(
        sizes["qr"],
        sizes["kr"],
        sizes["qc"],
        sizes["kc"],
        sizes["n_row"] // sizes["qr"],
        sizes["pr"],
        sizes["n_col"] // sizes["qc"],
        sizes["pc"],
        feats,
    )
    outgoing = outgoing.transpose(4, 0, 6, 2, 5, 1, 7, 3, 8)
    back = lax.all_to_all(
        outgoing.reshape(sizes["n_row"] * sizes["n_col"], message, feats),
        ("row", "col"),
        split_axis=0,
        concat_axis=0,
        tiled=True,
    )
    back = back.reshape(
        sizes["n_row"], sizes["n_col"], sizes["pr"], sizes["kr"], sizes["pc"], sizes["kc"], feats
    ).transpose(2, 0, 3, 4, 1, 5, 6)
    return back.reshape(tile_h, tile_w, feats)


def attend(qkv, pos_bias):
    groups, members, three = qkv.shape
    width = three // 3
    head_dim = width // HEADS
    query = qkv[:, :, :width].reshape(groups, members, HEADS, head_dim)
    keys = qkv[:, :, width : 2 * width].reshape(groups, members, HEADS, head_dim)
    values = qkv[:, :, 2 * width :].reshape(groups, members, HEADS, head_dim)
    scores = (
        jnp.einsum("gihd,gjhd->ghij", query, keys, preferred_element_type=jnp.float32)
        * head_dim ** (-0.5)
        + pos_bias[None]
    )
    top = jnp.max(scores, axis=-1, keepdims=True)
    expo = jnp.exp(scores - top)
    probs = (expo / jnp.sum(expo, axis=-1, keepdims=True)).astype(jnp.bfloat16)
    mixed = jnp.einsum("ghij,gjhd->gihd", probs, values, preferred_element_type=jnp.float32)
    return mixed.astype(jnp.bfloat16).reshape(groups, members, width)


def owner_kernel(mid_ref, gain_ref, bias_ref, wqkv_ref, pos_ref, wout_ref, bout_ref, out_ref, att_ref):
    block, members, width = mid_ref.shape
    head_dim = width // HEADS
    values = mid_ref[...].reshape(block * members, width).astype(jnp.float32)
    mean = jnp.mean(values, axis=-1, keepdims=True)
    centred = values - mean
    var = jnp.mean(jnp.square(centred), axis=-1, keepdims=True)
    normed = (centred * lax.rsqrt(var + 1e-05) * gain_ref[...] + bias_ref[...]).astype(jnp.bfloat16)
    qkv = jnp.dot(normed, wqkv_ref[...], preferred_element_type=jnp.float32).astype(jnp.bfloat16)
    for g in range(block):
        rows = slice(g * members, (g + 1) * members)
        for h in range(HEADS):
            lo = h * head_dim
            query = qkv[rows, lo : lo + head_dim]
            keys = qkv[rows, width + lo : width + lo + head_dim]
            vals = qkv[rows, 2 * width + lo : 2 * width + lo + head_dim]
            scores = lax.dot_general(
                query, keys, (((1,), (1,)), ((), ())), preferred_element_type=jnp.float32
            ) * head_dim ** (-0.5) + pos_ref[h]
            top = jnp.max(scores, axis=-1, keepdims=True)
            expo = jnp.exp(scores - top)
            probs = (expo / jnp.sum(expo, axis=-1, keepdims=True)).astype(jnp.bfloat16)
            mixed = jnp.dot(probs, vals, preferred_element_type=jnp.float32)
            att_ref[rows, lo : lo + head_dim] = mixed.astype(jnp.bfloat16)
    result = values + jnp.dot(att_ref[...], wout_ref[...], preferred_element_type=jnp.float32) + bout_ref[...]
    out_ref[...] = result.astype(jnp.bfloat16).reshape(block, members, width)


def owner_block(grouped, ln_gain, ln_bias, w_qkv, pos_bias, w_out, b_out):
    groups, members, width = grouped.shape
    block = math.gcd(groups, 4)
    whole = lambda shape: pl.BlockSpec(shape, lambda i: (0,) * len(shape))
    return pl.pallas_call(
        owner_kernel,
        out_shape=jax.ShapeDtypeStruct(grouped.shape, jnp.bfloat16),
        grid=(groups // block,),
        in_specs=[
            pl.BlockSpec((block, members, width), lambda i: (i, 0, 0)),
            whole((1, width)),
            whole((1, width)),
            whole(w_qkv.shape),
            whole(pos_bias.shape),
            whole(w_out.shape),
            whole((1, width)),
        ],
        out_specs=pl.BlockSpec((block, members, width), lambda i: (i, 0, 0)),
        scratch_shapes=[pltpu.VMEM((block * members, width), jnp.bfloat16)],
    )(
        grouped,
        ln_gain.reshape(1, width),
        ln_bias.reshape(1, width),
        w_qkv,
        pos_bias,
        w_out,
        b_out.reshape(1, width),
    )


def on_device(
    latent,
    bn_scale,
    bn_shift,
    w_expand,
    b_expand,
    dw_kernel,
    dw_bias,
    w_project,
    b_project,
    ln_gain,
    ln_bias,
    w_qkv,
    pos_bias,
    w_out,
    b_out,
):
    tile_h, tile_w, width = latent.shape
    hidden_width = w_expand.shape[1]
    rows_here = latent.shape[0]
    cols_here = latent.shape[1]
    normed_in = (latent.astype(jnp.float32) * bn_scale + bn_shift).astype(jnp.bfloat16)
    hidden = (
        jnp.dot(normed_in.reshape(-1, width), w_expand, preferred_element_type=jnp.float32)
        + b_expand
    )
    padded = extended(
        gelu_tanh(hidden).astype(jnp.bfloat16).reshape(rows_here, cols_here, hidden_width),
        (("row", 0), ("col", 1)),
        1,
    )
    total = jnp.zeros((tile_h, tile_w, hidden_width), jnp.float32)
    for down in range(3):
        for across in range(3):
            total = total + padded[down : down + tile_h, across : across + tile_w].astype(
                jnp.float32
            ) * dw_kernel[down, across].astype(jnp.float32)
    depth = gelu_tanh(total + dw_bias).astype(jnp.bfloat16)
    proj = jnp.dot(depth.reshape(-1, hidden_width), w_project, preferred_element_type=jnp.float32)
    mid = (latent.reshape(-1, width).astype(jnp.float32) + proj + b_project).astype(jnp.bfloat16)
    sizes = layout_sizes(tile_h, tile_w)
    grouped_mid = to_owner(mid.reshape(tile_h, tile_w, width), sizes)
    result = owner_block(grouped_mid, ln_gain, ln_bias, w_qkv, pos_bias, w_out, b_out)
    return to_home(result, sizes, tile_h, tile_w)


def solution(mesh):
    return jax.shard_map(
        on_device,
        mesh=mesh,
        in_specs=(
            P("row", "col", None),
            P(),
            P(),
            P(),
            P(),
            P(),
            P(),
            P(),
            P(),
            P(),
            P(),
            P(),
            P(),
            P(),
            P(),
        ),
        out_specs=P("row", "col", None),
        check_vma=False,
    )
```

```python
import math

import jax
import jax.numpy as jnp
from jax import lax
from jax.sharding import PartitionSpec as P
from jax.experimental import pallas as pl
from jax.experimental.pallas import tpu as pltpu

HEADS = 16
GRID = 8


def extended(block, sides, width):
    for axis, dim in sides:
        count = lax.axis_size(axis)
        forward = [(i, i + 1) for i in range(count - 1)]
        backward = [(target, source) for source, target in forward]
        low = lax.ppermute(
            lax.slice_in_dim(block, block.shape[dim] - width, None, axis=dim), axis, forward
        )
        high = lax.ppermute(lax.slice_in_dim(block, 0, width, axis=dim), axis, backward)
        block = jnp.concatenate([low, block, high], axis=dim)
    return block


def gelu_tanh(v):
    return jax.nn.gelu(v, approximate=True)


def layout_sizes(tile_h, tile_w):
    n_row = lax.axis_size("row")
    n_col = lax.axis_size("col")
    stride_h = tile_h * n_row // GRID
    stride_w = tile_w * n_col // GRID
    part_h = min(tile_h, stride_h)
    part_w = min(tile_w, stride_w)
    return dict(
        n_row=n_row,
        n_col=n_col,
        pr=tile_h // part_h,
        kr=part_h // n_row,
        qr=stride_h // part_h,
        pc=tile_w // part_w,
        kc=part_w // n_col,
        qc=stride_w // part_w,
    )


def to_owner(tile, sizes):
    tile_h, tile_w, feats = tile.shape
    message = sizes["pr"] * sizes["kr"] * sizes["pc"] * sizes["kc"]
    outgoing = tile.reshape(
        sizes["pr"], sizes["n_row"], sizes["kr"], sizes["pc"], sizes["n_col"], sizes["kc"], feats
    ).transpose(1, 4, 0, 2, 3, 5, 6)
    arrived = lax.all_to_all(
        outgoing.reshape(sizes["n_row"] * sizes["n_col"], message, feats),
        ("row", "col"),
        split_axis=0,
        concat_axis=0,
        tiled=True,
    )
    arrived = arrived.reshape(
        sizes["n_row"] // sizes["qr"],
        sizes["qr"],
        sizes["n_col"] // sizes["qc"],
        sizes["qc"],
        sizes["pr"],
        sizes["kr"],
        sizes["pc"],
        sizes["kc"],
        feats,
    )
    arrived = arrived.transpose(1, 5, 3, 7, 0, 4, 2, 6, 8)
    return arrived.reshape(
        sizes["qr"] * sizes["kr"] * sizes["qc"] * sizes["kc"], GRID * GRID, feats
    )


def to_home(grouped, sizes, tile_h, tile_w):
    feats = grouped.shape[-1]
    message = sizes["pr"] * sizes["kr"] * sizes["pc"] * sizes["kc"]
    outgoing = grouped.reshape(
        sizes["qr"],
        sizes["kr"],
        sizes["qc"],
        sizes["kc"],
        sizes["n_row"] // sizes["qr"],
        sizes["pr"],
        sizes["n_col"] // sizes["qc"],
        sizes["pc"],
        feats,
    )
    outgoing = outgoing.transpose(4, 0, 6, 2, 5, 1, 7, 3, 8)
    back = lax.all_to_all(
        outgoing.reshape(sizes["n_row"] * sizes["n_col"], message, feats),
        ("row", "col"),
        split_axis=0,
        concat_axis=0,
        tiled=True,
    )
    back = back.reshape(
        sizes["n_row"], sizes["n_col"], sizes["pr"], sizes["kr"], sizes["pc"], sizes["kc"], feats
    ).transpose(2, 0, 3, 4, 1, 5, 6)
    return back.reshape(tile_h, tile_w, feats)


def attend(qkv, pos_bias):
    groups, members, three = qkv.shape
    width = three // 3
    head_dim = width // HEADS
    query = qkv[:, :, :width].reshape(groups, members, HEADS, head_dim)
    keys = qkv[:, :, width : 2 * width].reshape(groups, members, HEADS, head_dim)
    values = qkv[:, :, 2 * width :].reshape(groups, members, HEADS, head_dim)
    scores = (
        jnp.einsum("gihd,gjhd->ghij", query, keys, preferred_element_type=jnp.float32)
        * head_dim ** (-0.5)
        + pos_bias[None]
    )
    top = jnp.max(scores, axis=-1, keepdims=True)
    expo = jnp.exp(scores - top)
    probs = (expo / jnp.sum(expo, axis=-1, keepdims=True)).astype(jnp.bfloat16)
    mixed = jnp.einsum("ghij,gjhd->gihd", probs, values, preferred_element_type=jnp.float32)
    return mixed.astype(jnp.bfloat16).reshape(groups, members, width)


def owner_kernel(mid_ref, gain_ref, bias_ref, wqkv_ref, pos_ref, wout_ref, bout_ref, out_ref, att_ref):
    block, members, width = mid_ref.shape
    head_dim = width // HEADS
    values = mid_ref[...].reshape(block * members, width).astype(jnp.float32)
    mean = jnp.mean(values, axis=-1, keepdims=True)
    centred = values - mean
    var = jnp.mean(jnp.square(centred), axis=-1, keepdims=True)
    normed = (centred * lax.rsqrt(var + 1e-05) * gain_ref[...] + bias_ref[...]).astype(jnp.bfloat16)
    qkv = jnp.dot(normed, wqkv_ref[...], preferred_element_type=jnp.float32).astype(jnp.bfloat16)
    lanes = 128
    per_tile = lanes // head_dim
    head_of = lax.broadcasted_iota(jnp.int32, (1, lanes), 1) // head_dim
    for g in range(block):
        rows = slice(g * members, (g + 1) * members)
        for k in range(width // lanes):
            lo = k * lanes
            query = qkv[rows, lo : lo + lanes]
            keys = qkv[rows, width + lo : width + lo + lanes]
            vals = qkv[rows, 2 * width + lo : 2 * width + lo + lanes]
            masked = jnp.concatenate(
                [jnp.where(head_of == t, query, jnp.zeros_like(query)) for t in range(per_tile)], axis=0
            )
            scores = lax.dot_general(
                masked, keys, (((1,), (1,)), ((), ())), preferred_element_type=jnp.float32
            ) * head_dim ** (-0.5) + pos_ref[k]
            top = jnp.max(scores, axis=-1, keepdims=True)
            expo = jnp.exp(scores - top)
            probs = (expo / jnp.sum(expo, axis=-1, keepdims=True)).astype(jnp.bfloat16)
            mixed = jnp.dot(probs, vals, preferred_element_type=jnp.float32)
            picked = jnp.where(head_of == 0, mixed[:members], 0.0)
            for t in range(1, per_tile):
                picked = picked + jnp.where(head_of == t, mixed[t * members : (t + 1) * members], 0.0)
            att_ref[rows, lo : lo + lanes] = picked.astype(jnp.bfloat16)
    result = values + jnp.dot(att_ref[...], wout_ref[...], preferred_element_type=jnp.float32) + bout_ref[...]
    out_ref[...] = result.astype(jnp.bfloat16).reshape(block, members, width)


def owner_block(grouped, ln_gain, ln_bias, w_qkv, pos_bias, w_out, b_out):
    groups, members, width = grouped.shape
    block = math.gcd(groups, 4)
    whole = lambda shape: pl.BlockSpec(shape, lambda i: (0,) * len(shape))
    return pl.pallas_call(
        owner_kernel,
        out_shape=jax.ShapeDtypeStruct(grouped.shape, jnp.bfloat16),
        grid=(groups // block,),
        in_specs=[
            pl.BlockSpec((block, members, width), lambda i: (i, 0, 0)),
            whole((1, width)),
            whole((1, width)),
            whole(w_qkv.shape),
            whole((width // 128, 128 // (width // HEADS) * members, members)),
            whole(w_out.shape),
            whole((1, width)),
        ],
        out_specs=pl.BlockSpec((block, members, width), lambda i: (i, 0, 0)),
        scratch_shapes=[pltpu.VMEM((block * members, width), jnp.bfloat16)],
    )(
        grouped,
        ln_gain.reshape(1, width),
        ln_bias.reshape(1, width),
        w_qkv,
        pos_bias.reshape(width // 128, -1, members),
        w_out,
        b_out.reshape(1, width),
    )


def on_device(
    latent,
    bn_scale,
    bn_shift,
    w_expand,
    b_expand,
    dw_kernel,
    dw_bias,
    w_project,
    b_project,
    ln_gain,
    ln_bias,
    w_qkv,
    pos_bias,
    w_out,
    b_out,
):
    tile_h, tile_w, width = latent.shape
    hidden_width = w_expand.shape[1]
    rows_here = latent.shape[0]
    cols_here = latent.shape[1]
    normed_in = (latent.astype(jnp.float32) * bn_scale + bn_shift).astype(jnp.bfloat16)
    hidden = (
        jnp.dot(normed_in.reshape(-1, width), w_expand, preferred_element_type=jnp.float32)
        + b_expand
    )
    padded = extended(
        gelu_tanh(hidden).astype(jnp.bfloat16).reshape(rows_here, cols_here, hidden_width),
        (("row", 0), ("col", 1)),
        1,
    )
    total = jnp.zeros((tile_h, tile_w, hidden_width), jnp.float32)
    for down in range(3):
        for across in range(3):
            total = total + padded[down : down + tile_h, across : across + tile_w].astype(
                jnp.float32
            ) * dw_kernel[down, across].astype(jnp.float32)
    depth = gelu_tanh(total + dw_bias).astype(jnp.bfloat16)
    proj = jnp.dot(depth.reshape(-1, hidden_width), w_project, preferred_element_type=jnp.float32)
    mid = (latent.reshape(-1, width).astype(jnp.float32) + proj + b_project).astype(jnp.bfloat16)
    sizes = layout_sizes(tile_h, tile_w)
    grouped_mid = to_owner(mid.reshape(tile_h, tile_w, width), sizes)
    result = owner_block(grouped_mid, ln_gain, ln_bias, w_qkv, pos_bias, w_out, b_out)
    return to_home(result, sizes, tile_h, tile_w)


def solution(mesh):
    return jax.shard_map(
        on_device,
        mesh=mesh,
        in_specs=(
            P("row", "col", None),
            P(),
            P(),
            P(),
            P(),
            P(),
            P(),
            P(),
            P(),
            P(),
            P(),
            P(),
            P(),
            P(),
            P(),
        ),
        out_specs=P("row", "col", None),
        check_vma=False,
    )
```

```python
import math

import jax
import jax.numpy as jnp
from jax import lax
from jax.sharding import PartitionSpec as P
from jax.experimental import pallas as pl
from jax.experimental.pallas import tpu as pltpu

HEADS = 16
GRID = 8


def extended(block, sides, width):
    for axis, dim in sides:
        count = lax.axis_size(axis)
        forward = [(i, i + 1) for i in range(count - 1)]
        backward = [(target, source) for source, target in forward]
        low = lax.ppermute(
            lax.slice_in_dim(block, block.shape[dim] - width, None, axis=dim), axis, forward
        )
        high = lax.ppermute(lax.slice_in_dim(block, 0, width, axis=dim), axis, backward)
        block = jnp.concatenate([low, block, high], axis=dim)
    return block


def gelu_tanh(v):
    return jax.nn.gelu(v, approximate=True)


def layout_sizes(tile_h, tile_w):
    n_row = lax.axis_size("row")
    n_col = lax.axis_size("col")
    stride_h = tile_h * n_row // GRID
    stride_w = tile_w * n_col // GRID
    part_h = min(tile_h, stride_h)
    part_w = min(tile_w, stride_w)
    return dict(
        n_row=n_row,
        n_col=n_col,
        pr=tile_h // part_h,
        kr=part_h // n_row,
        qr=stride_h // part_h,
        pc=tile_w // part_w,
        kc=part_w // n_col,
        qc=stride_w // part_w,
    )


def to_owner(tile, sizes):
    tile_h, tile_w, feats = tile.shape
    message = sizes["pr"] * sizes["kr"] * sizes["pc"] * sizes["kc"]
    outgoing = tile.reshape(
        sizes["pr"], sizes["n_row"], sizes["kr"], sizes["pc"], sizes["n_col"], sizes["kc"], feats
    ).transpose(1, 4, 0, 2, 3, 5, 6)
    arrived = lax.all_to_all(
        outgoing.reshape(sizes["n_row"] * sizes["n_col"], message, feats),
        ("row", "col"),
        split_axis=0,
        concat_axis=0,
        tiled=True,
    )
    arrived = arrived.reshape(
        sizes["n_row"] // sizes["qr"],
        sizes["qr"],
        sizes["n_col"] // sizes["qc"],
        sizes["qc"],
        sizes["pr"],
        sizes["kr"],
        sizes["pc"],
        sizes["kc"],
        feats,
    )
    arrived = arrived.transpose(1, 5, 3, 7, 0, 4, 2, 6, 8)
    return arrived.reshape(
        sizes["qr"] * sizes["kr"] * sizes["qc"] * sizes["kc"], GRID * GRID, feats
    )


def to_home(grouped, sizes, tile_h, tile_w):
    feats = grouped.shape[-1]
    message = sizes["pr"] * sizes["kr"] * sizes["pc"] * sizes["kc"]
    outgoing = grouped.reshape(
        sizes["qr"],
        sizes["kr"],
        sizes["qc"],
        sizes["kc"],
        sizes["n_row"] // sizes["qr"],
        sizes["pr"],
        sizes["n_col"] // sizes["qc"],
        sizes["pc"],
        feats,
    )
    outgoing = outgoing.transpose(4, 0, 6, 2, 5, 1, 7, 3, 8)
    back = lax.all_to_all(
        outgoing.reshape(sizes["n_row"] * sizes["n_col"], message, feats),
        ("row", "col"),
        split_axis=0,
        concat_axis=0,
        tiled=True,
    )
    back = back.reshape(
        sizes["n_row"], sizes["n_col"], sizes["pr"], sizes["kr"], sizes["pc"], sizes["kc"], feats
    ).transpose(2, 0, 3, 4, 1, 5, 6)
    return back.reshape(tile_h, tile_w, feats)


def attend(qkv, pos_bias):
    groups, members, three = qkv.shape
    width = three // 3
    head_dim = width // HEADS
    query = qkv[:, :, :width].reshape(groups, members, HEADS, head_dim)
    keys = qkv[:, :, width : 2 * width].reshape(groups, members, HEADS, head_dim)
    values = qkv[:, :, 2 * width :].reshape(groups, members, HEADS, head_dim)
    scores = (
        jnp.einsum("gihd,gjhd->ghij", query, keys, preferred_element_type=jnp.float32)
        * head_dim ** (-0.5)
        + pos_bias[None]
    )
    top = jnp.max(scores, axis=-1, keepdims=True)
    expo = jnp.exp(scores - top)
    probs = (expo / jnp.sum(expo, axis=-1, keepdims=True)).astype(jnp.bfloat16)
    mixed = jnp.einsum("ghij,gjhd->gihd", probs, values, preferred_element_type=jnp.float32)
    return mixed.astype(jnp.bfloat16).reshape(groups, members, width)


def owner_kernel(mid_ref, gain_ref, bias_ref, wqkv_ref, pos_ref, wout_ref, bout_ref, out_ref, att_ref):
    block, members, width = mid_ref.shape
    head_dim = width // HEADS
    values = mid_ref[...].reshape(block * members, width).astype(jnp.float32)
    mean = jnp.mean(values, axis=-1, keepdims=True)
    centred = values - mean
    var = jnp.mean(jnp.square(centred), axis=-1, keepdims=True)
    normed = (centred * lax.rsqrt(var + 1e-05) * gain_ref[...] + bias_ref[...]).astype(jnp.bfloat16)
    qkv = jnp.dot(normed, wqkv_ref[...], preferred_element_type=jnp.float32).astype(jnp.bfloat16)
    lanes = 128
    per_tile = lanes // head_dim
    head_of = lax.broadcasted_iota(jnp.int32, (1, lanes), 1) // head_dim
    for g in range(block):
        rows = slice(g * members, (g + 1) * members)
        for k in range(width // lanes):
            lo = k * lanes
            query = qkv[rows, lo : lo + lanes]
            keys = qkv[rows, width + lo : width + lo + lanes]
            vals = qkv[rows, 2 * width + lo : 2 * width + lo + lanes]
            masked = jnp.concatenate(
                [jnp.where(head_of == t, query, jnp.zeros_like(query)) for t in range(per_tile)], axis=0
            )
            scores = lax.dot_general(
                masked, keys, (((1,), (1,)), ((), ())), preferred_element_type=jnp.float32
            ) * head_dim ** (-0.5) + pos_ref[k]
            top = jnp.max(scores, axis=-1, keepdims=True)
            expo = jnp.exp(scores - top)
            probs = (expo / jnp.sum(expo, axis=-1, keepdims=True)).astype(jnp.bfloat16)
            mixed = jnp.dot(probs, vals, preferred_element_type=jnp.float32)
            picked = jnp.where(head_of == 0, mixed[:members], 0.0)
            for t in range(1, per_tile):
                picked = picked + jnp.where(head_of == t, mixed[t * members : (t + 1) * members], 0.0)
            att_ref[rows, lo : lo + lanes] = picked.astype(jnp.bfloat16)
    result = values + jnp.dot(att_ref[...], wout_ref[...], preferred_element_type=jnp.float32) + bout_ref[...]
    out_ref[...] = result.astype(jnp.bfloat16).reshape(block, members, width)


def owner_block(grouped, ln_gain, ln_bias, w_qkv, pos_bias, w_out, b_out):
    groups, members, width = grouped.shape
    block = math.gcd(groups, 4)
    whole = lambda shape: pl.BlockSpec(shape, lambda i: (0,) * len(shape))
    return pl.pallas_call(
        owner_kernel,
        out_shape=jax.ShapeDtypeStruct(grouped.shape, jnp.bfloat16),
        grid=(groups // block,),
        in_specs=[
            pl.BlockSpec((block, members, width), lambda i: (i, 0, 0)),
            whole((1, width)),
            whole((1, width)),
            whole(w_qkv.shape),
            whole((width // 128, 128 // (width // HEADS) * members, members)),
            whole(w_out.shape),
            whole((1, width)),
        ],
        out_specs=pl.BlockSpec((block, members, width), lambda i: (i, 0, 0)),
        scratch_shapes=[pltpu.VMEM((block * members, width), jnp.bfloat16)],
    )(
        grouped,
        ln_gain.reshape(1, width),
        ln_bias.reshape(1, width),
        w_qkv,
        pos_bias.reshape(width // 128, -1, members),
        w_out,
        b_out.reshape(1, width),
    )


def on_device(
    latent,
    bn_scale,
    bn_shift,
    w_expand,
    b_expand,
    dw_kernel,
    dw_bias,
    w_project,
    b_project,
    ln_gain,
    ln_bias,
    w_qkv,
    pos_bias,
    w_out,
    b_out,
):
    tile_h, tile_w, width = latent.shape
    hidden_width = w_expand.shape[1]
    rows_here = latent.shape[0]
    cols_here = latent.shape[1]
    wide_in = extended(latent, (("row", 0), ("col", 1)), 1)
    normed_in = (wide_in.astype(jnp.float32) * bn_scale + bn_shift).astype(jnp.bfloat16)
    hidden = (
        jnp.einsum("yxc,cd->yxd", normed_in, w_expand, preferred_element_type=jnp.float32)
        + b_expand
    )
    row_at = lax.axis_index("row") * rows_here - 1 + jnp.arange(rows_here + 2)
    col_at = lax.axis_index("col") * cols_here - 1 + jnp.arange(cols_here + 2)
    inside = ((row_at >= 0) & (row_at < lax.axis_size("row") * rows_here))[:, None] & (
        (col_at >= 0) & (col_at < lax.axis_size("col") * cols_here)
    )[None, :]
    hidden = gelu_tanh(hidden).astype(jnp.bfloat16)
    padded = jnp.where(inside[:, :, None], hidden, jnp.zeros_like(hidden))
    total = jnp.zeros((tile_h, tile_w, hidden_width), jnp.float32)
    for down in range(3):
        for across in range(3):
            total = total + padded[down : down + tile_h, across : across + tile_w].astype(
                jnp.float32
            ) * dw_kernel[down, across].astype(jnp.float32)
    depth = gelu_tanh(total + dw_bias).astype(jnp.bfloat16)
    proj = jnp.dot(depth.reshape(-1, hidden_width), w_project, preferred_element_type=jnp.float32)
    mid = (latent.reshape(-1, width).astype(jnp.float32) + proj + b_project).astype(jnp.bfloat16)
    sizes = layout_sizes(tile_h, tile_w)
    grouped_mid = to_owner(mid.reshape(tile_h, tile_w, width), sizes)
    result = owner_block(grouped_mid, ln_gain, ln_bias, w_qkv, pos_bias, w_out, b_out)
    return to_home(result, sizes, tile_h, tile_w)


def solution(mesh):
    return jax.shard_map(
        on_device,
        mesh=mesh,
        in_specs=(
            P("row", "col", None),
            P(),
            P(),
            P(),
            P(),
            P(),
            P(),
            P(),
            P(),
            P(),
            P(),
            P(),
            P(),
            P(),
            P(),
        ),
        out_specs=P("row", "col", None),
        check_vma=False,
    )
```

```python
import math

import jax
import jax.numpy as jnp
from jax import lax
from jax.sharding import PartitionSpec as P
from jax.experimental import pallas as pl
from jax.experimental.pallas import tpu as pltpu

HEADS = 16
GRID = 8


def extended(block, sides, width):
    for axis, dim in sides:
        count = lax.axis_size(axis)
        forward = [(i, i + 1) for i in range(count - 1)]
        backward = [(target, source) for source, target in forward]
        low = lax.ppermute(
            lax.slice_in_dim(block, block.shape[dim] - width, None, axis=dim), axis, forward
        )
        high = lax.ppermute(lax.slice_in_dim(block, 0, width, axis=dim), axis, backward)
        block = jnp.concatenate([low, block, high], axis=dim)
    return block


def gelu_tanh(v):
    return jax.nn.gelu(v, approximate=True)


def layout_sizes(tile_h, tile_w):
    n_row = lax.axis_size("row")
    n_col = lax.axis_size("col")
    stride_h = tile_h * n_row // GRID
    stride_w = tile_w * n_col // GRID
    part_h = min(tile_h, stride_h)
    part_w = min(tile_w, stride_w)
    return dict(
        n_row=n_row,
        n_col=n_col,
        pr=tile_h // part_h,
        kr=part_h // n_row,
        qr=stride_h // part_h,
        pc=tile_w // part_w,
        kc=part_w // n_col,
        qc=stride_w // part_w,
    )


def to_owner(tile, sizes):
    tile_h, tile_w, feats = tile.shape
    message = sizes["pr"] * sizes["kr"] * sizes["pc"] * sizes["kc"]
    outgoing = tile.reshape(
        sizes["pr"], sizes["n_row"], sizes["kr"], sizes["pc"], sizes["n_col"], sizes["kc"], feats
    ).transpose(1, 4, 0, 2, 3, 5, 6)
    arrived = lax.all_to_all(
        outgoing.reshape(sizes["n_row"] * sizes["n_col"], message, feats),
        ("row", "col"),
        split_axis=0,
        concat_axis=0,
        tiled=True,
    )
    arrived = arrived.reshape(
        sizes["n_row"] // sizes["qr"],
        sizes["qr"],
        sizes["n_col"] // sizes["qc"],
        sizes["qc"],
        sizes["pr"],
        sizes["kr"],
        sizes["pc"],
        sizes["kc"],
        feats,
    )
    arrived = arrived.transpose(1, 5, 3, 7, 0, 4, 2, 6, 8)
    return arrived.reshape(
        sizes["qr"] * sizes["kr"] * sizes["qc"] * sizes["kc"], GRID * GRID, feats
    )


def send_part(half, sizes):
    part_h, tile_w, feats = half.shape
    outgoing = half.reshape(
        sizes["n_row"], sizes["kr"], sizes["pc"], sizes["n_col"], sizes["kc"], feats
    ).transpose(0, 3, 1, 2, 4, 5)
    return lax.all_to_all(
        outgoing.reshape(sizes["n_row"] * sizes["n_col"], -1, feats),
        ("row", "col"),
        split_axis=0,
        concat_axis=0,
        tiled=True,
    )


def from_parts(parts, sizes):
    feats = parts[0].shape[-1]
    arrived = jnp.stack(parts, axis=1)
    arrived = arrived.reshape(
        sizes["n_row"] // sizes["qr"],
        sizes["qr"],
        sizes["n_col"] // sizes["qc"],
        sizes["qc"],
        sizes["pr"],
        sizes["kr"],
        sizes["pc"],
        sizes["kc"],
        feats,
    )
    arrived = arrived.transpose(1, 5, 3, 7, 0, 4, 2, 6, 8)
    return arrived.reshape(
        sizes["qr"] * sizes["kr"] * sizes["qc"] * sizes["kc"], GRID * GRID, feats
    )


def to_home(grouped, sizes, tile_h, tile_w):
    feats = grouped.shape[-1]
    message = sizes["pr"] * sizes["kr"] * sizes["pc"] * sizes["kc"]
    outgoing = grouped.reshape(
        sizes["qr"],
        sizes["kr"],
        sizes["qc"],
        sizes["kc"],
        sizes["n_row"] // sizes["qr"],
        sizes["pr"],
        sizes["n_col"] // sizes["qc"],
        sizes["pc"],
        feats,
    )
    outgoing = outgoing.transpose(4, 0, 6, 2, 5, 1, 7, 3, 8)
    back = lax.all_to_all(
        outgoing.reshape(sizes["n_row"] * sizes["n_col"], message, feats),
        ("row", "col"),
        split_axis=0,
        concat_axis=0,
        tiled=True,
    )
    back = back.reshape(
        sizes["n_row"], sizes["n_col"], sizes["pr"], sizes["kr"], sizes["pc"], sizes["kc"], feats
    ).transpose(2, 0, 3, 4, 1, 5, 6)
    return back.reshape(tile_h, tile_w, feats)


def attend(qkv, pos_bias):
    groups, members, three = qkv.shape
    width = three // 3
    head_dim = width // HEADS
    query = qkv[:, :, :width].reshape(groups, members, HEADS, head_dim)
    keys = qkv[:, :, width : 2 * width].reshape(groups, members, HEADS, head_dim)
    values = qkv[:, :, 2 * width :].reshape(groups, members, HEADS, head_dim)
    scores = (
        jnp.einsum("gihd,gjhd->ghij", query, keys, preferred_element_type=jnp.float32)
        * head_dim ** (-0.5)
        + pos_bias[None]
    )
    top = jnp.max(scores, axis=-1, keepdims=True)
    expo = jnp.exp(scores - top)
    probs = (expo / jnp.sum(expo, axis=-1, keepdims=True)).astype(jnp.bfloat16)
    mixed = jnp.einsum("ghij,gjhd->gihd", probs, values, preferred_element_type=jnp.float32)
    return mixed.astype(jnp.bfloat16).reshape(groups, members, width)


def owner_kernel(mid_ref, gain_ref, bias_ref, wqkv_ref, pos_ref, wout_ref, bout_ref, out_ref, att_ref):
    block, members, width = mid_ref.shape
    head_dim = width // HEADS
    values = mid_ref[...].reshape(block * members, width).astype(jnp.float32)
    mean = jnp.mean(values, axis=-1, keepdims=True)
    centred = values - mean
    var = jnp.mean(jnp.square(centred), axis=-1, keepdims=True)
    normed = (centred * lax.rsqrt(var + 1e-05) * gain_ref[...] + bias_ref[...]).astype(jnp.bfloat16)
    qkv = jnp.dot(normed, wqkv_ref[...], preferred_element_type=jnp.float32).astype(jnp.bfloat16)
    lanes = 128
    per_tile = lanes // head_dim
    head_of = lax.broadcasted_iota(jnp.int32, (1, lanes), 1) // head_dim
    for g in range(block):
        rows = slice(g * members, (g + 1) * members)
        for k in range(width // lanes):
            lo = k * lanes
            query = qkv[rows, lo : lo + lanes]
            keys = qkv[rows, width + lo : width + lo + lanes]
            vals = qkv[rows, 2 * width + lo : 2 * width + lo + lanes]
            masked = jnp.concatenate(
                [jnp.where(head_of == t, query, jnp.zeros_like(query)) for t in range(per_tile)], axis=0
            )
            scores = lax.dot_general(
                masked, keys, (((1,), (1,)), ((), ())), preferred_element_type=jnp.float32
            ) * head_dim ** (-0.5) + pos_ref[k]
            top = jnp.max(scores, axis=-1, keepdims=True)
            expo = jnp.exp(scores - top)
            probs = (expo / jnp.sum(expo, axis=-1, keepdims=True)).astype(jnp.bfloat16)
            mixed = jnp.dot(probs, vals, preferred_element_type=jnp.float32)
            picked = jnp.where(head_of == 0, mixed[:members], 0.0)
            for t in range(1, per_tile):
                picked = picked + jnp.where(head_of == t, mixed[t * members : (t + 1) * members], 0.0)
            att_ref[rows, lo : lo + lanes] = picked.astype(jnp.bfloat16)
    result = values + jnp.dot(att_ref[...], wout_ref[...], preferred_element_type=jnp.float32) + bout_ref[...]
    out_ref[...] = result.astype(jnp.bfloat16).reshape(block, members, width)


def owner_block(grouped, ln_gain, ln_bias, w_qkv, pos_bias, w_out, b_out):
    groups, members, width = grouped.shape
    block = math.gcd(groups, 4)
    whole = lambda shape: pl.BlockSpec(shape, lambda i: (0,) * len(shape))
    return pl.pallas_call(
        owner_kernel,
        out_shape=jax.ShapeDtypeStruct(grouped.shape, jnp.bfloat16),
        grid=(groups // block,),
        in_specs=[
            pl.BlockSpec((block, members, width), lambda i: (i, 0, 0)),
            whole((1, width)),
            whole((1, width)),
            whole(w_qkv.shape),
            whole((width // 128, 128 // (width // HEADS) * members, members)),
            whole(w_out.shape),
            whole((1, width)),
        ],
        out_specs=pl.BlockSpec((block, members, width), lambda i: (i, 0, 0)),
        scratch_shapes=[pltpu.VMEM((block * members, width), jnp.bfloat16)],
    )(
        grouped,
        ln_gain.reshape(1, width),
        ln_bias.reshape(1, width),
        w_qkv,
        pos_bias.reshape(width // 128, -1, members),
        w_out,
        b_out.reshape(1, width),
    )


def on_device(
    latent,
    bn_scale,
    bn_shift,
    w_expand,
    b_expand,
    dw_kernel,
    dw_bias,
    w_project,
    b_project,
    ln_gain,
    ln_bias,
    w_qkv,
    pos_bias,
    w_out,
    b_out,
):
    tile_h, tile_w, width = latent.shape
    hidden_width = w_expand.shape[1]
    rows_here = latent.shape[0]
    cols_here = latent.shape[1]
    wide_in = extended(latent, (("row", 0), ("col", 1)), 1)
    normed_in = (wide_in.astype(jnp.float32) * bn_scale + bn_shift).astype(jnp.bfloat16)
    hidden = (
        jnp.einsum("yxc,cd->yxd", normed_in, w_expand, preferred_element_type=jnp.float32)
        + b_expand
    )
    row_at = lax.axis_index("row") * rows_here - 1 + jnp.arange(rows_here + 2)
    col_at = lax.axis_index("col") * cols_here - 1 + jnp.arange(cols_here + 2)
    inside = ((row_at >= 0) & (row_at < lax.axis_size("row") * rows_here))[:, None] & (
        (col_at >= 0) & (col_at < lax.axis_size("col") * cols_here)
    )[None, :]
    hidden = gelu_tanh(hidden).astype(jnp.bfloat16)
    padded = jnp.where(inside[:, :, None], hidden, jnp.zeros_like(hidden))
    sizes = layout_sizes(tile_h, tile_w)
    part = tile_h // sizes["pr"]
    arrived = []
    for p in range(sizes["pr"]):
        total = jnp.zeros((part, tile_w, hidden_width), jnp.float32)
        for down in range(3):
            for across in range(3):
                total = total + padded[
                    p * part + down : p * part + down + part, across : across + tile_w
                ].astype(jnp.float32) * dw_kernel[down, across].astype(jnp.float32)
        depth = gelu_tanh(total + dw_bias).astype(jnp.bfloat16)
        proj = jnp.dot(
            depth.reshape(-1, hidden_width), w_project, preferred_element_type=jnp.float32
        )
        mid = (
            latent[p * part : (p + 1) * part].reshape(-1, width).astype(jnp.float32)
            + proj
            + b_project
        ).astype(jnp.bfloat16)
        arrived.append(send_part(mid.reshape(part, tile_w, width), sizes))
    grouped_mid = from_parts(arrived, sizes)
    result = owner_block(grouped_mid, ln_gain, ln_bias, w_qkv, pos_bias, w_out, b_out)
    return to_home(result, sizes, tile_h, tile_w)


def solution(mesh):
    return jax.shard_map(
        on_device,
        mesh=mesh,
        in_specs=(
            P("row", "col", None),
            P(),
            P(),
            P(),
            P(),
            P(),
            P(),
            P(),
            P(),
            P(),
            P(),
            P(),
            P(),
            P(),
            P(),
        ),
        out_specs=P("row", "col", None),
        check_vma=False,
    )
```

```python
import math

import jax
import jax.numpy as jnp
from jax import lax
from jax.sharding import PartitionSpec as P
from jax.experimental import pallas as pl
from jax.experimental.pallas import tpu as pltpu

HEADS = 16
GRID = 8


def neighbour(x, axis, step):
    count = lax.axis_size(axis)
    pairs = [(i, i + step) for i in range(count) if 0 <= i + step < count]
    return lax.ppermute(x, axis, pairs)


def extended(block, sides, width):
    for axis, dim in sides:
        count = lax.axis_size(axis)
        forward = [(i, i + 1) for i in range(count - 1)]
        backward = [(target, source) for source, target in forward]
        low = lax.ppermute(
            lax.slice_in_dim(block, block.shape[dim] - width, None, axis=dim), axis, forward
        )
        high = lax.ppermute(lax.slice_in_dim(block, 0, width, axis=dim), axis, backward)
        block = jnp.concatenate([low, block, high], axis=dim)
    return block


def gelu_tanh(v):
    return jax.nn.gelu(v, approximate=True)


def layout_sizes(tile_h, tile_w):
    n_row = lax.axis_size("row")
    n_col = lax.axis_size("col")
    stride_h = tile_h * n_row // GRID
    stride_w = tile_w * n_col // GRID
    part_h = min(tile_h, stride_h)
    part_w = min(tile_w, stride_w)
    return dict(
        n_row=n_row,
        n_col=n_col,
        pr=tile_h // part_h,
        kr=part_h // n_row,
        qr=stride_h // part_h,
        pc=tile_w // part_w,
        kc=part_w // n_col,
        qc=stride_w // part_w,
    )


def to_owner(tile, sizes):
    tile_h, tile_w, feats = tile.shape
    message = sizes["pr"] * sizes["kr"] * sizes["pc"] * sizes["kc"]
    outgoing = tile.reshape(
        sizes["pr"], sizes["n_row"], sizes["kr"], sizes["pc"], sizes["n_col"], sizes["kc"], feats
    ).transpose(1, 4, 0, 2, 3, 5, 6)
    arrived = lax.all_to_all(
        outgoing.reshape(sizes["n_row"] * sizes["n_col"], message, feats),
        ("row", "col"),
        split_axis=0,
        concat_axis=0,
        tiled=True,
    )
    arrived = arrived.reshape(
        sizes["n_row"] // sizes["qr"],
        sizes["qr"],
        sizes["n_col"] // sizes["qc"],
        sizes["qc"],
        sizes["pr"],
        sizes["kr"],
        sizes["pc"],
        sizes["kc"],
        feats,
    )
    arrived = arrived.transpose(1, 5, 3, 7, 0, 4, 2, 6, 8)
    return arrived.reshape(
        sizes["qr"] * sizes["kr"] * sizes["qc"] * sizes["kc"], GRID * GRID, feats
    )


def to_home(grouped, sizes, tile_h, tile_w):
    feats = grouped.shape[-1]
    message = sizes["pr"] * sizes["kr"] * sizes["pc"] * sizes["kc"]
    outgoing = grouped.reshape(
        sizes["qr"],
        sizes["kr"],
        sizes["qc"],
        sizes["kc"],
        sizes["n_row"] // sizes["qr"],
        sizes["pr"],
        sizes["n_col"] // sizes["qc"],
        sizes["pc"],
        feats,
    )
    outgoing = outgoing.transpose(4, 0, 6, 2, 5, 1, 7, 3, 8)
    back = lax.all_to_all(
        outgoing.reshape(sizes["n_row"] * sizes["n_col"], message, feats),
        ("row", "col"),
        split_axis=0,
        concat_axis=0,
        tiled=True,
    )
    back = back.reshape(
        sizes["n_row"], sizes["n_col"], sizes["pr"], sizes["kr"], sizes["pc"], sizes["kc"], feats
    ).transpose(2, 0, 3, 4, 1, 5, 6)
    return back.reshape(tile_h, tile_w, feats)


def attend(qkv, pos_bias):
    groups, members, three = qkv.shape
    width = three // 3
    head_dim = width // HEADS
    query = qkv[:, :, :width].reshape(groups, members, HEADS, head_dim)
    keys = qkv[:, :, width : 2 * width].reshape(groups, members, HEADS, head_dim)
    values = qkv[:, :, 2 * width :].reshape(groups, members, HEADS, head_dim)
    scores = (
        jnp.einsum("gihd,gjhd->ghij", query, keys, preferred_element_type=jnp.float32)
        * head_dim ** (-0.5)
        + pos_bias[None]
    )
    top = jnp.max(scores, axis=-1, keepdims=True)
    expo = jnp.exp(scores - top)
    probs = (expo / jnp.sum(expo, axis=-1, keepdims=True)).astype(jnp.bfloat16)
    mixed = jnp.einsum("ghij,gjhd->gihd", probs, values, preferred_element_type=jnp.float32)
    return mixed.astype(jnp.bfloat16).reshape(groups, members, width)


def owner_kernel(mid_ref, gain_ref, bias_ref, wqkv_ref, pos_ref, wout_ref, bout_ref, out_ref, att_ref):
    block, members, width = mid_ref.shape
    head_dim = width // HEADS
    values = mid_ref[...].reshape(block * members, width).astype(jnp.float32)
    mean = jnp.mean(values, axis=-1, keepdims=True)
    centred = values - mean
    var = jnp.mean(jnp.square(centred), axis=-1, keepdims=True)
    normed = (centred * lax.rsqrt(var + 1e-05) * gain_ref[...] + bias_ref[...]).astype(jnp.bfloat16)
    qkv = jnp.dot(normed, wqkv_ref[...], preferred_element_type=jnp.float32).astype(jnp.bfloat16)
    lanes = 128
    per_tile = lanes // head_dim
    head_of = lax.broadcasted_iota(jnp.int32, (1, lanes), 1) // head_dim
    for g in range(block):
        rows = slice(g * members, (g + 1) * members)
        for k in range(width // lanes):
            lo = k * lanes
            query = qkv[rows, lo : lo + lanes]
            keys = qkv[rows, width + lo : width + lo + lanes]
            vals = qkv[rows, 2 * width + lo : 2 * width + lo + lanes]
            masked = jnp.concatenate(
                [jnp.where(head_of == t, query, jnp.zeros_like(query)) for t in range(per_tile)], axis=0
            )
            scores = lax.dot_general(
                masked, keys, (((1,), (1,)), ((), ())), preferred_element_type=jnp.float32
            ) * head_dim ** (-0.5) + pos_ref[k]
            top = jnp.max(scores, axis=-1, keepdims=True)
            expo = jnp.exp(scores - top)
            probs = (expo / jnp.sum(expo, axis=-1, keepdims=True)).astype(jnp.bfloat16)
            mixed = jnp.dot(probs, vals, preferred_element_type=jnp.float32)
            picked = jnp.where(head_of == 0, mixed[:members], 0.0)
            for t in range(1, per_tile):
                picked = picked + jnp.where(head_of == t, mixed[t * members : (t + 1) * members], 0.0)
            att_ref[rows, lo : lo + lanes] = picked.astype(jnp.bfloat16)
    result = values + jnp.dot(att_ref[...], wout_ref[...], preferred_element_type=jnp.float32) + bout_ref[...]
    out_ref[...] = result.astype(jnp.bfloat16).reshape(block, members, width)


def owner_block(grouped, ln_gain, ln_bias, w_qkv, pos_bias, w_out, b_out):
    groups, members, width = grouped.shape
    block = math.gcd(groups, 4)
    whole = lambda shape: pl.BlockSpec(shape, lambda i: (0,) * len(shape))
    return pl.pallas_call(
        owner_kernel,
        out_shape=jax.ShapeDtypeStruct(grouped.shape, jnp.bfloat16),
        grid=(groups // block,),
        in_specs=[
            pl.BlockSpec((block, members, width), lambda i: (i, 0, 0)),
            whole((1, width)),
            whole((1, width)),
            whole(w_qkv.shape),
            whole((width // 128, 128 // (width // HEADS) * members, members)),
            whole(w_out.shape),
            whole((1, width)),
        ],
        out_specs=pl.BlockSpec((block, members, width), lambda i: (i, 0, 0)),
        scratch_shapes=[pltpu.VMEM((block * members, width), jnp.bfloat16)],
    )(
        grouped,
        ln_gain.reshape(1, width),
        ln_bias.reshape(1, width),
        w_qkv,
        pos_bias.reshape(width // 128, -1, members),
        w_out,
        b_out.reshape(1, width),
    )


def on_device(
    latent,
    bn_scale,
    bn_shift,
    w_expand,
    b_expand,
    dw_kernel,
    dw_bias,
    w_project,
    b_project,
    ln_gain,
    ln_bias,
    w_qkv,
    pos_bias,
    w_out,
    b_out,
):
    tile_h, tile_w, width = latent.shape
    hidden_width = w_expand.shape[1]
    rows_here = latent.shape[0]
    cols_here = latent.shape[1]
    def expand(pixels):
        normed_in = (pixels.astype(jnp.float32) * bn_scale + bn_shift).astype(jnp.bfloat16)
        hidden = (
            jnp.einsum("...c,cd->...d", normed_in, w_expand, preferred_element_type=jnp.float32)
            + b_expand
        )
        return gelu_tanh(hidden).astype(jnp.bfloat16)

    def conv(strip, out_h, out_w):
        total = jnp.zeros((out_h, out_w, hidden_width), jnp.float32)
        for down in range(3):
            for across in range(3):
                total = total + strip[down : down + out_h, across : across + out_w].astype(
                    jnp.float32
                ) * dw_kernel[down, across].astype(jnp.float32)
        return gelu_tanh(total + dw_bias).astype(jnp.bfloat16)

    up = neighbour(latent[-1:], "row", 1)
    down = neighbour(latent[:1], "row", -1)
    inner = expand(latent)
    inner, up, down = lax.optimization_barrier((inner, up, down))
    tall = jnp.concatenate([up, latent, down], axis=0)
    west = neighbour(tall[:, -1:], "col", 1)
    east = neighbour(tall[:, :1], "col", -1)
    rim = expand(
        jnp.concatenate(
            [up.reshape(-1, width), down.reshape(-1, width), west.reshape(-1, width), east.reshape(-1, width)],
            axis=0,
        )
    )
    up_e = rim[:cols_here].reshape(1, cols_here, hidden_width)
    down_e = rim[cols_here : 2 * cols_here].reshape(1, cols_here, hidden_width)
    west_e = rim[2 * cols_here : 2 * cols_here + rows_here + 2].reshape(rows_here + 2, 1, hidden_width)
    east_e = rim[2 * cols_here + rows_here + 2 :].reshape(rows_here + 2, 1, hidden_width)

    row_at = lax.axis_index("row") * rows_here - 1 + jnp.arange(rows_here + 2)
    col_at = lax.axis_index("col") * cols_here - 1 + jnp.arange(cols_here + 2)
    inside = ((row_at >= 0) & (row_at < lax.axis_size("row") * rows_here))[:, None] & (
        (col_at >= 0) & (col_at < lax.axis_size("col") * cols_here)
    )[None, :]

    def masked(strip, rows, cols):
        keep = inside[rows, cols][:, :, None]
        return jnp.where(keep, strip, jnp.zeros_like(strip))

    top_strip = jnp.concatenate(
        [
            jnp.concatenate([west_e[0:1], up_e, east_e[0:1]], axis=1),
            jnp.concatenate([west_e[1:3], inner[0:2], east_e[1:3]], axis=1),
        ],
        axis=0,
    )
    bottom_strip = jnp.concatenate(
        [
            jnp.concatenate([west_e[-3:-1], inner[-2:], east_e[-3:-1]], axis=1),
            jnp.concatenate([west_e[-1:], down_e, east_e[-1:]], axis=1),
        ],
        axis=0,
    )
    left_strip = jnp.concatenate([west_e[1:-1], inner[:, 0:2]], axis=1)
    right_strip = jnp.concatenate([inner[:, -2:], east_e[1:-1]], axis=1)
    top_d = conv(masked(top_strip, slice(0, 3), slice(None)), 1, cols_here)
    bottom_d = conv(masked(bottom_strip, slice(-3, None), slice(None)), 1, cols_here)
    left_d = conv(masked(left_strip, slice(1, -1), slice(0, 3)), rows_here - 2, 1)
    right_d = conv(masked(right_strip, slice(1, -1), slice(-3, None)), rows_here - 2, 1)

    def project(depth, skip):
        proj = jnp.einsum("...c,cd->...d", depth, w_project, preferred_element_type=jnp.float32)
        return (skip.astype(jnp.float32) + proj + b_project).astype(jnp.bfloat16)

    whole_mid = project(conv(jnp.pad(inner, ((1, 1), (1, 1), (0, 0))), rows_here, cols_here), latent)
    edge_d = jnp.concatenate(
        [
            top_d.reshape(-1, hidden_width),
            bottom_d.reshape(-1, hidden_width),
            left_d.reshape(-1, hidden_width),
            right_d.reshape(-1, hidden_width),
        ],
        axis=0,
    )
    edge_skip = jnp.concatenate(
        [
            latent[0],
            latent[-1],
            latent[1:-1, 0],
            latent[1:-1, -1],
        ],
        axis=0,
    )
    edge_mid = project(edge_d, edge_skip)
    n_side = rows_here - 2
    mid = jnp.concatenate(
        [
            edge_mid[:cols_here].reshape(1, cols_here, width),
            jnp.concatenate(
                [
                    edge_mid[2 * cols_here : 2 * cols_here + n_side].reshape(n_side, 1, width),
                    whole_mid[1:-1, 1:-1],
                    edge_mid[2 * cols_here + n_side :].reshape(n_side, 1, width),
                ],
                axis=1,
            ),
            edge_mid[cols_here : 2 * cols_here].reshape(1, cols_here, width),
        ],
        axis=0,
    )
    sizes = layout_sizes(tile_h, tile_w)
    grouped_mid = to_owner(mid.reshape(tile_h, tile_w, width), sizes)
    result = owner_block(grouped_mid, ln_gain, ln_bias, w_qkv, pos_bias, w_out, b_out)
    return to_home(result, sizes, tile_h, tile_w)


def solution(mesh):
    return jax.shard_map(
        on_device,
        mesh=mesh,
        in_specs=(
            P("row", "col", None),
            P(),
            P(),
            P(),
            P(),
            P(),
            P(),
            P(),
            P(),
            P(),
            P(),
            P(),
            P(),
            P(),
            P(),
        ),
        out_specs=P("row", "col", None),
        check_vma=False,
    )
```

```python
import math

import jax
import jax.numpy as jnp
from jax import lax
from jax.sharding import PartitionSpec as P
from jax.experimental import pallas as pl
from jax.experimental.pallas import tpu as pltpu

HEADS = 16
GRID = 8


def neighbour(x, axis, step):
    count = lax.axis_size(axis)
    pairs = [(i, i + step) for i in range(count) if 0 <= i + step < count]
    return lax.ppermute(x, axis, pairs)


def extended(block, sides, width):
    for axis, dim in sides:
        count = lax.axis_size(axis)
        forward = [(i, i + 1) for i in range(count - 1)]
        backward = [(target, source) for source, target in forward]
        low = lax.ppermute(
            lax.slice_in_dim(block, block.shape[dim] - width, None, axis=dim), axis, forward
        )
        high = lax.ppermute(lax.slice_in_dim(block, 0, width, axis=dim), axis, backward)
        block = jnp.concatenate([low, block, high], axis=dim)
    return block


def gelu_tanh(v):
    return jax.nn.gelu(v, approximate=True)


def layout_sizes(tile_h, tile_w):
    n_row = lax.axis_size("row")
    n_col = lax.axis_size("col")
    stride_h = tile_h * n_row // GRID
    stride_w = tile_w * n_col // GRID
    part_h = min(tile_h, stride_h)
    part_w = min(tile_w, stride_w)
    return dict(
        n_row=n_row,
        n_col=n_col,
        pr=tile_h // part_h,
        kr=part_h // n_row,
        qr=stride_h // part_h,
        pc=tile_w // part_w,
        kc=part_w // n_col,
        qc=stride_w // part_w,
    )


def to_owner(tile, sizes):
    tile_h, tile_w, feats = tile.shape
    message = sizes["pr"] * sizes["kr"] * sizes["pc"] * sizes["kc"]
    outgoing = tile.reshape(
        sizes["pr"], sizes["n_row"], sizes["kr"], sizes["pc"], sizes["n_col"], sizes["kc"], feats
    ).transpose(1, 4, 0, 2, 3, 5, 6)
    arrived = lax.all_to_all(
        outgoing.reshape(sizes["n_row"] * sizes["n_col"], message, feats),
        ("row", "col"),
        split_axis=0,
        concat_axis=0,
        tiled=True,
    )
    arrived = arrived.reshape(
        sizes["n_row"] // sizes["qr"],
        sizes["qr"],
        sizes["n_col"] // sizes["qc"],
        sizes["qc"],
        sizes["pr"],
        sizes["kr"],
        sizes["pc"],
        sizes["kc"],
        feats,
    )
    arrived = arrived.transpose(1, 5, 3, 7, 0, 4, 2, 6, 8)
    return arrived.reshape(
        sizes["qr"] * sizes["kr"] * sizes["qc"] * sizes["kc"], GRID * GRID, feats
    )


def to_home(grouped, sizes, tile_h, tile_w):
    feats = grouped.shape[-1]
    message = sizes["pr"] * sizes["kr"] * sizes["pc"] * sizes["kc"]
    outgoing = grouped.reshape(
        sizes["qr"],
        sizes["kr"],
        sizes["qc"],
        sizes["kc"],
        sizes["n_row"] // sizes["qr"],
        sizes["pr"],
        sizes["n_col"] // sizes["qc"],
        sizes["pc"],
        feats,
    )
    outgoing = outgoing.transpose(4, 0, 6, 2, 5, 1, 7, 3, 8)
    back = lax.all_to_all(
        outgoing.reshape(sizes["n_row"] * sizes["n_col"], message, feats),
        ("row", "col"),
        split_axis=0,
        concat_axis=0,
        tiled=True,
    )
    back = back.reshape(
        sizes["n_row"], sizes["n_col"], sizes["pr"], sizes["kr"], sizes["pc"], sizes["kc"], feats
    ).transpose(2, 0, 3, 4, 1, 5, 6)
    return back.reshape(tile_h, tile_w, feats)


def attend(qkv, pos_bias):
    groups, members, three = qkv.shape
    width = three // 3
    head_dim = width // HEADS
    query = qkv[:, :, :width].reshape(groups, members, HEADS, head_dim)
    keys = qkv[:, :, width : 2 * width].reshape(groups, members, HEADS, head_dim)
    values = qkv[:, :, 2 * width :].reshape(groups, members, HEADS, head_dim)
    scores = (
        jnp.einsum("gihd,gjhd->ghij", query, keys, preferred_element_type=jnp.float32)
        * head_dim ** (-0.5)
        + pos_bias[None]
    )
    top = jnp.max(scores, axis=-1, keepdims=True)
    expo = jnp.exp(scores - top)
    probs = (expo / jnp.sum(expo, axis=-1, keepdims=True)).astype(jnp.bfloat16)
    mixed = jnp.einsum("ghij,gjhd->gihd", probs, values, preferred_element_type=jnp.float32)
    return mixed.astype(jnp.bfloat16).reshape(groups, members, width)


def owner_kernel(mid_ref, gain_ref, bias_ref, wqkv_ref, pos_ref, wout_ref, bout_ref, out_ref, att_ref):
    block, members, width = mid_ref.shape
    head_dim = width // HEADS
    values = mid_ref[...].reshape(block * members, width).astype(jnp.float32)
    mean = jnp.mean(values, axis=-1, keepdims=True)
    centred = values - mean
    var = jnp.mean(jnp.square(centred), axis=-1, keepdims=True)
    normed = (centred * lax.rsqrt(var + 1e-05) * gain_ref[...] + bias_ref[...]).astype(jnp.bfloat16)
    qkv = jnp.dot(normed, wqkv_ref[...], preferred_element_type=jnp.float32).astype(jnp.bfloat16)
    lanes = 128
    per_tile = lanes // head_dim
    head_of = lax.broadcasted_iota(jnp.int32, (1, lanes), 1) // head_dim
    for g in range(block):
        rows = slice(g * members, (g + 1) * members)
        for k in range(width // lanes):
            lo = k * lanes
            query = qkv[rows, lo : lo + lanes]
            keys = qkv[rows, width + lo : width + lo + lanes]
            vals = qkv[rows, 2 * width + lo : 2 * width + lo + lanes]
            masked = jnp.concatenate(
                [jnp.where(head_of == t, query, jnp.zeros_like(query)) for t in range(per_tile)], axis=0
            )
            scores = lax.dot_general(
                masked, keys, (((1,), (1,)), ((), ())), preferred_element_type=jnp.float32
            ) * head_dim ** (-0.5) + pos_ref[k]
            top = jnp.max(scores, axis=-1, keepdims=True)
            expo = jnp.exp(scores - top)
            probs = (expo / jnp.sum(expo, axis=-1, keepdims=True)).astype(jnp.bfloat16)
            mixed = jnp.dot(probs, vals, preferred_element_type=jnp.float32)
            picked = jnp.where(head_of == 0, mixed[:members], 0.0)
            for t in range(1, per_tile):
                picked = picked + jnp.where(head_of == t, mixed[t * members : (t + 1) * members], 0.0)
            att_ref[rows, lo : lo + lanes] = picked.astype(jnp.bfloat16)
    result = values + jnp.dot(att_ref[...], wout_ref[...], preferred_element_type=jnp.float32) + bout_ref[...]
    out_ref[...] = result.astype(jnp.bfloat16).reshape(block, members, width)


def owner_block(grouped, ln_gain, ln_bias, w_qkv, pos_bias, w_out, b_out):
    groups, members, width = grouped.shape
    block = math.gcd(groups, 4)
    whole = lambda shape: pl.BlockSpec(shape, lambda i: (0,) * len(shape))
    return pl.pallas_call(
        owner_kernel,
        out_shape=jax.ShapeDtypeStruct(grouped.shape, jnp.bfloat16),
        grid=(groups // block,),
        in_specs=[
            pl.BlockSpec((block, members, width), lambda i: (i, 0, 0)),
            whole((1, width)),
            whole((1, width)),
            whole(w_qkv.shape),
            whole((width // 128, 128 // (width // HEADS) * members, members)),
            whole(w_out.shape),
            whole((1, width)),
        ],
        out_specs=pl.BlockSpec((block, members, width), lambda i: (i, 0, 0)),
        scratch_shapes=[pltpu.VMEM((block * members, width), jnp.bfloat16)],
    )(
        grouped,
        ln_gain.reshape(1, width),
        ln_bias.reshape(1, width),
        w_qkv,
        pos_bias.reshape(width // 128, -1, members),
        w_out,
        b_out.reshape(1, width),
    )


def on_device(
    latent,
    bn_scale,
    bn_shift,
    w_expand,
    b_expand,
    dw_kernel,
    dw_bias,
    w_project,
    b_project,
    ln_gain,
    ln_bias,
    w_qkv,
    pos_bias,
    w_out,
    b_out,
):
    tile_h, tile_w, width = latent.shape
    hidden_width = w_expand.shape[1]
    rows_here = latent.shape[0]
    cols_here = latent.shape[1]
    def expand(pixels):
        normed_in = (pixels.astype(jnp.float32) * bn_scale + bn_shift).astype(jnp.bfloat16)
        hidden = (
            jnp.dot(normed_in, w_expand, preferred_element_type=jnp.float32)
            + b_expand
        )
        return gelu_tanh(hidden).astype(jnp.bfloat16)

    def conv_across(strip, out_w):
        total = jnp.zeros((1, out_w, hidden_width), jnp.float32)
        for down in range(3):
            for across in range(3):
                total = total + strip[across : across + 1, down : down + out_w].astype(
                    jnp.float32
                ) * dw_kernel[down, across].astype(jnp.float32)
        return gelu_tanh(total + dw_bias).astype(jnp.bfloat16)

    def conv(strip, out_h, out_w):
        total = jnp.zeros((out_h, out_w, hidden_width), jnp.float32)
        for down in range(3):
            for across in range(3):
                total = total + strip[down : down + out_h, across : across + out_w].astype(
                    jnp.float32
                ) * dw_kernel[down, across].astype(jnp.float32)
        return gelu_tanh(total + dw_bias).astype(jnp.bfloat16)

    up = neighbour(latent[-1:], "row", 1)
    down = neighbour(latent[:1], "row", -1)
    inner = expand(latent.reshape(-1, width)).reshape(rows_here, cols_here, hidden_width)
    inner, up, down = lax.optimization_barrier((inner, up, down))
    tall = jnp.concatenate([up, latent, down], axis=0)
    west = neighbour(tall[:, -1:], "col", 1)
    east = neighbour(tall[:, :1], "col", -1)
    rim = expand(
        jnp.concatenate(
            [up.reshape(-1, width), down.reshape(-1, width), west.reshape(-1, width), east.reshape(-1, width)],
            axis=0,
        )
    )
    up_e = rim[:cols_here].reshape(1, cols_here, hidden_width)
    down_e = rim[cols_here : 2 * cols_here].reshape(1, cols_here, hidden_width)
    west_e = rim[2 * cols_here : 2 * cols_here + rows_here + 2].reshape(rows_here + 2, 1, hidden_width)
    east_e = rim[2 * cols_here + rows_here + 2 :].reshape(rows_here + 2, 1, hidden_width)

    row_at = lax.axis_index("row") * rows_here - 1 + jnp.arange(rows_here + 2)
    col_at = lax.axis_index("col") * cols_here - 1 + jnp.arange(cols_here + 2)
    inside = ((row_at >= 0) & (row_at < lax.axis_size("row") * rows_here))[:, None] & (
        (col_at >= 0) & (col_at < lax.axis_size("col") * cols_here)
    )[None, :]

    def masked(strip, rows, cols):
        keep = inside[rows, cols][:, :, None]
        return jnp.where(keep, strip, jnp.zeros_like(strip))

    def masked_t(strip, cols):
        keep = inside[1:-1, cols].T[:, :, None]
        return jnp.where(keep, strip, jnp.zeros_like(strip))

    top_strip = jnp.concatenate(
        [
            jnp.concatenate([west_e[0:1], up_e, east_e[0:1]], axis=1),
            jnp.concatenate([west_e[1:3], inner[0:2], east_e[1:3]], axis=1),
        ],
        axis=0,
    )
    bottom_strip = jnp.concatenate(
        [
            jnp.concatenate([west_e[-3:-1], inner[-2:], east_e[-3:-1]], axis=1),
            jnp.concatenate([west_e[-1:], down_e, east_e[-1:]], axis=1),
        ],
        axis=0,
    )
    left_strip = jnp.concatenate([west_e[1:-1], inner[:, 0:2]], axis=1).transpose(1, 0, 2)
    right_strip = jnp.concatenate([inner[:, -2:], east_e[1:-1]], axis=1).transpose(1, 0, 2)
    top_d = conv(masked(top_strip, slice(0, 3), slice(None)), 1, cols_here)
    bottom_d = conv(masked(bottom_strip, slice(-3, None), slice(None)), 1, cols_here)
    left_d = conv_across(masked_t(left_strip, slice(0, 3)), rows_here - 2)
    right_d = conv_across(masked_t(right_strip, slice(-3, None)), rows_here - 2)

    def project(depth, skip):
        proj = jnp.einsum("...c,cd->...d", depth, w_project, preferred_element_type=jnp.float32)
        return (skip.astype(jnp.float32) + proj + b_project).astype(jnp.bfloat16)

    whole_d = conv(jnp.pad(inner, ((1, 1), (1, 1), (0, 0))), rows_here, cols_here)
    whole_mid = (
        latent.reshape(-1, width).astype(jnp.float32)
        + jnp.dot(whole_d.reshape(-1, hidden_width), w_project, preferred_element_type=jnp.float32)
        + b_project
    ).astype(jnp.bfloat16).reshape(rows_here, cols_here, width)
    edge_d = jnp.concatenate(
        [
            top_d.reshape(-1, hidden_width),
            bottom_d.reshape(-1, hidden_width),
            left_d.reshape(-1, hidden_width),
            right_d.reshape(-1, hidden_width),
        ],
        axis=0,
    )
    edge_skip = jnp.concatenate(
        [
            latent[0],
            latent[-1],
            latent[1:-1, 0],
            latent[1:-1, -1],
        ],
        axis=0,
    )
    edge_mid = project(edge_d, edge_skip)
    n_side = rows_here - 2
    mid = jnp.concatenate(
        [
            edge_mid[:cols_here].reshape(1, cols_here, width),
            jnp.concatenate(
                [
                    edge_mid[2 * cols_here : 2 * cols_here + n_side].reshape(n_side, 1, width),
                    whole_mid[1:-1, 1:-1],
                    edge_mid[2 * cols_here + n_side :].reshape(n_side, 1, width),
                ],
                axis=1,
            ),
            edge_mid[cols_here : 2 * cols_here].reshape(1, cols_here, width),
        ],
        axis=0,
    )
    sizes = layout_sizes(tile_h, tile_w)
    grouped_mid = to_owner(mid.reshape(tile_h, tile_w, width), sizes)
    result = owner_block(grouped_mid, ln_gain, ln_bias, w_qkv, pos_bias, w_out, b_out)
    return to_home(result, sizes, tile_h, tile_w)


def solution(mesh):
    return jax.shard_map(
        on_device,
        mesh=mesh,
        in_specs=(
            P("row", "col", None),
            P(),
            P(),
            P(),
            P(),
            P(),
            P(),
            P(),
            P(),
            P(),
            P(),
            P(),
            P(),
            P(),
            P(),
        ),
        out_specs=P("row", "col", None),
        check_vma=False,
    )
```

```python
import math

import jax
import jax.numpy as jnp
from jax import lax
from jax.sharding import PartitionSpec as P
from jax.experimental import pallas as pl
from jax.experimental.pallas import tpu as pltpu

HEADS = 16
GRID = 8


def extended(block, sides, width):
    for axis, dim in sides:
        count = lax.axis_size(axis)
        forward = [(i, i + 1) for i in range(count - 1)]
        backward = [(target, source) for source, target in forward]
        low = lax.ppermute(
            lax.slice_in_dim(block, block.shape[dim] - width, None, axis=dim), axis, forward
        )
        high = lax.ppermute(lax.slice_in_dim(block, 0, width, axis=dim), axis, backward)
        block = jnp.concatenate([low, block, high], axis=dim)
    return block


def gelu_tanh(v):
    return jax.nn.gelu(v, approximate=True)


def layout_sizes(tile_h, tile_w):
    n_row = lax.axis_size("row")
    n_col = lax.axis_size("col")
    stride_h = tile_h * n_row // GRID
    stride_w = tile_w * n_col // GRID
    part_h = min(tile_h, stride_h)
    part_w = min(tile_w, stride_w)
    return dict(
        n_row=n_row,
        n_col=n_col,
        pr=tile_h // part_h,
        kr=part_h // n_row,
        qr=stride_h // part_h,
        pc=tile_w // part_w,
        kc=part_w // n_col,
        qc=stride_w // part_w,
    )


def to_owner(tile, sizes):
    tile_h, tile_w, feats = tile.shape
    message = sizes["pr"] * sizes["kr"] * sizes["pc"] * sizes["kc"]
    outgoing = tile.reshape(
        sizes["pr"], sizes["n_row"], sizes["kr"], sizes["pc"], sizes["n_col"], sizes["kc"], feats
    ).transpose(1, 4, 0, 2, 3, 5, 6)
    arrived = lax.all_to_all(
        outgoing.reshape(sizes["n_row"] * sizes["n_col"], message, feats),
        ("row", "col"),
        split_axis=0,
        concat_axis=0,
        tiled=True,
    )
    arrived = arrived.reshape(
        sizes["n_row"] // sizes["qr"],
        sizes["qr"],
        sizes["n_col"] // sizes["qc"],
        sizes["qc"],
        sizes["pr"],
        sizes["kr"],
        sizes["pc"],
        sizes["kc"],
        feats,
    )
    arrived = arrived.transpose(1, 5, 3, 7, 0, 4, 2, 6, 8)
    return arrived.reshape(
        sizes["qr"] * sizes["kr"] * sizes["qc"] * sizes["kc"], GRID * GRID, feats
    )


def to_home(grouped, sizes, tile_h, tile_w):
    feats = grouped.shape[-1]
    message = sizes["pr"] * sizes["kr"] * sizes["pc"] * sizes["kc"]
    outgoing = grouped.reshape(
        sizes["qr"],
        sizes["kr"],
        sizes["qc"],
        sizes["kc"],
        sizes["n_row"] // sizes["qr"],
        sizes["pr"],
        sizes["n_col"] // sizes["qc"],
        sizes["pc"],
        feats,
    )
    outgoing = outgoing.transpose(4, 0, 6, 2, 5, 1, 7, 3, 8)
    back = lax.all_to_all(
        outgoing.reshape(sizes["n_row"] * sizes["n_col"], message, feats),
        ("row", "col"),
        split_axis=0,
        concat_axis=0,
        tiled=True,
    )
    back = back.reshape(
        sizes["n_row"], sizes["n_col"], sizes["pr"], sizes["kr"], sizes["pc"], sizes["kc"], feats
    ).transpose(2, 0, 3, 4, 1, 5, 6)
    return back.reshape(tile_h, tile_w, feats)


def attend(qkv, pos_bias):
    groups, members, three = qkv.shape
    width = three // 3
    head_dim = width // HEADS
    query = qkv[:, :, :width].reshape(groups, members, HEADS, head_dim)
    keys = qkv[:, :, width : 2 * width].reshape(groups, members, HEADS, head_dim)
    values = qkv[:, :, 2 * width :].reshape(groups, members, HEADS, head_dim)
    scores = (
        jnp.einsum("gihd,gjhd->ghij", query, keys, preferred_element_type=jnp.float32)
        * head_dim ** (-0.5)
        + pos_bias[None]
    )
    top = jnp.max(scores, axis=-1, keepdims=True)
    expo = jnp.exp(scores - top)
    probs = (expo / jnp.sum(expo, axis=-1, keepdims=True)).astype(jnp.bfloat16)
    mixed = jnp.einsum("ghij,gjhd->gihd", probs, values, preferred_element_type=jnp.float32)
    return mixed.astype(jnp.bfloat16).reshape(groups, members, width)


def owner_kernel(mid_ref, gain_ref, bias_ref, wqkv_ref, pos_ref, wout_ref, bout_ref, out_ref, qkv_ref, att_ref):
    rows_all, width = mid_ref.shape
    lanes = qkv_ref.shape[-1]
    members = pos_ref.shape[-1]
    groups = rows_all // members
    head_dim = width // HEADS
    values = mid_ref[...].astype(jnp.float32)
    mean = jnp.mean(values, axis=-1, keepdims=True)
    centred = values - mean
    var = jnp.mean(jnp.square(centred), axis=-1, keepdims=True)
    normed = (centred * lax.rsqrt(var + 1e-05) * gain_ref[...] + bias_ref[...]).astype(jnp.bfloat16)
    qkv = jnp.dot(normed, wqkv_ref[...], preferred_element_type=jnp.float32)
    qkv = qkv.astype(jnp.bfloat16).astype(jnp.float32)
    for t in range(qkv_ref.shape[0]):
        qkv_ref[t] = qkv[:, t * lanes : (t + 1) * lanes]
    tiles = width // lanes
    per_tile = lanes // head_dim
    head_of = lax.broadcasted_iota(jnp.int32, (1, lanes), 1) // head_dim
    for g in range(groups):
        rows = pl.ds(g, members, stride=groups)
        for k in range(tiles):
            query = qkv_ref[k, rows, :].astype(jnp.bfloat16)
            keys = qkv_ref[tiles + k, rows, :].astype(jnp.bfloat16)
            vals = qkv_ref[2 * tiles + k, rows, :].astype(jnp.bfloat16)
            masked = jnp.concatenate(
                [jnp.where(head_of == t, query, jnp.zeros_like(query)) for t in range(per_tile)], axis=0
            )
            scores = lax.dot_general(
                masked, keys, (((1,), (1,)), ((), ())), preferred_element_type=jnp.float32
            ) * head_dim ** (-0.5) + pos_ref[k]
            top = jnp.max(scores, axis=-1, keepdims=True)
            expo = jnp.exp(scores - top)
            probs = (expo / jnp.sum(expo, axis=-1, keepdims=True)).astype(jnp.bfloat16)
            mixed = jnp.dot(probs, vals, preferred_element_type=jnp.float32)
            picked = jnp.where(head_of == 0, mixed[:members], 0.0)
            for t in range(1, per_tile):
                picked = picked + jnp.where(head_of == t, mixed[t * members : (t + 1) * members], 0.0)
            att_ref[k, rows, :] = picked.astype(jnp.bfloat16).astype(jnp.float32)
    attended = jnp.concatenate([att_ref[k] for k in range(tiles)], axis=1).astype(jnp.bfloat16)
    result = values + jnp.dot(attended, wout_ref[...], preferred_element_type=jnp.float32) + bout_ref[...]
    out_ref[...] = result.astype(jnp.bfloat16)


def owner_block(arrived, ln_gain, ln_bias, w_qkv, pos_bias, w_out, b_out):
    rows_all, width = arrived.shape
    members = pos_bias.shape[-1]
    lanes = 128
    whole = lambda shape: pl.BlockSpec(shape, lambda: (0,) * len(shape))
    return pl.pallas_call(
        owner_kernel,
        out_shape=jax.ShapeDtypeStruct(arrived.shape, jnp.bfloat16),
        in_specs=[
            whole(arrived.shape),
            whole((1, width)),
            whole((1, width)),
            whole(w_qkv.shape),
            whole((width // lanes, lanes // (width // HEADS) * members, members)),
            whole(w_out.shape),
            whole((1, width)),
        ],
        out_specs=whole(arrived.shape),
        scratch_shapes=[
            pltpu.VMEM((3 * width // lanes, rows_all, lanes), jnp.float32),
            pltpu.VMEM((width // lanes, rows_all, lanes), jnp.float32),
        ],
    )(
        arrived,
        ln_gain.reshape(1, width),
        ln_bias.reshape(1, width),
        w_qkv,
        pos_bias.reshape(width // lanes, -1, members),
        w_out,
        b_out.reshape(1, width),
    )


def send_to_owner(tile, sizes):
    tile_h, tile_w, feats = tile.shape
    outgoing = tile.reshape(
        sizes["pr"], sizes["n_row"], sizes["kr"], sizes["pc"], sizes["n_col"], sizes["kc"], feats
    ).transpose(1, 4, 0, 2, 3, 5, 6)
    arrived = lax.all_to_all(
        outgoing.reshape(sizes["n_row"] * sizes["n_col"], -1, feats),
        ("row", "col"),
        split_axis=0,
        concat_axis=0,
        tiled=True,
    )
    return arrived.reshape(-1, feats)


def back_home(rows, sizes, tile_h, tile_w):
    feats = rows.shape[-1]
    back = lax.all_to_all(
        rows.reshape(sizes["n_row"] * sizes["n_col"], -1, feats),
        ("row", "col"),
        split_axis=0,
        concat_axis=0,
        tiled=True,
    )
    back = back.reshape(
        sizes["n_row"], sizes["n_col"], sizes["pr"], sizes["kr"], sizes["pc"], sizes["kc"], feats
    ).transpose(2, 0, 3, 4, 1, 5, 6)
    return back.reshape(tile_h, tile_w, feats)


def arrived_bias(pos_bias, sizes):
    heads, members, _ = pos_bias.shape
    a = sizes["n_row"] // sizes["qr"]
    b = sizes["n_col"] // sizes["qc"]
    c, d = sizes["pr"], sizes["pc"]
    assert sizes["qr"] == 1 or b * c * d == 1
    assert sizes["qc"] == 1 or c * d == 1
    assert sizes["kr"] == 1 or d == 1
    return (
        pos_bias.reshape(heads, a, c, b, d, a, c, b, d)
        .transpose(0, 1, 3, 2, 4, 5, 7, 6, 8)
        .reshape(heads, members, members)
    )

def on_device(
    latent,
    bn_scale,
    bn_shift,
    w_expand,
    b_expand,
    dw_kernel,
    dw_bias,
    w_project,
    b_project,
    ln_gain,
    ln_bias,
    w_qkv,
    pos_bias,
    w_out,
    b_out,
):
    tile_h, tile_w, width = latent.shape
    hidden_width = w_expand.shape[1]
    rows_here = latent.shape[0]
    cols_here = latent.shape[1]
    wide_in = extended(latent, (("row", 0), ("col", 1)), 1)
    normed_in = (wide_in.astype(jnp.float32) * bn_scale + bn_shift).astype(jnp.bfloat16)
    hidden = (
        jnp.einsum("yxc,cd->yxd", normed_in, w_expand, preferred_element_type=jnp.float32)
        + b_expand
    )
    row_at = lax.axis_index("row") * rows_here - 1 + jnp.arange(rows_here + 2)
    col_at = lax.axis_index("col") * cols_here - 1 + jnp.arange(cols_here + 2)
    inside = ((row_at >= 0) & (row_at < lax.axis_size("row") * rows_here))[:, None] & (
        (col_at >= 0) & (col_at < lax.axis_size("col") * cols_here)
    )[None, :]
    hidden = gelu_tanh(hidden).astype(jnp.bfloat16)
    padded = jnp.where(inside[:, :, None], hidden, jnp.zeros_like(hidden))
    total = jnp.zeros((tile_h, tile_w, hidden_width), jnp.float32)
    for down in range(3):
        for across in range(3):
            total = total + padded[down : down + tile_h, across : across + tile_w].astype(
                jnp.float32
            ) * dw_kernel[down, across].astype(jnp.float32)
    depth = gelu_tanh(total + dw_bias).astype(jnp.bfloat16)
    proj = jnp.dot(depth.reshape(-1, hidden_width), w_project, preferred_element_type=jnp.float32)
    mid = (latent.reshape(-1, width).astype(jnp.float32) + proj + b_project).astype(jnp.bfloat16)
    sizes = layout_sizes(tile_h, tile_w)
    arrived = send_to_owner(mid.reshape(tile_h, tile_w, width), sizes)
    result = owner_block(arrived, ln_gain, ln_bias, w_qkv, arrived_bias(pos_bias, sizes), w_out, b_out)
    return back_home(result, sizes, tile_h, tile_w)

def solution(mesh):
    return jax.shard_map(
        on_device,
        mesh=mesh,
        in_specs=(
            P("row", "col", None),
            P(),
            P(),
            P(),
            P(),
            P(),
            P(),
            P(),
            P(),
            P(),
            P(),
            P(),
            P(),
            P(),
            P(),
        ),
        out_specs=P("row", "col", None),
        check_vma=False,
    )
```

```python
import math

import numpy as np

import jax
import jax.numpy as jnp
from jax import lax
from jax.sharding import PartitionSpec as P
from jax.experimental import pallas as pl
from jax.experimental.pallas import tpu as pltpu

HEADS = 16
GRID = 8


def extended(block, sides, width):
    for axis, dim in sides:
        count = lax.axis_size(axis)
        forward = [(i, i + 1) for i in range(count - 1)]
        backward = [(target, source) for source, target in forward]
        low = lax.ppermute(
            lax.slice_in_dim(block, block.shape[dim] - width, None, axis=dim), axis, forward
        )
        high = lax.ppermute(lax.slice_in_dim(block, 0, width, axis=dim), axis, backward)
        block = jnp.concatenate([low, block, high], axis=dim)
    return block


def gelu_tanh(v):
    return jax.nn.gelu(v, approximate=True)


def layout_sizes(tile_h, tile_w):
    n_row = lax.axis_size("row")
    n_col = lax.axis_size("col")
    stride_h = tile_h * n_row // GRID
    stride_w = tile_w * n_col // GRID
    part_h = min(tile_h, stride_h)
    part_w = min(tile_w, stride_w)
    return dict(
        n_row=n_row,
        n_col=n_col,
        pr=tile_h // part_h,
        kr=part_h // n_row,
        qr=stride_h // part_h,
        pc=tile_w // part_w,
        kc=part_w // n_col,
        qc=stride_w // part_w,
    )


def to_owner(tile, sizes):
    tile_h, tile_w, feats = tile.shape
    message = sizes["pr"] * sizes["kr"] * sizes["pc"] * sizes["kc"]
    outgoing = tile.reshape(
        sizes["pr"], sizes["n_row"], sizes["kr"], sizes["pc"], sizes["n_col"], sizes["kc"], feats
    ).transpose(1, 4, 0, 2, 3, 5, 6)
    arrived = lax.all_to_all(
        outgoing.reshape(sizes["n_row"] * sizes["n_col"], message, feats),
        ("row", "col"),
        split_axis=0,
        concat_axis=0,
        tiled=True,
    )
    arrived = arrived.reshape(
        sizes["n_row"] // sizes["qr"],
        sizes["qr"],
        sizes["n_col"] // sizes["qc"],
        sizes["qc"],
        sizes["pr"],
        sizes["kr"],
        sizes["pc"],
        sizes["kc"],
        feats,
    )
    arrived = arrived.transpose(1, 5, 3, 7, 0, 4, 2, 6, 8)
    return arrived.reshape(
        sizes["qr"] * sizes["kr"] * sizes["qc"] * sizes["kc"], GRID * GRID, feats
    )


def to_home(grouped, sizes, tile_h, tile_w):
    feats = grouped.shape[-1]
    message = sizes["pr"] * sizes["kr"] * sizes["pc"] * sizes["kc"]
    outgoing = grouped.reshape(
        sizes["qr"],
        sizes["kr"],
        sizes["qc"],
        sizes["kc"],
        sizes["n_row"] // sizes["qr"],
        sizes["pr"],
        sizes["n_col"] // sizes["qc"],
        sizes["pc"],
        feats,
    )
    outgoing = outgoing.transpose(4, 0, 6, 2, 5, 1, 7, 3, 8)
    back = lax.all_to_all(
        outgoing.reshape(sizes["n_row"] * sizes["n_col"], message, feats),
        ("row", "col"),
        split_axis=0,
        concat_axis=0,
        tiled=True,
    )
    back = back.reshape(
        sizes["n_row"], sizes["n_col"], sizes["pr"], sizes["kr"], sizes["pc"], sizes["kc"], feats
    ).transpose(2, 0, 3, 4, 1, 5, 6)
    return back.reshape(tile_h, tile_w, feats)


def attend(qkv, pos_bias):
    groups, members, three = qkv.shape
    width = three // 3
    head_dim = width // HEADS
    query = qkv[:, :, :width].reshape(groups, members, HEADS, head_dim)
    keys = qkv[:, :, width : 2 * width].reshape(groups, members, HEADS, head_dim)
    values = qkv[:, :, 2 * width :].reshape(groups, members, HEADS, head_dim)
    scores = (
        jnp.einsum("gihd,gjhd->ghij", query, keys, preferred_element_type=jnp.float32)
        * head_dim ** (-0.5)
        + pos_bias[None]
    )
    top = jnp.max(scores, axis=-1, keepdims=True)
    expo = jnp.exp(scores - top)
    probs = (expo / jnp.sum(expo, axis=-1, keepdims=True)).astype(jnp.bfloat16)
    mixed = jnp.einsum("ghij,gjhd->gihd", probs, values, preferred_element_type=jnp.float32)
    return mixed.astype(jnp.bfloat16).reshape(groups, members, width)


def owner_kernel(mid_ref, gain_ref, bias_ref, wqkv_ref, pos_ref, wout_ref, bout_ref, out_ref, qkv_ref, att_ref):
    rows_all, width = mid_ref.shape
    lanes = qkv_ref.shape[-1]
    members = pos_ref.shape[-1]
    groups = rows_all // members
    head_dim = width // HEADS
    values = mid_ref[...].astype(jnp.float32)
    mean = jnp.mean(values, axis=-1, keepdims=True)
    centred = values - mean
    var = jnp.mean(jnp.square(centred), axis=-1, keepdims=True)
    normed = (centred * lax.rsqrt(var + 1e-05) * gain_ref[...] + bias_ref[...]).astype(jnp.bfloat16)
    qkv = jnp.dot(normed, wqkv_ref[...], preferred_element_type=jnp.float32)
    qkv = qkv.astype(jnp.bfloat16).astype(jnp.float32)
    for t in range(qkv_ref.shape[0]):
        qkv_ref[t] = qkv[:, t * lanes : (t + 1) * lanes]
    tiles = width // lanes
    per_tile = lanes // head_dim
    head_of = lax.broadcasted_iota(jnp.int32, (1, lanes), 1) // head_dim
    for g in range(groups):
        rows = pl.ds(g, members, stride=groups)
        for k in range(tiles):
            query = qkv_ref[k, rows, :].astype(jnp.bfloat16)
            keys = qkv_ref[tiles + k, rows, :].astype(jnp.bfloat16)
            vals = qkv_ref[2 * tiles + k, rows, :].astype(jnp.bfloat16)
            masked = jnp.concatenate(
                [jnp.where(head_of == t, query, jnp.zeros_like(query)) for t in range(per_tile)], axis=0
            )
            scores = lax.dot_general(
                masked, keys, (((1,), (1,)), ((), ())), preferred_element_type=jnp.float32
            ) * head_dim ** (-0.5) + pos_ref[k]
            top = jnp.max(scores, axis=-1, keepdims=True)
            expo = jnp.exp(scores - top)
            probs = (expo / jnp.sum(expo, axis=-1, keepdims=True)).astype(jnp.bfloat16)
            mixed = jnp.dot(probs, vals, preferred_element_type=jnp.float32)
            picked = jnp.where(head_of == 0, mixed[:members], 0.0)
            for t in range(1, per_tile):
                picked = picked + jnp.where(head_of == t, mixed[t * members : (t + 1) * members], 0.0)
            att_ref[k, rows, :] = picked.astype(jnp.bfloat16).astype(jnp.float32)
    attended = jnp.concatenate([att_ref[k] for k in range(tiles)], axis=1).astype(jnp.bfloat16)
    result = values + jnp.dot(attended, wout_ref[...], preferred_element_type=jnp.float32) + bout_ref[...]
    out_ref[...] = result.astype(jnp.bfloat16)


def owner_block(arrived, ln_gain, ln_bias, w_qkv, pos_bias, w_out, b_out):
    rows_all, width = arrived.shape
    members = pos_bias.shape[-1]
    lanes = 128
    whole = lambda shape: pl.BlockSpec(shape, lambda: (0,) * len(shape))
    return pl.pallas_call(
        owner_kernel,
        out_shape=jax.ShapeDtypeStruct(arrived.shape, jnp.bfloat16),
        in_specs=[
            whole(arrived.shape),
            whole((1, width)),
            whole((1, width)),
            whole(w_qkv.shape),
            whole((width // lanes, lanes // (width // HEADS) * members, members)),
            whole(w_out.shape),
            whole((1, width)),
        ],
        out_specs=whole(arrived.shape),
        scratch_shapes=[
            pltpu.VMEM((3 * width // lanes, rows_all, lanes), jnp.float32),
            pltpu.VMEM((width // lanes, rows_all, lanes), jnp.float32),
        ],
    )(
        arrived,
        ln_gain.reshape(1, width),
        ln_bias.reshape(1, width),
        w_qkv,
        pos_bias.reshape(width // lanes, -1, members),
        w_out,
        b_out.reshape(1, width),
    )


def send_to_owner(tile, sizes):
    tile_h, tile_w, feats = tile.shape
    outgoing = tile.reshape(
        sizes["pr"], sizes["n_row"], sizes["kr"], sizes["pc"], sizes["n_col"], sizes["kc"], feats
    ).transpose(1, 4, 0, 2, 3, 5, 6)
    arrived = lax.all_to_all(
        outgoing.reshape(sizes["n_row"] * sizes["n_col"], -1, feats),
        ("row", "col"),
        split_axis=0,
        concat_axis=0,
        tiled=True,
    )
    return arrived.reshape(-1, feats)


def back_home(rows, sizes, tile_h, tile_w):
    feats = rows.shape[-1]
    back = lax.all_to_all(
        rows.reshape(sizes["n_row"] * sizes["n_col"], -1, feats),
        ("row", "col"),
        split_axis=0,
        concat_axis=0,
        tiled=True,
    )
    back = back.reshape(
        sizes["n_row"], sizes["n_col"], sizes["pr"], sizes["kr"], sizes["pc"], sizes["kc"], feats
    ).transpose(2, 0, 3, 4, 1, 5, 6)
    return back.reshape(tile_h, tile_w, feats)


def arrived_bias(pos_bias, sizes):
    heads, members, _ = pos_bias.shape
    a = sizes["n_row"] // sizes["qr"]
    b = sizes["n_col"] // sizes["qc"]
    c, d = sizes["pr"], sizes["pc"]
    assert sizes["qr"] == 1 or b * c * d == 1
    assert sizes["qc"] == 1 or c * d == 1
    assert sizes["kr"] == 1 or d == 1
    order = np.arange(members).reshape(a, c, b, d).transpose(0, 2, 1, 3).reshape(-1)
    pick = jnp.asarray(np.eye(members, dtype=np.float32)[order])
    picked = jnp.einsum("hij,bj->hib", pos_bias, pick, precision=lax.Precision.HIGHEST)
    return jnp.einsum("ai,hib->hab", pick, picked, precision=lax.Precision.HIGHEST)

def on_device(
    latent,
    bn_scale,
    bn_shift,
    w_expand,
    b_expand,
    dw_kernel,
    dw_bias,
    w_project,
    b_project,
    ln_gain,
    ln_bias,
    w_qkv,
    pos_bias,
    w_out,
    b_out,
):
    tile_h, tile_w, width = latent.shape
    hidden_width = w_expand.shape[1]
    rows_here = latent.shape[0]
    cols_here = latent.shape[1]
    wide_in = extended(latent, (("row", 0), ("col", 1)), 1)
    normed_in = (wide_in.astype(jnp.float32) * bn_scale + bn_shift).astype(jnp.bfloat16)
    hidden = (
        jnp.einsum("yxc,cd->yxd", normed_in, w_expand, preferred_element_type=jnp.float32)
        + b_expand
    )
    row_at = lax.axis_index("row") * rows_here - 1 + jnp.arange(rows_here + 2)
    col_at = lax.axis_index("col") * cols_here - 1 + jnp.arange(cols_here + 2)
    inside = ((row_at >= 0) & (row_at < lax.axis_size("row") * rows_here))[:, None] & (
        (col_at >= 0) & (col_at < lax.axis_size("col") * cols_here)
    )[None, :]
    hidden = gelu_tanh(hidden).astype(jnp.bfloat16)
    padded = jnp.where(inside[:, :, None], hidden, jnp.zeros_like(hidden))
    total = jnp.zeros((tile_h, tile_w, hidden_width), jnp.float32)
    for down in range(3):
        for across in range(3):
            total = total + padded[down : down + tile_h, across : across + tile_w].astype(
                jnp.float32
            ) * dw_kernel[down, across].astype(jnp.float32)
    depth = gelu_tanh(total + dw_bias).astype(jnp.bfloat16)
    proj = jnp.dot(depth.reshape(-1, hidden_width), w_project, preferred_element_type=jnp.float32)
    mid = (latent.reshape(-1, width).astype(jnp.float32) + proj + b_project).astype(jnp.bfloat16)
    sizes = layout_sizes(tile_h, tile_w)
    arrived = send_to_owner(mid.reshape(tile_h, tile_w, width), sizes)
    result = owner_block(arrived, ln_gain, ln_bias, w_qkv, arrived_bias(pos_bias, sizes), w_out, b_out)
    return back_home(result, sizes, tile_h, tile_w)

def solution(mesh):
    return jax.shard_map(
        on_device,
        mesh=mesh,
        in_specs=(
            P("row", "col", None),
            P(),
            P(),
            P(),
            P(),
            P(),
            P(),
            P(),
            P(),
            P(),
            P(),
            P(),
            P(),
            P(),
            P(),
        ),
        out_specs=P("row", "col", None),
        check_vma=False,
    )
```

```python
import math

import numpy as np

import jax
import jax.numpy as jnp
from jax import lax
from jax.sharding import PartitionSpec as P
from jax.experimental import pallas as pl
from jax.experimental.pallas import tpu as pltpu

HEADS = 16
GRID = 8


def extended(block, sides, width):
    for axis, dim in sides:
        count = lax.axis_size(axis)
        forward = [(i, i + 1) for i in range(count - 1)]
        backward = [(target, source) for source, target in forward]
        low = lax.ppermute(
            lax.slice_in_dim(block, block.shape[dim] - width, None, axis=dim), axis, forward
        )
        high = lax.ppermute(lax.slice_in_dim(block, 0, width, axis=dim), axis, backward)
        block = jnp.concatenate([low, block, high], axis=dim)
    return block


def gelu_tanh(v):
    return jax.nn.gelu(v, approximate=True)


def layout_sizes(tile_h, tile_w):
    n_row = lax.axis_size("row")
    n_col = lax.axis_size("col")
    stride_h = tile_h * n_row // GRID
    stride_w = tile_w * n_col // GRID
    part_h = min(tile_h, stride_h)
    part_w = min(tile_w, stride_w)
    return dict(
        n_row=n_row,
        n_col=n_col,
        pr=tile_h // part_h,
        kr=part_h // n_row,
        qr=stride_h // part_h,
        pc=tile_w // part_w,
        kc=part_w // n_col,
        qc=stride_w // part_w,
    )


def to_owner(tile, sizes):
    tile_h, tile_w, feats = tile.shape
    message = sizes["pr"] * sizes["kr"] * sizes["pc"] * sizes["kc"]
    outgoing = tile.reshape(
        sizes["pr"], sizes["n_row"], sizes["kr"], sizes["pc"], sizes["n_col"], sizes["kc"], feats
    ).transpose(1, 4, 0, 2, 3, 5, 6)
    arrived = lax.all_to_all(
        outgoing.reshape(sizes["n_row"] * sizes["n_col"], message, feats),
        ("row", "col"),
        split_axis=0,
        concat_axis=0,
        tiled=True,
    )
    arrived = arrived.reshape(
        sizes["n_row"] // sizes["qr"],
        sizes["qr"],
        sizes["n_col"] // sizes["qc"],
        sizes["qc"],
        sizes["pr"],
        sizes["kr"],
        sizes["pc"],
        sizes["kc"],
        feats,
    )
    arrived = arrived.transpose(1, 5, 3, 7, 0, 4, 2, 6, 8)
    return arrived.reshape(
        sizes["qr"] * sizes["kr"] * sizes["qc"] * sizes["kc"], GRID * GRID, feats
    )


def to_home(grouped, sizes, tile_h, tile_w):
    feats = grouped.shape[-1]
    message = sizes["pr"] * sizes["kr"] * sizes["pc"] * sizes["kc"]
    outgoing = grouped.reshape(
        sizes["qr"],
        sizes["kr"],
        sizes["qc"],
        sizes["kc"],
        sizes["n_row"] // sizes["qr"],
        sizes["pr"],
        sizes["n_col"] // sizes["qc"],
        sizes["pc"],
        feats,
    )
    outgoing = outgoing.transpose(4, 0, 6, 2, 5, 1, 7, 3, 8)
    back = lax.all_to_all(
        outgoing.reshape(sizes["n_row"] * sizes["n_col"], message, feats),
        ("row", "col"),
        split_axis=0,
        concat_axis=0,
        tiled=True,
    )
    back = back.reshape(
        sizes["n_row"], sizes["n_col"], sizes["pr"], sizes["kr"], sizes["pc"], sizes["kc"], feats
    ).transpose(2, 0, 3, 4, 1, 5, 6)
    return back.reshape(tile_h, tile_w, feats)


def attend(qkv, pos_bias):
    groups, members, three = qkv.shape
    width = three // 3
    head_dim = width // HEADS
    query = qkv[:, :, :width].reshape(groups, members, HEADS, head_dim)
    keys = qkv[:, :, width : 2 * width].reshape(groups, members, HEADS, head_dim)
    values = qkv[:, :, 2 * width :].reshape(groups, members, HEADS, head_dim)
    scores = (
        jnp.einsum("gihd,gjhd->ghij", query, keys, preferred_element_type=jnp.float32)
        * head_dim ** (-0.5)
        + pos_bias[None]
    )
    top = jnp.max(scores, axis=-1, keepdims=True)
    expo = jnp.exp(scores - top)
    probs = (expo / jnp.sum(expo, axis=-1, keepdims=True)).astype(jnp.bfloat16)
    mixed = jnp.einsum("ghij,gjhd->gihd", probs, values, preferred_element_type=jnp.float32)
    return mixed.astype(jnp.bfloat16).reshape(groups, members, width)


def owner_kernel(mid_ref, gain_ref, bias_ref, wqkv_ref, pos_ref, wout_ref, bout_ref, out_ref, qkv_ref, att_ref):
    rows_all, width = mid_ref.shape
    lanes = qkv_ref.shape[-1]
    members = pos_ref.shape[-1]
    groups = rows_all // members
    head_dim = width // HEADS
    values = mid_ref[...].astype(jnp.float32)
    mean = jnp.mean(values, axis=-1, keepdims=True)
    centred = values - mean
    var = jnp.mean(jnp.square(centred), axis=-1, keepdims=True)
    normed = (centred * lax.rsqrt(var + 1e-05) * gain_ref[...] + bias_ref[...]).astype(jnp.bfloat16)
    qkv = jnp.dot(normed, wqkv_ref[...], preferred_element_type=jnp.float32)
    qkv = qkv.astype(jnp.bfloat16).astype(jnp.float32)
    for t in range(qkv_ref.shape[0]):
        qkv_ref[t] = qkv[:, t * lanes : (t + 1) * lanes]
    tiles = width // lanes
    per_tile = lanes // head_dim
    head_of = lax.broadcasted_iota(jnp.int32, (1, lanes), 1) // head_dim
    for g in range(groups):
        rows = pl.ds(g, members, stride=groups)
        for k in range(tiles):
            query = qkv_ref[k, rows, :].astype(jnp.bfloat16)
            keys = qkv_ref[tiles + k, rows, :].astype(jnp.bfloat16)
            vals = qkv_ref[2 * tiles + k, rows, :].astype(jnp.bfloat16)
            masked = jnp.concatenate(
                [jnp.where(head_of == t, query, jnp.zeros_like(query)) for t in range(per_tile)], axis=0
            )
            scores = lax.dot_general(
                masked, keys, (((1,), (1,)), ((), ())), preferred_element_type=jnp.float32
            ) * head_dim ** (-0.5) + pos_ref[k]
            top = jnp.max(scores, axis=-1, keepdims=True)
            expo = jnp.exp(scores - top)
            probs = (expo / jnp.sum(expo, axis=-1, keepdims=True)).astype(jnp.bfloat16)
            mixed = jnp.dot(probs, vals, preferred_element_type=jnp.float32)
            picked = jnp.where(head_of == 0, mixed[:members], 0.0)
            for t in range(1, per_tile):
                picked = picked + jnp.where(head_of == t, mixed[t * members : (t + 1) * members], 0.0)
            att_ref[k, rows, :] = picked.astype(jnp.bfloat16).astype(jnp.float32)
    attended = jnp.concatenate([att_ref[k] for k in range(tiles)], axis=1).astype(jnp.bfloat16)
    result = values + jnp.dot(attended, wout_ref[...], preferred_element_type=jnp.float32) + bout_ref[...]
    out_ref[...] = result.astype(jnp.bfloat16)


def owner_block(arrived, ln_gain, ln_bias, w_qkv, pos_bias, w_out, b_out):
    rows_all, width = arrived.shape
    members = pos_bias.shape[-1]
    lanes = 128
    whole = lambda shape: pl.BlockSpec(shape, lambda: (0,) * len(shape))
    return pl.pallas_call(
        owner_kernel,
        out_shape=jax.ShapeDtypeStruct(arrived.shape, jnp.bfloat16),
        in_specs=[
            whole(arrived.shape),
            whole((1, width)),
            whole((1, width)),
            whole(w_qkv.shape),
            whole((width // lanes, lanes // (width // HEADS) * members, members)),
            whole(w_out.shape),
            whole((1, width)),
        ],
        out_specs=whole(arrived.shape),
        scratch_shapes=[
            pltpu.VMEM((3 * width // lanes, rows_all, lanes), jnp.float32),
            pltpu.VMEM((width // lanes, rows_all, lanes), jnp.float32),
        ],
    )(
        arrived,
        ln_gain.reshape(1, width),
        ln_bias.reshape(1, width),
        w_qkv,
        pos_bias.reshape(width // lanes, -1, members),
        w_out,
        b_out.reshape(1, width),
    )


def send_to_owner(tile, sizes):
    tile_h, tile_w, feats = tile.shape
    outgoing = tile.reshape(
        sizes["pr"], sizes["n_row"], sizes["kr"], sizes["pc"], sizes["n_col"], sizes["kc"], feats
    ).transpose(1, 4, 0, 2, 3, 5, 6)
    arrived = lax.all_to_all(
        outgoing.reshape(sizes["n_row"] * sizes["n_col"], -1, feats),
        ("row", "col"),
        split_axis=0,
        concat_axis=0,
        tiled=True,
    )
    return arrived.reshape(-1, feats)


def back_home(rows, sizes, tile_h, tile_w):
    feats = rows.shape[-1]
    back = lax.all_to_all(
        rows.reshape(sizes["n_row"] * sizes["n_col"], -1, feats),
        ("row", "col"),
        split_axis=0,
        concat_axis=0,
        tiled=True,
    )
    back = back.reshape(
        sizes["n_row"], sizes["n_col"], sizes["pr"], sizes["kr"], sizes["pc"], sizes["kc"], feats
    ).transpose(2, 0, 3, 4, 1, 5, 6)
    return back.reshape(tile_h, tile_w, feats)


def runs_plan(tile_h, tile_w):
    n_row = lax.axis_size("row")
    n_col = lax.axis_size("col")
    stride_h = tile_h * n_row // GRID
    stride_w = tile_w * n_col // GRID
    n_dev = n_row * n_col
    per_owner = stride_h * stride_w // n_dev
    if tile_w != stride_w or tile_h % stride_h or stride_w % per_owner or per_owner % 16:
        return None
    return dict(parts=tile_h // stride_h, stride_h=stride_h, blocks=stride_w // per_owner, run=per_owner)


def send_runs(tile, plan):
    feats = tile.shape[-1]
    outgoing = tile.reshape(
        plan["parts"], plan["stride_h"], plan["blocks"], plan["run"], feats
    ).transpose(1, 2, 0, 3, 4)
    arrived = lax.all_to_all(
        outgoing.reshape(plan["stride_h"] * plan["blocks"], -1, feats),
        ("row", "col"),
        split_axis=0,
        concat_axis=0,
        tiled=True,
    )
    return arrived.reshape(-1, feats)


def back_runs(rows, plan, tile_h, tile_w):
    feats = rows.shape[-1]
    back = lax.all_to_all(
        rows.reshape(plan["stride_h"] * plan["blocks"], -1, feats),
        ("row", "col"),
        split_axis=0,
        concat_axis=0,
        tiled=True,
    )
    back = back.reshape(
        plan["stride_h"], plan["blocks"], plan["parts"], plan["run"], feats
    ).transpose(2, 0, 1, 3, 4)
    return back.reshape(tile_h, tile_w, feats)


def arrived_bias(pos_bias, a, b, c, d):
    heads, members, _ = pos_bias.shape
    order = np.arange(members).reshape(a, c, b, d).transpose(0, 2, 1, 3).reshape(-1)
    pick = jnp.asarray(np.eye(members, dtype=np.float32)[order])
    picked = jnp.einsum("hij,bj->hib", pos_bias, pick, precision=lax.Precision.HIGHEST)
    return jnp.einsum("ai,hib->hab", pick, picked, precision=lax.Precision.HIGHEST)

def on_device(
    latent,
    bn_scale,
    bn_shift,
    w_expand,
    b_expand,
    dw_kernel,
    dw_bias,
    w_project,
    b_project,
    ln_gain,
    ln_bias,
    w_qkv,
    pos_bias,
    w_out,
    b_out,
):
    tile_h, tile_w, width = latent.shape
    hidden_width = w_expand.shape[1]
    rows_here = latent.shape[0]
    cols_here = latent.shape[1]
    wide_in = extended(latent, (("row", 0), ("col", 1)), 1)
    normed_in = (wide_in.astype(jnp.float32) * bn_scale + bn_shift).astype(jnp.bfloat16)
    hidden = (
        jnp.einsum("yxc,cd->yxd", normed_in, w_expand, preferred_element_type=jnp.float32)
        + b_expand
    )
    row_at = lax.axis_index("row") * rows_here - 1 + jnp.arange(rows_here + 2)
    col_at = lax.axis_index("col") * cols_here - 1 + jnp.arange(cols_here + 2)
    inside = ((row_at >= 0) & (row_at < lax.axis_size("row") * rows_here))[:, None] & (
        (col_at >= 0) & (col_at < lax.axis_size("col") * cols_here)
    )[None, :]
    hidden = gelu_tanh(hidden).astype(jnp.bfloat16)
    padded = jnp.where(inside[:, :, None], hidden, jnp.zeros_like(hidden))
    total = jnp.zeros((tile_h, tile_w, hidden_width), jnp.float32)
    for down in range(3):
        for across in range(3):
            total = total + padded[down : down + tile_h, across : across + tile_w].astype(
                jnp.float32
            ) * dw_kernel[down, across].astype(jnp.float32)
    depth = gelu_tanh(total + dw_bias).astype(jnp.bfloat16)
    proj = jnp.dot(depth.reshape(-1, hidden_width), w_project, preferred_element_type=jnp.float32)
    mid = (latent.reshape(-1, width).astype(jnp.float32) + proj + b_project).astype(jnp.bfloat16)
    sizes = layout_sizes(tile_h, tile_w)
    plan = runs_plan(tile_h, tile_w)
    if plan is not None:
        arrived = send_runs(mid.reshape(tile_h, tile_w, width), plan)
        order = (lax.axis_size("row"), lax.axis_size("col"), plan["parts"], 1)
    else:
        arrived = send_to_owner(mid.reshape(tile_h, tile_w, width), sizes)
        order = (
            sizes["n_row"] // sizes["qr"], sizes["n_col"] // sizes["qc"], sizes["pr"], sizes["pc"]
        )
        assert sizes["qr"] == 1 or order[1] * order[2] * order[3] == 1
        assert sizes["qc"] == 1 or order[2] * order[3] == 1
        assert sizes["kr"] == 1 or order[3] == 1
    result = owner_block(arrived, ln_gain, ln_bias, w_qkv, arrived_bias(pos_bias, *order), w_out, b_out)
    if plan is not None:
        return back_runs(result, plan, tile_h, tile_w)
    return back_home(result, sizes, tile_h, tile_w)

def solution(mesh):
    return jax.shard_map(
        on_device,
        mesh=mesh,
        in_specs=(
            P("row", "col", None),
            P(),
            P(),
            P(),
            P(),
            P(),
            P(),
            P(),
            P(),
            P(),
            P(),
            P(),
            P(),
            P(),
            P(),
        ),
        out_specs=P("row", "col", None),
        check_vma=False,
    )
```

```python
import math

import numpy as np

import jax
import jax.numpy as jnp
from jax import lax
from jax.sharding import PartitionSpec as P
from jax.experimental import pallas as pl
from jax.experimental.pallas import tpu as pltpu

HEADS = 16
GRID = 8


def extended(block, sides, width):
    for axis, dim in sides:
        count = lax.axis_size(axis)
        forward = [(i, i + 1) for i in range(count - 1)]
        backward = [(target, source) for source, target in forward]
        low = lax.ppermute(
            lax.slice_in_dim(block, block.shape[dim] - width, None, axis=dim), axis, forward
        )
        high = lax.ppermute(lax.slice_in_dim(block, 0, width, axis=dim), axis, backward)
        block = jnp.concatenate([low, block, high], axis=dim)
    return block


def gelu_tanh(v):
    return jax.nn.gelu(v, approximate=True)


def layout_sizes(tile_h, tile_w):
    n_row = lax.axis_size("row")
    n_col = lax.axis_size("col")
    stride_h = tile_h * n_row // GRID
    stride_w = tile_w * n_col // GRID
    part_h = min(tile_h, stride_h)
    part_w = min(tile_w, stride_w)
    return dict(
        n_row=n_row,
        n_col=n_col,
        pr=tile_h // part_h,
        kr=part_h // n_row,
        qr=stride_h // part_h,
        pc=tile_w // part_w,
        kc=part_w // n_col,
        qc=stride_w // part_w,
    )


def to_owner(tile, sizes):
    tile_h, tile_w, feats = tile.shape
    message = sizes["pr"] * sizes["kr"] * sizes["pc"] * sizes["kc"]
    outgoing = tile.reshape(
        sizes["pr"], sizes["n_row"], sizes["kr"], sizes["pc"], sizes["n_col"], sizes["kc"], feats
    ).transpose(1, 4, 0, 2, 3, 5, 6)
    arrived = lax.all_to_all(
        outgoing.reshape(sizes["n_row"] * sizes["n_col"], message, feats),
        ("row", "col"),
        split_axis=0,
        concat_axis=0,
        tiled=True,
    )
    arrived = arrived.reshape(
        sizes["n_row"] // sizes["qr"],
        sizes["qr"],
        sizes["n_col"] // sizes["qc"],
        sizes["qc"],
        sizes["pr"],
        sizes["kr"],
        sizes["pc"],
        sizes["kc"],
        feats,
    )
    arrived = arrived.transpose(1, 5, 3, 7, 0, 4, 2, 6, 8)
    return arrived.reshape(
        sizes["qr"] * sizes["kr"] * sizes["qc"] * sizes["kc"], GRID * GRID, feats
    )


def to_home(grouped, sizes, tile_h, tile_w):
    feats = grouped.shape[-1]
    message = sizes["pr"] * sizes["kr"] * sizes["pc"] * sizes["kc"]
    outgoing = grouped.reshape(
        sizes["qr"],
        sizes["kr"],
        sizes["qc"],
        sizes["kc"],
        sizes["n_row"] // sizes["qr"],
        sizes["pr"],
        sizes["n_col"] // sizes["qc"],
        sizes["pc"],
        feats,
    )
    outgoing = outgoing.transpose(4, 0, 6, 2, 5, 1, 7, 3, 8)
    back = lax.all_to_all(
        outgoing.reshape(sizes["n_row"] * sizes["n_col"], message, feats),
        ("row", "col"),
        split_axis=0,
        concat_axis=0,
        tiled=True,
    )
    back = back.reshape(
        sizes["n_row"], sizes["n_col"], sizes["pr"], sizes["kr"], sizes["pc"], sizes["kc"], feats
    ).transpose(2, 0, 3, 4, 1, 5, 6)
    return back.reshape(tile_h, tile_w, feats)


def attend(qkv, pos_bias):
    groups, members, three = qkv.shape
    width = three // 3
    head_dim = width // HEADS
    query = qkv[:, :, :width].reshape(groups, members, HEADS, head_dim)
    keys = qkv[:, :, width : 2 * width].reshape(groups, members, HEADS, head_dim)
    values = qkv[:, :, 2 * width :].reshape(groups, members, HEADS, head_dim)
    scores = (
        jnp.einsum("gihd,gjhd->ghij", query, keys, preferred_element_type=jnp.float32)
        * head_dim ** (-0.5)
        + pos_bias[None]
    )
    top = jnp.max(scores, axis=-1, keepdims=True)
    expo = jnp.exp(scores - top)
    probs = (expo / jnp.sum(expo, axis=-1, keepdims=True)).astype(jnp.bfloat16)
    mixed = jnp.einsum("ghij,gjhd->gihd", probs, values, preferred_element_type=jnp.float32)
    return mixed.astype(jnp.bfloat16).reshape(groups, members, width)


def owner_kernel(mid_ref, gain_ref, bias_ref, wqkv_ref, pos_ref, wout_ref, bout_ref, out_ref, qkv_ref, att_ref):
    rows_all, width = mid_ref.shape
    lanes = qkv_ref.shape[-1]
    members = pos_ref.shape[-1]
    groups = rows_all // members
    head_dim = width // HEADS
    values = mid_ref[...].astype(jnp.float32)
    mean = jnp.mean(values, axis=-1, keepdims=True)
    centred = values - mean
    var = jnp.mean(jnp.square(centred), axis=-1, keepdims=True)
    normed = (centred * lax.rsqrt(var + 1e-05) * gain_ref[...] + bias_ref[...]).astype(jnp.bfloat16)
    qkv = jnp.dot(normed, wqkv_ref[...], preferred_element_type=jnp.float32)
    qkv = qkv.astype(jnp.bfloat16).astype(jnp.float32)
    for t in range(qkv_ref.shape[0]):
        qkv_ref[t] = qkv[:, t * lanes : (t + 1) * lanes]
    tiles = width // lanes
    per_tile = lanes // head_dim
    head_of = lax.broadcasted_iota(jnp.int32, (1, lanes), 1) // head_dim
    for g in range(groups):
        rows = pl.ds(g, members, stride=groups)
        for k in range(tiles):
            query = qkv_ref[k, rows, :].astype(jnp.bfloat16)
            keys = qkv_ref[tiles + k, rows, :].astype(jnp.bfloat16)
            vals = qkv_ref[2 * tiles + k, rows, :].astype(jnp.bfloat16)
            masked = jnp.concatenate(
                [jnp.where(head_of == t, query, jnp.zeros_like(query)) for t in range(per_tile)], axis=0
            )
            scores = lax.dot_general(
                masked, keys, (((1,), (1,)), ((), ())), preferred_element_type=jnp.float32
            ) * head_dim ** (-0.5) + pos_ref[k]
            top = jnp.max(scores, axis=-1, keepdims=True)
            expo = jnp.exp(scores - top)
            probs = (expo / jnp.sum(expo, axis=-1, keepdims=True)).astype(jnp.bfloat16)
            mixed = jnp.dot(probs, vals, preferred_element_type=jnp.float32)
            picked = jnp.where(head_of == 0, mixed[:members], 0.0)
            for t in range(1, per_tile):
                picked = picked + jnp.where(head_of == t, mixed[t * members : (t + 1) * members], 0.0)
            att_ref[k, rows, :] = picked.astype(jnp.bfloat16).astype(jnp.float32)
    attended = jnp.concatenate([att_ref[k] for k in range(tiles)], axis=1).astype(jnp.bfloat16)
    result = values + jnp.dot(attended, wout_ref[...], preferred_element_type=jnp.float32) + bout_ref[...]
    out_ref[...] = result.astype(jnp.bfloat16)


def owner_block(arrived, ln_gain, ln_bias, w_qkv, pos_bias, w_out, b_out):
    rows_all, width = arrived.shape
    members = pos_bias.shape[-1]
    lanes = 128
    whole = lambda shape: pl.BlockSpec(shape, lambda: (0,) * len(shape))
    return pl.pallas_call(
        owner_kernel,
        out_shape=jax.ShapeDtypeStruct(arrived.shape, jnp.bfloat16),
        in_specs=[
            whole(arrived.shape),
            whole((1, width)),
            whole((1, width)),
            whole(w_qkv.shape),
            whole((width // lanes, lanes // (width // HEADS) * members, members)),
            whole(w_out.shape),
            whole((1, width)),
        ],
        out_specs=whole(arrived.shape),
        scratch_shapes=[
            pltpu.VMEM((3 * width // lanes, rows_all, lanes), jnp.float32),
            pltpu.VMEM((width // lanes, rows_all, lanes), jnp.float32),
        ],
    )(
        arrived,
        ln_gain.reshape(1, width),
        ln_bias.reshape(1, width),
        w_qkv,
        pos_bias.reshape(width // lanes, -1, members),
        w_out,
        b_out.reshape(1, width),
    )


def send_to_owner(tile, sizes):
    tile_h, tile_w, feats = tile.shape
    outgoing = tile.reshape(
        sizes["pr"], sizes["n_row"], sizes["kr"], sizes["pc"], sizes["n_col"], sizes["kc"], feats
    ).transpose(1, 4, 0, 2, 3, 5, 6)
    arrived = lax.all_to_all(
        outgoing.reshape(sizes["n_row"] * sizes["n_col"], -1, feats),
        ("row", "col"),
        split_axis=0,
        concat_axis=0,
        tiled=True,
    )
    return arrived.reshape(-1, feats)


def back_home(rows, sizes, tile_h, tile_w):
    feats = rows.shape[-1]
    back = lax.all_to_all(
        rows.reshape(sizes["n_row"] * sizes["n_col"], -1, feats),
        ("row", "col"),
        split_axis=0,
        concat_axis=0,
        tiled=True,
    )
    back = back.reshape(
        sizes["n_row"], sizes["n_col"], sizes["pr"], sizes["kr"], sizes["pc"], sizes["kc"], feats
    ).transpose(2, 0, 3, 4, 1, 5, 6)
    return back.reshape(tile_h, tile_w, feats)


def runs_plan(tile_h, tile_w):
    n_row = lax.axis_size("row")
    n_col = lax.axis_size("col")
    stride_h = tile_h * n_row // GRID
    stride_w = tile_w * n_col // GRID
    n_dev = n_row * n_col
    per_owner = stride_h * stride_w // n_dev
    if tile_w != stride_w or tile_h % stride_h or stride_w % per_owner or per_owner % 16:
        return None
    return dict(parts=tile_h // stride_h, stride_h=stride_h, blocks=stride_w // per_owner, run=per_owner)


def send_runs(tile, plan):
    feats = tile.shape[-1]
    outgoing = tile.reshape(
        plan["parts"], plan["stride_h"], plan["blocks"], plan["run"], feats
    ).transpose(1, 2, 0, 3, 4)
    arrived = lax.all_to_all(
        outgoing.reshape(plan["stride_h"] * plan["blocks"], -1, feats),
        ("row", "col"),
        split_axis=0,
        concat_axis=0,
        tiled=True,
    )
    return arrived.reshape(-1, feats)


def back_runs(rows, plan, tile_h, tile_w):
    feats = rows.shape[-1]
    back = lax.all_to_all(
        rows.reshape(plan["stride_h"] * plan["blocks"], -1, feats),
        ("row", "col"),
        split_axis=0,
        concat_axis=0,
        tiled=True,
    )
    back = back.reshape(
        plan["stride_h"], plan["blocks"], plan["parts"], plan["run"], feats
    ).transpose(2, 0, 1, 3, 4)
    return back.reshape(tile_h, tile_w, feats)


def arrived_bias(pos_bias, a, b, c, d):
    heads, members, _ = pos_bias.shape
    order = np.arange(members).reshape(a, c, b, d).transpose(0, 2, 1, 3).reshape(-1)
    pick = jnp.asarray(np.eye(members, dtype=np.float32)[order])
    picked = jnp.einsum("hij,bj->hib", pos_bias, pick, precision=lax.Precision.HIGHEST)
    return jnp.einsum("ai,hib->hab", pick, picked, precision=lax.Precision.HIGHEST)

def on_device(
    latent,
    bn_scale,
    bn_shift,
    w_expand,
    b_expand,
    dw_kernel,
    dw_bias,
    w_project,
    b_project,
    ln_gain,
    ln_bias,
    w_qkv,
    pos_bias,
    w_out,
    b_out,
):
    tile_h, tile_w, width = latent.shape
    hidden_width = w_expand.shape[1]
    rows_here = latent.shape[0]
    cols_here = latent.shape[1]
    wide_in = extended(latent, (("row", 0), ("col", 1)), 1)
    normed_in = (wide_in.astype(jnp.float32) * bn_scale + bn_shift).astype(jnp.bfloat16)
    hidden = (
        jnp.einsum("yxc,cd->yxd", normed_in, w_expand, preferred_element_type=jnp.float32)
        + b_expand
    )
    row_at = lax.axis_index("row") * rows_here - 1 + jnp.arange(rows_here + 2)
    col_at = lax.axis_index("col") * cols_here - 1 + jnp.arange(cols_here + 2)
    inside = ((row_at >= 0) & (row_at < lax.axis_size("row") * rows_here))[:, None] & (
        (col_at >= 0) & (col_at < lax.axis_size("col") * cols_here)
    )[None, :]
    hidden = lax.reduce_precision(gelu_tanh(hidden), exponent_bits=8, mantissa_bits=7)
    padded = jnp.where(inside[:, :, None], hidden, jnp.zeros_like(hidden))
    total = jnp.zeros((tile_h, tile_w, hidden_width), jnp.float32)
    for down in range(3):
        for across in range(3):
            total = total + padded[down : down + tile_h, across : across + tile_w].astype(
                jnp.float32
            ) * dw_kernel[down, across].astype(jnp.float32)
    depth = gelu_tanh(total + dw_bias).astype(jnp.bfloat16)
    proj = jnp.dot(depth.reshape(-1, hidden_width), w_project, preferred_element_type=jnp.float32)
    mid = (latent.reshape(-1, width).astype(jnp.float32) + proj + b_project).astype(jnp.bfloat16)
    sizes = layout_sizes(tile_h, tile_w)
    plan = runs_plan(tile_h, tile_w)
    if plan is not None:
        arrived = send_runs(mid.reshape(tile_h, tile_w, width), plan)
        order = (lax.axis_size("row"), lax.axis_size("col"), plan["parts"], 1)
    else:
        arrived = send_to_owner(mid.reshape(tile_h, tile_w, width), sizes)
        order = (
            sizes["n_row"] // sizes["qr"], sizes["n_col"] // sizes["qc"], sizes["pr"], sizes["pc"]
        )
        assert sizes["qr"] == 1 or order[1] * order[2] * order[3] == 1
        assert sizes["qc"] == 1 or order[2] * order[3] == 1
        assert sizes["kr"] == 1 or order[3] == 1
    result = owner_block(arrived, ln_gain, ln_bias, w_qkv, arrived_bias(pos_bias, *order), w_out, b_out)
    if plan is not None:
        return back_runs(result, plan, tile_h, tile_w)
    return back_home(result, sizes, tile_h, tile_w)

def solution(mesh):
    return jax.shard_map(
        on_device,
        mesh=mesh,
        in_specs=(
            P("row", "col", None),
            P(),
            P(),
            P(),
            P(),
            P(),
            P(),
            P(),
            P(),
            P(),
            P(),
            P(),
            P(),
            P(),
            P(),
        ),
        out_specs=P("row", "col", None),
        check_vma=False,
    )
```

```python
import math

import numpy as np

import jax
import jax.numpy as jnp
from jax import lax
from jax.sharding import PartitionSpec as P
from jax.experimental import pallas as pl
from jax.experimental.pallas import tpu as pltpu

HEADS = 16
GRID = 8


def extended(block, sides, width):
    for axis, dim in sides:
        count = lax.axis_size(axis)
        forward = [(i, i + 1) for i in range(count - 1)]
        backward = [(target, source) for source, target in forward]
        low = lax.ppermute(
            lax.slice_in_dim(block, block.shape[dim] - width, None, axis=dim), axis, forward
        )
        high = lax.ppermute(lax.slice_in_dim(block, 0, width, axis=dim), axis, backward)
        block = jnp.concatenate([low, block, high], axis=dim)
    return block


def gelu_tanh(v):
    return jax.nn.gelu(v, approximate=True)


def layout_sizes(tile_h, tile_w):
    n_row = lax.axis_size("row")
    n_col = lax.axis_size("col")
    stride_h = tile_h * n_row // GRID
    stride_w = tile_w * n_col // GRID
    part_h = min(tile_h, stride_h)
    part_w = min(tile_w, stride_w)
    return dict(
        n_row=n_row,
        n_col=n_col,
        pr=tile_h // part_h,
        kr=part_h // n_row,
        qr=stride_h // part_h,
        pc=tile_w // part_w,
        kc=part_w // n_col,
        qc=stride_w // part_w,
    )


def to_owner(tile, sizes):
    tile_h, tile_w, feats = tile.shape
    message = sizes["pr"] * sizes["kr"] * sizes["pc"] * sizes["kc"]
    outgoing = tile.reshape(
        sizes["pr"], sizes["n_row"], sizes["kr"], sizes["pc"], sizes["n_col"], sizes["kc"], feats
    ).transpose(1, 4, 0, 2, 3, 5, 6)
    arrived = lax.all_to_all(
        outgoing.reshape(sizes["n_row"] * sizes["n_col"], message, feats),
        ("row", "col"),
        split_axis=0,
        concat_axis=0,
        tiled=True,
    )
    arrived = arrived.reshape(
        sizes["n_row"] // sizes["qr"],
        sizes["qr"],
        sizes["n_col"] // sizes["qc"],
        sizes["qc"],
        sizes["pr"],
        sizes["kr"],
        sizes["pc"],
        sizes["kc"],
        feats,
    )
    arrived = arrived.transpose(1, 5, 3, 7, 0, 4, 2, 6, 8)
    return arrived.reshape(
        sizes["qr"] * sizes["kr"] * sizes["qc"] * sizes["kc"], GRID * GRID, feats
    )


def to_home(grouped, sizes, tile_h, tile_w):
    feats = grouped.shape[-1]
    message = sizes["pr"] * sizes["kr"] * sizes["pc"] * sizes["kc"]
    outgoing = grouped.reshape(
        sizes["qr"],
        sizes["kr"],
        sizes["qc"],
        sizes["kc"],
        sizes["n_row"] // sizes["qr"],
        sizes["pr"],
        sizes["n_col"] // sizes["qc"],
        sizes["pc"],
        feats,
    )
    outgoing = outgoing.transpose(4, 0, 6, 2, 5, 1, 7, 3, 8)
    back = lax.all_to_all(
        outgoing.reshape(sizes["n_row"] * sizes["n_col"], message, feats),
        ("row", "col"),
        split_axis=0,
        concat_axis=0,
        tiled=True,
    )
    back = back.reshape(
        sizes["n_row"], sizes["n_col"], sizes["pr"], sizes["kr"], sizes["pc"], sizes["kc"], feats
    ).transpose(2, 0, 3, 4, 1, 5, 6)
    return back.reshape(tile_h, tile_w, feats)


def attend(qkv, pos_bias):
    groups, members, three = qkv.shape
    width = three // 3
    head_dim = width // HEADS
    query = qkv[:, :, :width].reshape(groups, members, HEADS, head_dim)
    keys = qkv[:, :, width : 2 * width].reshape(groups, members, HEADS, head_dim)
    values = qkv[:, :, 2 * width :].reshape(groups, members, HEADS, head_dim)
    scores = (
        jnp.einsum("gihd,gjhd->ghij", query, keys, preferred_element_type=jnp.float32)
        * head_dim ** (-0.5)
        + pos_bias[None]
    )
    top = jnp.max(scores, axis=-1, keepdims=True)
    expo = jnp.exp(scores - top)
    probs = (expo / jnp.sum(expo, axis=-1, keepdims=True)).astype(jnp.bfloat16)
    mixed = jnp.einsum("ghij,gjhd->gihd", probs, values, preferred_element_type=jnp.float32)
    return mixed.astype(jnp.bfloat16).reshape(groups, members, width)


def owner_kernel(mid_ref, gain_ref, bias_ref, wqkv_ref, pos_ref, wout_ref, bout_ref, out_ref, qkv_ref, att_ref):
    rows_all, width = mid_ref.shape
    lanes = qkv_ref.shape[-1]
    members = pos_ref.shape[-1]
    groups = rows_all // members
    head_dim = width // HEADS
    values = mid_ref[...].astype(jnp.float32)
    mean = jnp.mean(values, axis=-1, keepdims=True)
    centred = values - mean
    var = jnp.mean(jnp.square(centred), axis=-1, keepdims=True)
    normed = (centred * lax.rsqrt(var + 1e-05) * gain_ref[...] + bias_ref[...]).astype(jnp.bfloat16)
    qkv = jnp.dot(normed, wqkv_ref[...], preferred_element_type=jnp.float32)
    qkv = qkv.astype(jnp.bfloat16).astype(jnp.float32)
    for t in range(qkv_ref.shape[0]):
        qkv_ref[t] = qkv[:, t * lanes : (t + 1) * lanes]
    tiles = width // lanes
    per_tile = lanes // head_dim
    head_of = lax.broadcasted_iota(jnp.int32, (1, lanes), 1) // head_dim
    for g in range(groups):
        rows = pl.ds(g, members, stride=groups)
        for k in range(tiles):
            query = qkv_ref[k, rows, :].astype(jnp.bfloat16)
            keys = qkv_ref[tiles + k, rows, :].astype(jnp.bfloat16)
            vals = qkv_ref[2 * tiles + k, rows, :].astype(jnp.bfloat16)
            masked = jnp.concatenate(
                [jnp.where(head_of == t, query, jnp.zeros_like(query)) for t in range(per_tile)], axis=0
            )
            scores = lax.dot_general(
                masked, keys, (((1,), (1,)), ((), ())), preferred_element_type=jnp.float32
            ) * head_dim ** (-0.5) + pos_ref[k]
            top = jnp.max(scores, axis=-1, keepdims=True)
            expo = jnp.exp(scores - top)
            probs = (expo / jnp.sum(expo, axis=-1, keepdims=True)).astype(jnp.bfloat16)
            mixed = jnp.dot(probs, vals, preferred_element_type=jnp.float32)
            picked = jnp.where(head_of == 0, mixed[:members], 0.0)
            for t in range(1, per_tile):
                picked = picked + jnp.where(head_of == t, mixed[t * members : (t + 1) * members], 0.0)
            att_ref[k, rows, :] = picked.astype(jnp.bfloat16).astype(jnp.float32)
    attended = jnp.concatenate([att_ref[k] for k in range(tiles)], axis=1).astype(jnp.bfloat16)
    result = values + jnp.dot(attended, wout_ref[...], preferred_element_type=jnp.float32) + bout_ref[...]
    out_ref[...] = result.astype(jnp.bfloat16)


def owner_block(arrived, ln_gain, ln_bias, w_qkv, pos_bias, w_out, b_out):
    rows_all, width = arrived.shape
    members = pos_bias.shape[-1]
    lanes = 128
    whole = lambda shape: pl.BlockSpec(shape, lambda: (0,) * len(shape))
    return pl.pallas_call(
        owner_kernel,
        out_shape=jax.ShapeDtypeStruct(arrived.shape, jnp.bfloat16),
        in_specs=[
            whole(arrived.shape),
            whole((1, width)),
            whole((1, width)),
            whole(w_qkv.shape),
            whole((width // lanes, lanes // (width // HEADS) * members, members)),
            whole(w_out.shape),
            whole((1, width)),
        ],
        out_specs=whole(arrived.shape),
        scratch_shapes=[
            pltpu.VMEM((3 * width // lanes, rows_all, lanes), jnp.float32),
            pltpu.VMEM((width // lanes, rows_all, lanes), jnp.float32),
        ],
    )(
        arrived,
        ln_gain.reshape(1, width),
        ln_bias.reshape(1, width),
        w_qkv,
        pos_bias.reshape(width // lanes, -1, members),
        w_out,
        b_out.reshape(1, width),
    )


def send_to_owner(tile, sizes):
    tile_h, tile_w, feats = tile.shape
    outgoing = tile.reshape(
        sizes["pr"], sizes["n_row"], sizes["kr"], sizes["pc"], sizes["n_col"], sizes["kc"], feats
    ).transpose(1, 4, 0, 2, 3, 5, 6)
    arrived = lax.all_to_all(
        outgoing.reshape(sizes["n_row"] * sizes["n_col"], -1, feats),
        ("row", "col"),
        split_axis=0,
        concat_axis=0,
        tiled=True,
    )
    return arrived.reshape(-1, feats)


def back_home(rows, sizes, tile_h, tile_w):
    feats = rows.shape[-1]
    back = lax.all_to_all(
        rows.reshape(sizes["n_row"] * sizes["n_col"], -1, feats),
        ("row", "col"),
        split_axis=0,
        concat_axis=0,
        tiled=True,
    )
    back = back.reshape(
        sizes["n_row"], sizes["n_col"], sizes["pr"], sizes["kr"], sizes["pc"], sizes["kc"], feats
    ).transpose(2, 0, 3, 4, 1, 5, 6)
    return back.reshape(tile_h, tile_w, feats)


def runs_plan(tile_h, tile_w):
    n_row = lax.axis_size("row")
    n_col = lax.axis_size("col")
    stride_h = tile_h * n_row // GRID
    stride_w = tile_w * n_col // GRID
    n_dev = n_row * n_col
    per_owner = stride_h * stride_w // n_dev
    if tile_w != stride_w or tile_h % stride_h or stride_w % per_owner or per_owner % 16:
        return None
    return dict(parts=tile_h // stride_h, stride_h=stride_h, blocks=stride_w // per_owner, run=per_owner)


def send_runs(tile, plan):
    feats = tile.shape[-1]
    outgoing = tile.reshape(
        plan["parts"], plan["stride_h"], plan["blocks"], plan["run"], feats
    ).transpose(1, 2, 0, 3, 4)
    arrived = lax.all_to_all(
        outgoing.reshape(plan["stride_h"] * plan["blocks"], -1, feats),
        ("row", "col"),
        split_axis=0,
        concat_axis=0,
        tiled=True,
    )
    return arrived.reshape(-1, feats)


def back_runs(rows, plan, tile_h, tile_w):
    feats = rows.shape[-1]
    back = lax.all_to_all(
        rows.reshape(plan["stride_h"] * plan["blocks"], -1, feats),
        ("row", "col"),
        split_axis=0,
        concat_axis=0,
        tiled=True,
    )
    back = back.reshape(
        plan["stride_h"], plan["blocks"], plan["parts"], plan["run"], feats
    ).transpose(2, 0, 1, 3, 4)
    return back.reshape(tile_h, tile_w, feats)


def arrived_bias(pos_bias, a, b, c, d):
    heads, members, _ = pos_bias.shape
    order = np.arange(members).reshape(a, c, b, d).transpose(0, 2, 1, 3).reshape(-1)
    pick = jnp.asarray(np.eye(members, dtype=np.float32)[order])
    picked = jnp.einsum("hij,bj->hib", pos_bias, pick, precision=lax.Precision.HIGHEST)
    return jnp.einsum("ai,hib->hab", pick, picked, precision=lax.Precision.HIGHEST)

def on_device(
    latent,
    bn_scale,
    bn_shift,
    w_expand,
    b_expand,
    dw_kernel,
    dw_bias,
    w_project,
    b_project,
    ln_gain,
    ln_bias,
    w_qkv,
    pos_bias,
    w_out,
    b_out,
):
    tile_h, tile_w, width = latent.shape
    hidden_width = w_expand.shape[1]
    rows_here = latent.shape[0]
    cols_here = latent.shape[1]
    wide_in = extended(latent, (("row", 0), ("col", 1)), 1)
    normed_in = (wide_in.astype(jnp.float32) * bn_scale + bn_shift).astype(jnp.bfloat16)
    blocks = hidden_width // 128
    hidden = jnp.einsum(
        "yxc,cbl->yxbl",
        normed_in,
        w_expand.reshape(width, blocks, 128),
        preferred_element_type=jnp.float32,
    ) + b_expand.reshape(blocks, 128)
    row_at = lax.axis_index("row") * rows_here - 1 + jnp.arange(rows_here + 2)
    col_at = lax.axis_index("col") * cols_here - 1 + jnp.arange(cols_here + 2)
    inside = ((row_at >= 0) & (row_at < lax.axis_size("row") * rows_here))[:, None] & (
        (col_at >= 0) & (col_at < lax.axis_size("col") * cols_here)
    )[None, :]
    hidden = gelu_tanh(hidden).astype(jnp.bfloat16)
    padded = jnp.where(inside[:, :, None, None], hidden, jnp.zeros_like(hidden))
    taps = dw_kernel.astype(jnp.float32).reshape(3, 3, blocks, 128)
    total = jnp.zeros((tile_h, tile_w, blocks, 128), jnp.float32)
    for down in range(3):
        for across in range(3):
            total = total + padded[down : down + tile_h, across : across + tile_w].astype(
                jnp.float32
            ) * taps[down, across]
    depth = gelu_tanh(total + dw_bias.reshape(blocks, 128)).astype(jnp.bfloat16)
    proj = jnp.dot(depth.reshape(-1, hidden_width), w_project, preferred_element_type=jnp.float32)
    mid = (latent.reshape(-1, width).astype(jnp.float32) + proj + b_project).astype(jnp.bfloat16)
    sizes = layout_sizes(tile_h, tile_w)
    plan = runs_plan(tile_h, tile_w)
    if plan is not None:
        arrived = send_runs(mid.reshape(tile_h, tile_w, width), plan)
        order = (lax.axis_size("row"), lax.axis_size("col"), plan["parts"], 1)
    else:
        arrived = send_to_owner(mid.reshape(tile_h, tile_w, width), sizes)
        order = (
            sizes["n_row"] // sizes["qr"], sizes["n_col"] // sizes["qc"], sizes["pr"], sizes["pc"]
        )
        assert sizes["qr"] == 1 or order[1] * order[2] * order[3] == 1
        assert sizes["qc"] == 1 or order[2] * order[3] == 1
        assert sizes["kr"] == 1 or order[3] == 1
    result = owner_block(arrived, ln_gain, ln_bias, w_qkv, arrived_bias(pos_bias, *order), w_out, b_out)
    if plan is not None:
        return back_runs(result, plan, tile_h, tile_w)
    return back_home(result, sizes, tile_h, tile_w)

def solution(mesh):
    return jax.shard_map(
        on_device,
        mesh=mesh,
        in_specs=(
            P("row", "col", None),
            P(),
            P(),
            P(),
            P(),
            P(),
            P(),
            P(),
            P(),
            P(),
            P(),
            P(),
            P(),
            P(),
            P(),
        ),
        out_specs=P("row", "col", None),
        check_vma=False,
    )
```

```python
import math

import numpy as np

import jax
import jax.numpy as jnp
from jax import lax
from jax.sharding import PartitionSpec as P
from jax.experimental import pallas as pl
from jax.experimental.pallas import tpu as pltpu

HEADS = 16
GRID = 8


def extended(block, sides, width):
    for axis, dim in sides:
        count = lax.axis_size(axis)
        forward = [(i, i + 1) for i in range(count - 1)]
        backward = [(target, source) for source, target in forward]
        low = lax.ppermute(
            lax.slice_in_dim(block, block.shape[dim] - width, None, axis=dim), axis, forward
        )
        high = lax.ppermute(lax.slice_in_dim(block, 0, width, axis=dim), axis, backward)
        block = jnp.concatenate([low, block, high], axis=dim)
    return block


def gelu_tanh(v):
    return jax.nn.gelu(v, approximate=True)


def layout_sizes(tile_h, tile_w):
    n_row = lax.axis_size("row")
    n_col = lax.axis_size("col")
    stride_h = tile_h * n_row // GRID
    stride_w = tile_w * n_col // GRID
    part_h = min(tile_h, stride_h)
    part_w = min(tile_w, stride_w)
    return dict(
        n_row=n_row,
        n_col=n_col,
        pr=tile_h // part_h,
        kr=part_h // n_row,
        qr=stride_h // part_h,
        pc=tile_w // part_w,
        kc=part_w // n_col,
        qc=stride_w // part_w,
    )


def to_owner(tile, sizes):
    tile_h, tile_w, feats = tile.shape
    message = sizes["pr"] * sizes["kr"] * sizes["pc"] * sizes["kc"]
    outgoing = tile.reshape(
        sizes["pr"], sizes["n_row"], sizes["kr"], sizes["pc"], sizes["n_col"], sizes["kc"], feats
    ).transpose(1, 4, 0, 2, 3, 5, 6)
    arrived = lax.all_to_all(
        outgoing.reshape(sizes["n_row"] * sizes["n_col"], message, feats),
        ("row", "col"),
        split_axis=0,
        concat_axis=0,
        tiled=True,
    )
    arrived = arrived.reshape(
        sizes["n_row"] // sizes["qr"],
        sizes["qr"],
        sizes["n_col"] // sizes["qc"],
        sizes["qc"],
        sizes["pr"],
        sizes["kr"],
        sizes["pc"],
        sizes["kc"],
        feats,
    )
    arrived = arrived.transpose(1, 5, 3, 7, 0, 4, 2, 6, 8)
    return arrived.reshape(
        sizes["qr"] * sizes["kr"] * sizes["qc"] * sizes["kc"], GRID * GRID, feats
    )


def to_home(grouped, sizes, tile_h, tile_w):
    feats = grouped.shape[-1]
    message = sizes["pr"] * sizes["kr"] * sizes["pc"] * sizes["kc"]
    outgoing = grouped.reshape(
        sizes["qr"],
        sizes["kr"],
        sizes["qc"],
        sizes["kc"],
        sizes["n_row"] // sizes["qr"],
        sizes["pr"],
        sizes["n_col"] // sizes["qc"],
        sizes["pc"],
        feats,
    )
    outgoing = outgoing.transpose(4, 0, 6, 2, 5, 1, 7, 3, 8)
    back = lax.all_to_all(
        outgoing.reshape(sizes["n_row"] * sizes["n_col"], message, feats),
        ("row", "col"),
        split_axis=0,
        concat_axis=0,
        tiled=True,
    )
    back = back.reshape(
        sizes["n_row"], sizes["n_col"], sizes["pr"], sizes["kr"], sizes["pc"], sizes["kc"], feats
    ).transpose(2, 0, 3, 4, 1, 5, 6)
    return back.reshape(tile_h, tile_w, feats)


def attend(qkv, pos_bias):
    groups, members, three = qkv.shape
    width = three // 3
    head_dim = width // HEADS
    query = qkv[:, :, :width].reshape(groups, members, HEADS, head_dim)
    keys = qkv[:, :, width : 2 * width].reshape(groups, members, HEADS, head_dim)
    values = qkv[:, :, 2 * width :].reshape(groups, members, HEADS, head_dim)
    scores = (
        jnp.einsum("gihd,gjhd->ghij", query, keys, preferred_element_type=jnp.float32)
        * head_dim ** (-0.5)
        + pos_bias[None]
    )
    top = jnp.max(scores, axis=-1, keepdims=True)
    expo = jnp.exp(scores - top)
    probs = (expo / jnp.sum(expo, axis=-1, keepdims=True)).astype(jnp.bfloat16)
    mixed = jnp.einsum("ghij,gjhd->gihd", probs, values, preferred_element_type=jnp.float32)
    return mixed.astype(jnp.bfloat16).reshape(groups, members, width)


def owner_kernel(mid_ref, gain_ref, bias_ref, wqkv_ref, pos_ref, wout_ref, bout_ref, out_ref, qkv_ref, att_ref):
    rows_all, width = mid_ref.shape
    lanes = qkv_ref.shape[-1]
    members = pos_ref.shape[-1]
    groups = rows_all // members
    head_dim = width // HEADS
    values = mid_ref[...].astype(jnp.float32)
    mean = jnp.mean(values, axis=-1, keepdims=True)
    centred = values - mean
    var = jnp.mean(jnp.square(centred), axis=-1, keepdims=True)
    normed = (centred * lax.rsqrt(var + 1e-05) * gain_ref[...] + bias_ref[...]).astype(jnp.bfloat16)
    qkv = jnp.dot(normed, wqkv_ref[...], preferred_element_type=jnp.float32)
    qkv = qkv.astype(jnp.bfloat16).astype(jnp.float32)
    for t in range(qkv_ref.shape[0]):
        qkv_ref[t] = qkv[:, t * lanes : (t + 1) * lanes]
    tiles = width // lanes
    per_tile = lanes // head_dim
    head_of = lax.broadcasted_iota(jnp.int32, (1, lanes), 1) // head_dim
    for g in range(groups):
        rows = pl.ds(g, members, stride=groups)
        for k in range(tiles):
            query = qkv_ref[k, rows, :].astype(jnp.bfloat16)
            keys = qkv_ref[tiles + k, rows, :].astype(jnp.bfloat16)
            vals = qkv_ref[2 * tiles + k, rows, :].astype(jnp.bfloat16)
            masked = jnp.concatenate(
                [jnp.where(head_of == t, query, jnp.zeros_like(query)) for t in range(per_tile)], axis=0
            )
            scores = lax.dot_general(
                masked, keys, (((1,), (1,)), ((), ())), preferred_element_type=jnp.float32
            ) * head_dim ** (-0.5) + pos_ref[k]
            top = jnp.max(scores, axis=-1, keepdims=True)
            expo = jnp.exp(scores - top)
            probs = (expo * (1.0 / jnp.sum(expo, axis=-1, keepdims=True))).astype(jnp.bfloat16)
            mixed = jnp.dot(probs, vals, preferred_element_type=jnp.float32)
            picked = jnp.where(head_of == 0, mixed[:members], 0.0)
            for t in range(1, per_tile):
                picked = picked + jnp.where(head_of == t, mixed[t * members : (t + 1) * members], 0.0)
            att_ref[k, rows, :] = picked.astype(jnp.bfloat16).astype(jnp.float32)
    attended = jnp.concatenate([att_ref[k] for k in range(tiles)], axis=1).astype(jnp.bfloat16)
    result = values + jnp.dot(attended, wout_ref[...], preferred_element_type=jnp.float32) + bout_ref[...]
    out_ref[...] = result.astype(jnp.bfloat16)


def owner_block(arrived, ln_gain, ln_bias, w_qkv, pos_bias, w_out, b_out):
    rows_all, width = arrived.shape
    members = pos_bias.shape[-1]
    lanes = 128
    whole = lambda shape: pl.BlockSpec(shape, lambda: (0,) * len(shape))
    return pl.pallas_call(
        owner_kernel,
        out_shape=jax.ShapeDtypeStruct(arrived.shape, jnp.bfloat16),
        in_specs=[
            whole(arrived.shape),
            whole((1, width)),
            whole((1, width)),
            whole(w_qkv.shape),
            whole((width // lanes, lanes // (width // HEADS) * members, members)),
            whole(w_out.shape),
            whole((1, width)),
        ],
        out_specs=whole(arrived.shape),
        scratch_shapes=[
            pltpu.VMEM((3 * width // lanes, rows_all, lanes), jnp.float32),
            pltpu.VMEM((width // lanes, rows_all, lanes), jnp.float32),
        ],
    )(
        arrived,
        ln_gain.reshape(1, width),
        ln_bias.reshape(1, width),
        w_qkv,
        pos_bias.reshape(width // lanes, -1, members),
        w_out,
        b_out.reshape(1, width),
    )


def send_to_owner(tile, sizes):
    tile_h, tile_w, feats = tile.shape
    outgoing = tile.reshape(
        sizes["pr"], sizes["n_row"], sizes["kr"], sizes["pc"], sizes["n_col"], sizes["kc"], feats
    ).transpose(1, 4, 0, 2, 3, 5, 6)
    arrived = lax.all_to_all(
        outgoing.reshape(sizes["n_row"] * sizes["n_col"], -1, feats),
        ("row", "col"),
        split_axis=0,
        concat_axis=0,
        tiled=True,
    )
    return arrived.reshape(-1, feats)


def back_home(rows, sizes, tile_h, tile_w):
    feats = rows.shape[-1]
    back = lax.all_to_all(
        rows.reshape(sizes["n_row"] * sizes["n_col"], -1, feats),
        ("row", "col"),
        split_axis=0,
        concat_axis=0,
        tiled=True,
    )
    back = back.reshape(
        sizes["n_row"], sizes["n_col"], sizes["pr"], sizes["kr"], sizes["pc"], sizes["kc"], feats
    ).transpose(2, 0, 3, 4, 1, 5, 6)
    return back.reshape(tile_h, tile_w, feats)


def runs_plan(tile_h, tile_w):
    n_row = lax.axis_size("row")
    n_col = lax.axis_size("col")
    stride_h = tile_h * n_row // GRID
    stride_w = tile_w * n_col // GRID
    n_dev = n_row * n_col
    per_owner = stride_h * stride_w // n_dev
    if tile_w != stride_w or tile_h % stride_h or stride_w % per_owner or per_owner % 16:
        return None
    return dict(parts=tile_h // stride_h, stride_h=stride_h, blocks=stride_w // per_owner, run=per_owner)


def send_runs(tile, plan):
    feats = tile.shape[-1]
    outgoing = tile.reshape(
        plan["parts"], plan["stride_h"], plan["blocks"], plan["run"], feats
    ).transpose(1, 2, 0, 3, 4)
    arrived = lax.all_to_all(
        outgoing.reshape(plan["stride_h"] * plan["blocks"], -1, feats),
        ("row", "col"),
        split_axis=0,
        concat_axis=0,
        tiled=True,
    )
    return arrived.reshape(-1, feats)


def back_runs(rows, plan, tile_h, tile_w):
    feats = rows.shape[-1]
    back = lax.all_to_all(
        rows.reshape(plan["stride_h"] * plan["blocks"], -1, feats),
        ("row", "col"),
        split_axis=0,
        concat_axis=0,
        tiled=True,
    )
    back = back.reshape(
        plan["stride_h"], plan["blocks"], plan["parts"], plan["run"], feats
    ).transpose(2, 0, 1, 3, 4)
    return back.reshape(tile_h, tile_w, feats)


def arrived_bias(pos_bias, a, b, c, d):
    heads, members, _ = pos_bias.shape
    order = np.arange(members).reshape(a, c, b, d).transpose(0, 2, 1, 3).reshape(-1)
    pick = jnp.asarray(np.eye(members, dtype=np.float32)[order])
    picked = jnp.einsum("hij,bj->hib", pos_bias, pick, precision=lax.Precision.HIGHEST)
    return jnp.einsum("ai,hib->hab", pick, picked, precision=lax.Precision.HIGHEST)

def on_device(
    latent,
    bn_scale,
    bn_shift,
    w_expand,
    b_expand,
    dw_kernel,
    dw_bias,
    w_project,
    b_project,
    ln_gain,
    ln_bias,
    w_qkv,
    pos_bias,
    w_out,
    b_out,
):
    tile_h, tile_w, width = latent.shape
    hidden_width = w_expand.shape[1]
    rows_here = latent.shape[0]
    cols_here = latent.shape[1]
    wide_in = extended(latent, (("row", 0), ("col", 1)), 1)
    normed_in = (wide_in.astype(jnp.float32) * bn_scale + bn_shift).astype(jnp.bfloat16)
    hidden = (
        jnp.einsum("yxc,cd->yxd", normed_in, w_expand, preferred_element_type=jnp.float32)
        + b_expand
    )
    row_at = lax.axis_index("row") * rows_here - 1 + jnp.arange(rows_here + 2)
    col_at = lax.axis_index("col") * cols_here - 1 + jnp.arange(cols_here + 2)
    inside = ((row_at >= 0) & (row_at < lax.axis_size("row") * rows_here))[:, None] & (
        (col_at >= 0) & (col_at < lax.axis_size("col") * cols_here)
    )[None, :]
    hidden = gelu_tanh(hidden).astype(jnp.bfloat16)
    padded = jnp.where(inside[:, :, None], hidden, jnp.zeros_like(hidden))
    total = jnp.zeros((tile_h, tile_w, hidden_width), jnp.float32)
    for down in range(3):
        for across in range(3):
            total = total + padded[down : down + tile_h, across : across + tile_w].astype(
                jnp.float32
            ) * dw_kernel[down, across].astype(jnp.float32)
    depth = gelu_tanh(total + dw_bias).astype(jnp.bfloat16)
    proj = jnp.dot(depth.reshape(-1, hidden_width), w_project, preferred_element_type=jnp.float32)
    mid = (latent.reshape(-1, width).astype(jnp.float32) + proj + b_project).astype(jnp.bfloat16)
    sizes = layout_sizes(tile_h, tile_w)
    plan = runs_plan(tile_h, tile_w)
    if plan is not None:
        arrived = send_runs(mid.reshape(tile_h, tile_w, width), plan)
        order = (lax.axis_size("row"), lax.axis_size("col"), plan["parts"], 1)
    else:
        arrived = send_to_owner(mid.reshape(tile_h, tile_w, width), sizes)
        order = (
            sizes["n_row"] // sizes["qr"], sizes["n_col"] // sizes["qc"], sizes["pr"], sizes["pc"]
        )
        assert sizes["qr"] == 1 or order[1] * order[2] * order[3] == 1
        assert sizes["qc"] == 1 or order[2] * order[3] == 1
        assert sizes["kr"] == 1 or order[3] == 1
    result = owner_block(arrived, ln_gain, ln_bias, w_qkv, arrived_bias(pos_bias, *order), w_out, b_out)
    if plan is not None:
        return back_runs(result, plan, tile_h, tile_w)
    return back_home(result, sizes, tile_h, tile_w)

def solution(mesh):
    return jax.shard_map(
        on_device,
        mesh=mesh,
        in_specs=(
            P("row", "col", None),
            P(),
            P(),
            P(),
            P(),
            P(),
            P(),
            P(),
            P(),
            P(),
            P(),
            P(),
            P(),
            P(),
            P(),
        ),
        out_specs=P("row", "col", None),
        check_vma=False,
    )
```

```python
import math

import numpy as np

import jax
import jax.numpy as jnp
from jax import lax
from jax.sharding import PartitionSpec as P
from jax.experimental import pallas as pl
from jax.experimental.pallas import tpu as pltpu

HEADS = 16
GRID = 8


def extended(block, sides, width):
    for axis, dim in sides:
        count = lax.axis_size(axis)
        forward = [(i, i + 1) for i in range(count - 1)]
        backward = [(target, source) for source, target in forward]
        low = lax.ppermute(
            lax.slice_in_dim(block, block.shape[dim] - width, None, axis=dim), axis, forward
        )
        high = lax.ppermute(lax.slice_in_dim(block, 0, width, axis=dim), axis, backward)
        block = jnp.concatenate([low, block, high], axis=dim)
    return block


def gelu_tanh(v):
    return jax.nn.gelu(v, approximate=True)


def layout_sizes(tile_h, tile_w):
    n_row = lax.axis_size("row")
    n_col = lax.axis_size("col")
    stride_h = tile_h * n_row // GRID
    stride_w = tile_w * n_col // GRID
    part_h = min(tile_h, stride_h)
    part_w = min(tile_w, stride_w)
    return dict(
        n_row=n_row,
        n_col=n_col,
        pr=tile_h // part_h,
        kr=part_h // n_row,
        qr=stride_h // part_h,
        pc=tile_w // part_w,
        kc=part_w // n_col,
        qc=stride_w // part_w,
    )


def to_owner(tile, sizes):
    tile_h, tile_w, feats = tile.shape
    message = sizes["pr"] * sizes["kr"] * sizes["pc"] * sizes["kc"]
    outgoing = tile.reshape(
        sizes["pr"], sizes["n_row"], sizes["kr"], sizes["pc"], sizes["n_col"], sizes["kc"], feats
    ).transpose(1, 4, 0, 2, 3, 5, 6)
    arrived = lax.all_to_all(
        outgoing.reshape(sizes["n_row"] * sizes["n_col"], message, feats),
        ("row", "col"),
        split_axis=0,
        concat_axis=0,
        tiled=True,
    )
    arrived = arrived.reshape(
        sizes["n_row"] // sizes["qr"],
        sizes["qr"],
        sizes["n_col"] // sizes["qc"],
        sizes["qc"],
        sizes["pr"],
        sizes["kr"],
        sizes["pc"],
        sizes["kc"],
        feats,
    )
    arrived = arrived.transpose(1, 5, 3, 7, 0, 4, 2, 6, 8)
    return arrived.reshape(
        sizes["qr"] * sizes["kr"] * sizes["qc"] * sizes["kc"], GRID * GRID, feats
    )


def to_home(grouped, sizes, tile_h, tile_w):
    feats = grouped.shape[-1]
    message = sizes["pr"] * sizes["kr"] * sizes["pc"] * sizes["kc"]
    outgoing = grouped.reshape(
        sizes["qr"],
        sizes["kr"],
        sizes["qc"],
        sizes["kc"],
        sizes["n_row"] // sizes["qr"],
        sizes["pr"],
        sizes["n_col"] // sizes["qc"],
        sizes["pc"],
        feats,
    )
    outgoing = outgoing.transpose(4, 0, 6, 2, 5, 1, 7, 3, 8)
    back = lax.all_to_all(
        outgoing.reshape(sizes["n_row"] * sizes["n_col"], message, feats),
        ("row", "col"),
        split_axis=0,
        concat_axis=0,
        tiled=True,
    )
    back = back.reshape(
        sizes["n_row"], sizes["n_col"], sizes["pr"], sizes["kr"], sizes["pc"], sizes["kc"], feats
    ).transpose(2, 0, 3, 4, 1, 5, 6)
    return back.reshape(tile_h, tile_w, feats)


def attend(qkv, pos_bias):
    groups, members, three = qkv.shape
    width = three // 3
    head_dim = width // HEADS
    query = qkv[:, :, :width].reshape(groups, members, HEADS, head_dim)
    keys = qkv[:, :, width : 2 * width].reshape(groups, members, HEADS, head_dim)
    values = qkv[:, :, 2 * width :].reshape(groups, members, HEADS, head_dim)
    scores = (
        jnp.einsum("gihd,gjhd->ghij", query, keys, preferred_element_type=jnp.float32)
        * head_dim ** (-0.5)
        + pos_bias[None]
    )
    top = jnp.max(scores, axis=-1, keepdims=True)
    expo = jnp.exp(scores - top)
    probs = (expo / jnp.sum(expo, axis=-1, keepdims=True)).astype(jnp.bfloat16)
    mixed = jnp.einsum("ghij,gjhd->gihd", probs, values, preferred_element_type=jnp.float32)
    return mixed.astype(jnp.bfloat16).reshape(groups, members, width)


def owner_kernel(mid_ref, gain_ref, bias_ref, wqkv_ref, pos_ref, wout_ref, bout_ref, out_ref, qkv_ref, att_ref):
    rows_all, width = mid_ref.shape
    lanes = qkv_ref.shape[-1]
    members = pos_ref.shape[-1]
    groups = rows_all // members
    head_dim = width // HEADS
    values = mid_ref[...].astype(jnp.float32)
    mean = jnp.mean(values, axis=-1, keepdims=True)
    centred = values - mean
    var = jnp.mean(jnp.square(centred), axis=-1, keepdims=True)
    normed = (centred * lax.rsqrt(var + 1e-05) * gain_ref[...] + bias_ref[...]).astype(jnp.bfloat16)
    qkv = jnp.dot(normed, wqkv_ref[...], preferred_element_type=jnp.float32)
    qkv = qkv.astype(jnp.bfloat16).astype(jnp.float32)
    for t in range(qkv_ref.shape[0]):
        qkv_ref[t] = qkv[:, t * lanes : (t + 1) * lanes]
    tiles = width // lanes
    per_tile = lanes // head_dim
    head_of = lax.broadcasted_iota(jnp.int32, (1, lanes), 1) // head_dim
    heads_all = width // head_dim
    head_all = lax.broadcasted_iota(jnp.int32, (1, width), 1) // head_dim
    for g in range(groups):
        rows = pl.ds(g, members, stride=groups)
        query = jnp.concatenate([qkv_ref[k, rows, :] for k in range(tiles)], axis=1).astype(jnp.bfloat16)
        keys = jnp.concatenate([qkv_ref[tiles + k, rows, :] for k in range(tiles)], axis=1).astype(jnp.bfloat16)
        vals = jnp.concatenate([qkv_ref[2 * tiles + k, rows, :] for k in range(tiles)], axis=1).astype(jnp.bfloat16)
        masked = jnp.concatenate(
            [jnp.where(head_all == t, query, jnp.zeros_like(query)) for t in range(heads_all)], axis=0
        )
        scores = lax.dot_general(
            masked, keys, (((1,), (1,)), ((), ())), preferred_element_type=jnp.float32
        ) * head_dim ** (-0.5) + pos_ref[...].reshape(heads_all * members, members)
        top = jnp.max(scores, axis=-1, keepdims=True)
        expo = jnp.exp(scores - top)
        probs = (expo / jnp.sum(expo, axis=-1, keepdims=True)).astype(jnp.bfloat16)
        mixed = jnp.dot(probs, vals, preferred_element_type=jnp.float32)
        for k in range(tiles):
            lo = k * lanes
            picked = jnp.where(head_of == 0, mixed[k * per_tile * members : (k * per_tile + 1) * members, lo : lo + lanes], 0.0)
            for t in range(1, per_tile):
                h = k * per_tile + t
                picked = picked + jnp.where(head_of == t, mixed[h * members : (h + 1) * members, lo : lo + lanes], 0.0)
            att_ref[k, rows, :] = picked.astype(jnp.bfloat16).astype(jnp.float32)
    attended = jnp.concatenate([att_ref[k] for k in range(tiles)], axis=1).astype(jnp.bfloat16)
    result = values + jnp.dot(attended, wout_ref[...], preferred_element_type=jnp.float32) + bout_ref[...]
    out_ref[...] = result.astype(jnp.bfloat16)


def owner_block(arrived, ln_gain, ln_bias, w_qkv, pos_bias, w_out, b_out):
    rows_all, width = arrived.shape
    members = pos_bias.shape[-1]
    lanes = 128
    whole = lambda shape: pl.BlockSpec(shape, lambda: (0,) * len(shape))
    return pl.pallas_call(
        owner_kernel,
        out_shape=jax.ShapeDtypeStruct(arrived.shape, jnp.bfloat16),
        in_specs=[
            whole(arrived.shape),
            whole((1, width)),
            whole((1, width)),
            whole(w_qkv.shape),
            whole((width // lanes, lanes // (width // HEADS) * members, members)),
            whole(w_out.shape),
            whole((1, width)),
        ],
        out_specs=whole(arrived.shape),
        scratch_shapes=[
            pltpu.VMEM((3 * width // lanes, rows_all, lanes), jnp.float32),
            pltpu.VMEM((width // lanes, rows_all, lanes), jnp.float32),
        ],
    )(
        arrived,
        ln_gain.reshape(1, width),
        ln_bias.reshape(1, width),
        w_qkv,
        pos_bias.reshape(width // lanes, -1, members),
        w_out,
        b_out.reshape(1, width),
    )


def send_to_owner(tile, sizes):
    tile_h, tile_w, feats = tile.shape
    outgoing = tile.reshape(
        sizes["pr"], sizes["n_row"], sizes["kr"], sizes["pc"], sizes["n_col"], sizes["kc"], feats
    ).transpose(1, 4, 0, 2, 3, 5, 6)
    arrived = lax.all_to_all(
        outgoing.reshape(sizes["n_row"] * sizes["n_col"], -1, feats),
        ("row", "col"),
        split_axis=0,
        concat_axis=0,
        tiled=True,
    )
    return arrived.reshape(-1, feats)


def back_home(rows, sizes, tile_h, tile_w):
    feats = rows.shape[-1]
    back = lax.all_to_all(
        rows.reshape(sizes["n_row"] * sizes["n_col"], -1, feats),
        ("row", "col"),
        split_axis=0,
        concat_axis=0,
        tiled=True,
    )
    back = back.reshape(
        sizes["n_row"], sizes["n_col"], sizes["pr"], sizes["kr"], sizes["pc"], sizes["kc"], feats
    ).transpose(2, 0, 3, 4, 1, 5, 6)
    return back.reshape(tile_h, tile_w, feats)


def runs_plan(tile_h, tile_w):
    n_row = lax.axis_size("row")
    n_col = lax.axis_size("col")
    stride_h = tile_h * n_row // GRID
    stride_w = tile_w * n_col // GRID
    n_dev = n_row * n_col
    per_owner = stride_h * stride_w // n_dev
    if tile_w != stride_w or tile_h % stride_h or stride_w % per_owner or per_owner % 16:
        return None
    return dict(parts=tile_h // stride_h, stride_h=stride_h, blocks=stride_w // per_owner, run=per_owner)


def send_runs(tile, plan):
    feats = tile.shape[-1]
    outgoing = tile.reshape(
        plan["parts"], plan["stride_h"], plan["blocks"], plan["run"], feats
    ).transpose(1, 2, 0, 3, 4)
    arrived = lax.all_to_all(
        outgoing.reshape(plan["stride_h"] * plan["blocks"], -1, feats),
        ("row", "col"),
        split_axis=0,
        concat_axis=0,
        tiled=True,
    )
    return arrived.reshape(-1, feats)


def back_runs(rows, plan, tile_h, tile_w):
    feats = rows.shape[-1]
    back = lax.all_to_all(
        rows.reshape(plan["stride_h"] * plan["blocks"], -1, feats),
        ("row", "col"),
        split_axis=0,
        concat_axis=0,
        tiled=True,
    )
    back = back.reshape(
        plan["stride_h"], plan["blocks"], plan["parts"], plan["run"], feats
    ).transpose(2, 0, 1, 3, 4)
    return back.reshape(tile_h, tile_w, feats)


def arrived_bias(pos_bias, a, b, c, d):
    heads, members, _ = pos_bias.shape
    order = np.arange(members).reshape(a, c, b, d).transpose(0, 2, 1, 3).reshape(-1)
    pick = jnp.asarray(np.eye(members, dtype=np.float32)[order])
    picked = jnp.einsum("hij,bj->hib", pos_bias, pick, precision=lax.Precision.HIGHEST)
    return jnp.einsum("ai,hib->hab", pick, picked, precision=lax.Precision.HIGHEST)

def on_device(
    latent,
    bn_scale,
    bn_shift,
    w_expand,
    b_expand,
    dw_kernel,
    dw_bias,
    w_project,
    b_project,
    ln_gain,
    ln_bias,
    w_qkv,
    pos_bias,
    w_out,
    b_out,
):
    tile_h, tile_w, width = latent.shape
    hidden_width = w_expand.shape[1]
    rows_here = latent.shape[0]
    cols_here = latent.shape[1]
    wide_in = extended(latent, (("row", 0), ("col", 1)), 1)
    normed_in = (wide_in.astype(jnp.float32) * bn_scale + bn_shift).astype(jnp.bfloat16)
    hidden = (
        jnp.einsum("yxc,cd->yxd", normed_in, w_expand, preferred_element_type=jnp.float32)
        + b_expand
    )
    row_at = lax.axis_index("row") * rows_here - 1 + jnp.arange(rows_here + 2)
    col_at = lax.axis_index("col") * cols_here - 1 + jnp.arange(cols_here + 2)
    inside = ((row_at >= 0) & (row_at < lax.axis_size("row") * rows_here))[:, None] & (
        (col_at >= 0) & (col_at < lax.axis_size("col") * cols_here)
    )[None, :]
    hidden = gelu_tanh(hidden).astype(jnp.bfloat16)
    padded = jnp.where(inside[:, :, None], hidden, jnp.zeros_like(hidden))
    total = jnp.zeros((tile_h, tile_w, hidden_width), jnp.float32)
    for down in range(3):
        for across in range(3):
            total = total + padded[down : down + tile_h, across : across + tile_w].astype(
                jnp.float32
            ) * dw_kernel[down, across].astype(jnp.float32)
    depth = gelu_tanh(total + dw_bias).astype(jnp.bfloat16)
    proj = jnp.dot(depth.reshape(-1, hidden_width), w_project, preferred_element_type=jnp.float32)
    mid = (latent.reshape(-1, width).astype(jnp.float32) + proj + b_project).astype(jnp.bfloat16)
    sizes = layout_sizes(tile_h, tile_w)
    plan = runs_plan(tile_h, tile_w)
    if plan is not None:
        arrived = send_runs(mid.reshape(tile_h, tile_w, width), plan)
        order = (lax.axis_size("row"), lax.axis_size("col"), plan["parts"], 1)
    else:
        arrived = send_to_owner(mid.reshape(tile_h, tile_w, width), sizes)
        order = (
            sizes["n_row"] // sizes["qr"], sizes["n_col"] // sizes["qc"], sizes["pr"], sizes["pc"]
        )
        assert sizes["qr"] == 1 or order[1] * order[2] * order[3] == 1
        assert sizes["qc"] == 1 or order[2] * order[3] == 1
        assert sizes["kr"] == 1 or order[3] == 1
    result = owner_block(arrived, ln_gain, ln_bias, w_qkv, arrived_bias(pos_bias, *order), w_out, b_out)
    if plan is not None:
        return back_runs(result, plan, tile_h, tile_w)
    return back_home(result, sizes, tile_h, tile_w)

def solution(mesh):
    return jax.shard_map(
        on_device,
        mesh=mesh,
        in_specs=(
            P("row", "col", None),
            P(),
            P(),
            P(),
            P(),
            P(),
            P(),
            P(),
            P(),
            P(),
            P(),
            P(),
            P(),
            P(),
            P(),
        ),
        out_specs=P("row", "col", None),
        check_vma=False,
    )
```

```python
import functools
import math

import numpy as np

import jax
import jax.numpy as jnp
from jax import lax
from jax.sharding import PartitionSpec as P
from jax.experimental import pallas as pl
from jax.experimental.pallas import tpu as pltpu

HEADS = 16
GRID = 8


def extended(block, sides, width):
    for axis, dim in sides:
        count = lax.axis_size(axis)
        forward = [(i, i + 1) for i in range(count - 1)]
        backward = [(target, source) for source, target in forward]
        low = lax.ppermute(
            lax.slice_in_dim(block, block.shape[dim] - width, None, axis=dim), axis, forward
        )
        high = lax.ppermute(lax.slice_in_dim(block, 0, width, axis=dim), axis, backward)
        block = jnp.concatenate([low, block, high], axis=dim)
    return block


def gelu_tanh(v):
    return jax.nn.gelu(v, approximate=True)


def layout_sizes(tile_h, tile_w):
    n_row = lax.axis_size("row")
    n_col = lax.axis_size("col")
    stride_h = tile_h * n_row // GRID
    stride_w = tile_w * n_col // GRID
    part_h = min(tile_h, stride_h)
    part_w = min(tile_w, stride_w)
    return dict(
        n_row=n_row,
        n_col=n_col,
        pr=tile_h // part_h,
        kr=part_h // n_row,
        qr=stride_h // part_h,
        pc=tile_w // part_w,
        kc=part_w // n_col,
        qc=stride_w // part_w,
    )


def to_owner(tile, sizes):
    tile_h, tile_w, feats = tile.shape
    message = sizes["pr"] * sizes["kr"] * sizes["pc"] * sizes["kc"]
    outgoing = tile.reshape(
        sizes["pr"], sizes["n_row"], sizes["kr"], sizes["pc"], sizes["n_col"], sizes["kc"], feats
    ).transpose(1, 4, 0, 2, 3, 5, 6)
    arrived = lax.all_to_all(
        outgoing.reshape(sizes["n_row"] * sizes["n_col"], message, feats),
        ("row", "col"),
        split_axis=0,
        concat_axis=0,
        tiled=True,
    )
    arrived = arrived.reshape(
        sizes["n_row"] // sizes["qr"],
        sizes["qr"],
        sizes["n_col"] // sizes["qc"],
        sizes["qc"],
        sizes["pr"],
        sizes["kr"],
        sizes["pc"],
        sizes["kc"],
        feats,
    )
    arrived = arrived.transpose(1, 5, 3, 7, 0, 4, 2, 6, 8)
    return arrived.reshape(
        sizes["qr"] * sizes["kr"] * sizes["qc"] * sizes["kc"], GRID * GRID, feats
    )


def to_home(grouped, sizes, tile_h, tile_w):
    feats = grouped.shape[-1]
    message = sizes["pr"] * sizes["kr"] * sizes["pc"] * sizes["kc"]
    outgoing = grouped.reshape(
        sizes["qr"],
        sizes["kr"],
        sizes["qc"],
        sizes["kc"],
        sizes["n_row"] // sizes["qr"],
        sizes["pr"],
        sizes["n_col"] // sizes["qc"],
        sizes["pc"],
        feats,
    )
    outgoing = outgoing.transpose(4, 0, 6, 2, 5, 1, 7, 3, 8)
    back = lax.all_to_all(
        outgoing.reshape(sizes["n_row"] * sizes["n_col"], message, feats),
        ("row", "col"),
        split_axis=0,
        concat_axis=0,
        tiled=True,
    )
    back = back.reshape(
        sizes["n_row"], sizes["n_col"], sizes["pr"], sizes["kr"], sizes["pc"], sizes["kc"], feats
    ).transpose(2, 0, 3, 4, 1, 5, 6)
    return back.reshape(tile_h, tile_w, feats)


def attend(qkv, pos_bias):
    groups, members, three = qkv.shape
    width = three // 3
    head_dim = width // HEADS
    query = qkv[:, :, :width].reshape(groups, members, HEADS, head_dim)
    keys = qkv[:, :, width : 2 * width].reshape(groups, members, HEADS, head_dim)
    values = qkv[:, :, 2 * width :].reshape(groups, members, HEADS, head_dim)
    scores = (
        jnp.einsum("gihd,gjhd->ghij", query, keys, preferred_element_type=jnp.float32)
        * head_dim ** (-0.5)
        + pos_bias[None]
    )
    top = jnp.max(scores, axis=-1, keepdims=True)
    expo = jnp.exp(scores - top)
    probs = (expo / jnp.sum(expo, axis=-1, keepdims=True)).astype(jnp.bfloat16)
    mixed = jnp.einsum("ghij,gjhd->gihd", probs, values, preferred_element_type=jnp.float32)
    return mixed.astype(jnp.bfloat16).reshape(groups, members, width)


def owner_kernel(pieces, mid_ref, gain_ref, bias_ref, wqkv_ref, pos_ref, wout_ref, bout_ref, out_ref, qkv_ref, att_ref):
    rows_all, width = mid_ref.shape
    lanes = qkv_ref.shape[-1]
    members = pos_ref.shape[-1]
    groups = rows_all // members
    head_dim = width // HEADS
    values = mid_ref[...].astype(jnp.float32)
    mean = jnp.mean(values, axis=-1, keepdims=True)
    centred = values - mean
    var = jnp.mean(jnp.square(centred), axis=-1, keepdims=True)
    normed = (centred * lax.rsqrt(var + 1e-05) * gain_ref[...] + bias_ref[...]).astype(jnp.bfloat16)
    qkv = jnp.dot(normed, wqkv_ref[...], preferred_element_type=jnp.float32)
    qkv = qkv.astype(jnp.bfloat16).astype(jnp.float32)
    for t in range(qkv_ref.shape[0]):
        qkv_ref[t] = qkv[:, t * lanes : (t + 1) * lanes]
    tiles = width // lanes
    per_tile = lanes // head_dim
    head_of = lax.broadcasted_iota(jnp.int32, (1, lanes), 1) // head_dim
    def gather(t, spans):
        return jnp.concatenate([qkv_ref[t, span, :] for span in spans], axis=0).astype(jnp.bfloat16)

    for g in range(groups):
        spans = pieces(g, groups, members)
        for k in range(tiles):
            query = gather(k, spans)
            keys = gather(tiles + k, spans)
            vals = gather(2 * tiles + k, spans)
            masked = jnp.concatenate(
                [jnp.where(head_of == t, query, jnp.zeros_like(query)) for t in range(per_tile)], axis=0
            )
            scores = lax.dot_general(
                masked, keys, (((1,), (1,)), ((), ())), preferred_element_type=jnp.float32
            ) * head_dim ** (-0.5) + pos_ref[k]
            top = jnp.max(scores, axis=-1, keepdims=True)
            expo = jnp.exp(scores - top)
            probs = (expo / jnp.sum(expo, axis=-1, keepdims=True)).astype(jnp.bfloat16)
            mixed = jnp.dot(probs, vals, preferred_element_type=jnp.float32)
            picked = jnp.where(head_of == 0, mixed[:members], 0.0)
            for t in range(1, per_tile):
                picked = picked + jnp.where(head_of == t, mixed[t * members : (t + 1) * members], 0.0)
            picked = picked.astype(jnp.bfloat16).astype(jnp.float32)
            at = 0
            for span in spans:
                att_ref[k, span, :] = picked[at : at + span.size]
                at += span.size
    attended = jnp.concatenate([att_ref[k] for k in range(tiles)], axis=1).astype(jnp.bfloat16)
    result = values + jnp.dot(attended, wout_ref[...], preferred_element_type=jnp.float32) + bout_ref[...]
    out_ref[...] = result.astype(jnp.bfloat16)


def strided_rows(g, groups, members):
    return [pl.ds(g, members, stride=groups)]


def owner_block(arrived, ln_gain, ln_bias, w_qkv, pos_bias, w_out, b_out, pieces=strided_rows):
    rows_all, width = arrived.shape
    members = pos_bias.shape[-1]
    lanes = 128
    whole = lambda shape: pl.BlockSpec(shape, lambda: (0,) * len(shape))
    return pl.pallas_call(
        functools.partial(owner_kernel, pieces),
        out_shape=jax.ShapeDtypeStruct(arrived.shape, jnp.bfloat16),
        in_specs=[
            whole(arrived.shape),
            whole((1, width)),
            whole((1, width)),
            whole(w_qkv.shape),
            whole((width // lanes, lanes // (width // HEADS) * members, members)),
            whole(w_out.shape),
            whole((1, width)),
        ],
        out_specs=whole(arrived.shape),
        scratch_shapes=[
            pltpu.VMEM((3 * width // lanes, rows_all, lanes), jnp.float32),
            pltpu.VMEM((width // lanes, rows_all, lanes), jnp.float32),
        ],
    )(
        arrived,
        ln_gain.reshape(1, width),
        ln_bias.reshape(1, width),
        w_qkv,
        pos_bias.reshape(width // lanes, -1, members),
        w_out,
        b_out.reshape(1, width),
    )


def send_to_owner(tile, sizes):
    tile_h, tile_w, feats = tile.shape
    outgoing = tile.reshape(
        sizes["pr"], sizes["n_row"], sizes["kr"], sizes["pc"], sizes["n_col"], sizes["kc"], feats
    ).transpose(1, 4, 0, 2, 3, 5, 6)
    arrived = lax.all_to_all(
        outgoing.reshape(sizes["n_row"] * sizes["n_col"], -1, feats),
        ("row", "col"),
        split_axis=0,
        concat_axis=0,
        tiled=True,
    )
    return arrived.reshape(-1, feats)


def back_home(rows, sizes, tile_h, tile_w):
    feats = rows.shape[-1]
    back = lax.all_to_all(
        rows.reshape(sizes["n_row"] * sizes["n_col"], -1, feats),
        ("row", "col"),
        split_axis=0,
        concat_axis=0,
        tiled=True,
    )
    back = back.reshape(
        sizes["n_row"], sizes["n_col"], sizes["pr"], sizes["kr"], sizes["pc"], sizes["kc"], feats
    ).transpose(2, 0, 3, 4, 1, 5, 6)
    return back.reshape(tile_h, tile_w, feats)


def runs_plan(tile_h, tile_w):
    n_row = lax.axis_size("row")
    n_col = lax.axis_size("col")
    stride_h = tile_h * n_row // GRID
    stride_w = tile_w * n_col // GRID
    n_dev = n_row * n_col
    per_owner = stride_h * stride_w // n_dev
    if tile_w != stride_w or tile_h % stride_h or stride_w % per_owner or per_owner % 16:
        return None
    return dict(parts=tile_h // stride_h, stride_h=stride_h, blocks=stride_w // per_owner, run=per_owner)


def send_runs(tile, plan):
    feats = tile.shape[-1]
    outgoing = tile.reshape(
        plan["parts"], plan["stride_h"], plan["blocks"], plan["run"], feats
    ).transpose(1, 2, 0, 3, 4)
    arrived = lax.all_to_all(
        outgoing.reshape(plan["stride_h"] * plan["blocks"], -1, feats),
        ("row", "col"),
        split_axis=0,
        concat_axis=1,
    )
    return arrived.reshape(-1, feats)


def block_rows(sources):
    def pieces(g, groups, members):
        return [pl.ds((p * groups + g) * sources, sources) for p in range(members // sources)]

    return pieces


def back_runs(rows, plan, tile_h, tile_w):
    feats = rows.shape[-1]
    n_dev = plan["stride_h"] * plan["blocks"]
    back = lax.all_to_all(
        rows.reshape(-1, n_dev, feats),
        ("row", "col"),
        split_axis=1,
        concat_axis=0,
    )
    back = back.reshape(
        plan["stride_h"], plan["blocks"], plan["parts"], plan["run"], feats
    ).transpose(2, 0, 1, 3, 4)
    return back.reshape(tile_h, tile_w, feats)


def arrived_bias(pos_bias, order):
    heads, members, _ = pos_bias.shape
    pick = jnp.asarray(np.eye(members, dtype=np.float32)[order])
    picked = jnp.einsum("hij,bj->hib", pos_bias, pick, precision=lax.Precision.HIGHEST)
    return jnp.einsum("ai,hib->hab", pick, picked, precision=lax.Precision.HIGHEST)

def on_device(
    latent,
    bn_scale,
    bn_shift,
    w_expand,
    b_expand,
    dw_kernel,
    dw_bias,
    w_project,
    b_project,
    ln_gain,
    ln_bias,
    w_qkv,
    pos_bias,
    w_out,
    b_out,
):
    tile_h, tile_w, width = latent.shape
    hidden_width = w_expand.shape[1]
    rows_here = latent.shape[0]
    cols_here = latent.shape[1]
    wide_in = extended(latent, (("row", 0), ("col", 1)), 1)
    normed_in = (wide_in.astype(jnp.float32) * bn_scale + bn_shift).astype(jnp.bfloat16)
    hidden = (
        jnp.einsum("yxc,cd->yxd", normed_in, w_expand, preferred_element_type=jnp.float32)
        + b_expand
    )
    row_at = lax.axis_index("row") * rows_here - 1 + jnp.arange(rows_here + 2)
    col_at = lax.axis_index("col") * cols_here - 1 + jnp.arange(cols_here + 2)
    inside = ((row_at >= 0) & (row_at < lax.axis_size("row") * rows_here))[:, None] & (
        (col_at >= 0) & (col_at < lax.axis_size("col") * cols_here)
    )[None, :]
    hidden = gelu_tanh(hidden).astype(jnp.bfloat16)
    padded = jnp.where(inside[:, :, None], hidden, jnp.zeros_like(hidden))
    total = jnp.zeros((tile_h, tile_w, hidden_width), jnp.float32)
    for down in range(3):
        for across in range(3):
            total = total + padded[down : down + tile_h, across : across + tile_w].astype(
                jnp.float32
            ) * dw_kernel[down, across].astype(jnp.float32)
    depth = gelu_tanh(total + dw_bias).astype(jnp.bfloat16)
    proj = jnp.dot(depth.reshape(-1, hidden_width), w_project, preferred_element_type=jnp.float32)
    mid = (latent.reshape(-1, width).astype(jnp.float32) + proj + b_project).astype(jnp.bfloat16)
    sizes = layout_sizes(tile_h, tile_w)
    plan = runs_plan(tile_h, tile_w)
    if plan is not None:
        arrived = send_runs(mid.reshape(tile_h, tile_w, width), plan)
        n_row, n_col = lax.axis_size("row"), lax.axis_size("col")
        order = np.arange(GRID * GRID).reshape(n_row, plan["parts"], n_col).transpose(1, 0, 2).reshape(-1)
        pieces = block_rows(n_row * n_col)
    else:
        arrived = send_to_owner(mid.reshape(tile_h, tile_w, width), sizes)
        a, b = sizes["n_row"] // sizes["qr"], sizes["n_col"] // sizes["qc"]
        c, d = sizes["pr"], sizes["pc"]
        assert sizes["qr"] == 1 or b * c * d == 1
        assert sizes["qc"] == 1 or c * d == 1
        assert sizes["kr"] == 1 or d == 1
        order = np.arange(GRID * GRID).reshape(a, c, b, d).transpose(0, 2, 1, 3).reshape(-1)
        pieces = strided_rows
    result = owner_block(
        arrived, ln_gain, ln_bias, w_qkv, arrived_bias(pos_bias, order), w_out, b_out, pieces
    )
    if plan is not None:
        return back_runs(result, plan, tile_h, tile_w)
    return back_home(result, sizes, tile_h, tile_w)

def solution(mesh):
    return jax.shard_map(
        on_device,
        mesh=mesh,
        in_specs=(
            P("row", "col", None),
            P(),
            P(),
            P(),
            P(),
            P(),
            P(),
            P(),
            P(),
            P(),
            P(),
            P(),
            P(),
            P(),
            P(),
        ),
        out_specs=P("row", "col", None),
        check_vma=False,
    )
```

```python
import math

import numpy as np

import jax
import jax.numpy as jnp
from jax import lax
from jax.sharding import PartitionSpec as P
from jax.experimental import pallas as pl
from jax.experimental.pallas import tpu as pltpu

HEADS = 16
GRID = 8


def extended(block, sides, width):
    for axis, dim in sides:
        count = lax.axis_size(axis)
        forward = [(i, i + 1) for i in range(count - 1)]
        backward = [(target, source) for source, target in forward]
        low = lax.ppermute(
            lax.slice_in_dim(block, block.shape[dim] - width, None, axis=dim), axis, forward
        )
        high = lax.ppermute(lax.slice_in_dim(block, 0, width, axis=dim), axis, backward)
        block = jnp.concatenate([low, block, high], axis=dim)
    return block


def gelu_tanh(v):
    return jax.nn.gelu(v, approximate=True)


def layout_sizes(tile_h, tile_w):
    n_row = lax.axis_size("row")
    n_col = lax.axis_size("col")
    stride_h = tile_h * n_row // GRID
    stride_w = tile_w * n_col // GRID
    part_h = min(tile_h, stride_h)
    part_w = min(tile_w, stride_w)
    return dict(
        n_row=n_row,
        n_col=n_col,
        pr=tile_h // part_h,
        kr=part_h // n_row,
        qr=stride_h // part_h,
        pc=tile_w // part_w,
        kc=part_w // n_col,
        qc=stride_w // part_w,
    )


def to_owner(tile, sizes):
    tile_h, tile_w, feats = tile.shape
    message = sizes["pr"] * sizes["kr"] * sizes["pc"] * sizes["kc"]
    outgoing = tile.reshape(
        sizes["pr"], sizes["n_row"], sizes["kr"], sizes["pc"], sizes["n_col"], sizes["kc"], feats
    ).transpose(1, 4, 0, 2, 3, 5, 6)
    arrived = lax.all_to_all(
        outgoing.reshape(sizes["n_row"] * sizes["n_col"], message, feats),
        ("row", "col"),
        split_axis=0,
        concat_axis=0,
        tiled=True,
    )
    arrived = arrived.reshape(
        sizes["n_row"] // sizes["qr"],
        sizes["qr"],
        sizes["n_col"] // sizes["qc"],
        sizes["qc"],
        sizes["pr"],
        sizes["kr"],
        sizes["pc"],
        sizes["kc"],
        feats,
    )
    arrived = arrived.transpose(1, 5, 3, 7, 0, 4, 2, 6, 8)
    return arrived.reshape(
        sizes["qr"] * sizes["kr"] * sizes["qc"] * sizes["kc"], GRID * GRID, feats
    )


def to_home(grouped, sizes, tile_h, tile_w):
    feats = grouped.shape[-1]
    message = sizes["pr"] * sizes["kr"] * sizes["pc"] * sizes["kc"]
    outgoing = grouped.reshape(
        sizes["qr"],
        sizes["kr"],
        sizes["qc"],
        sizes["kc"],
        sizes["n_row"] // sizes["qr"],
        sizes["pr"],
        sizes["n_col"] // sizes["qc"],
        sizes["pc"],
        feats,
    )
    outgoing = outgoing.transpose(4, 0, 6, 2, 5, 1, 7, 3, 8)
    back = lax.all_to_all(
        outgoing.reshape(sizes["n_row"] * sizes["n_col"], message, feats),
        ("row", "col"),
        split_axis=0,
        concat_axis=0,
        tiled=True,
    )
    back = back.reshape(
        sizes["n_row"], sizes["n_col"], sizes["pr"], sizes["kr"], sizes["pc"], sizes["kc"], feats
    ).transpose(2, 0, 3, 4, 1, 5, 6)
    return back.reshape(tile_h, tile_w, feats)


def attend(qkv, pos_bias):
    groups, members, three = qkv.shape
    width = three // 3
    head_dim = width // HEADS
    query = qkv[:, :, :width].reshape(groups, members, HEADS, head_dim)
    keys = qkv[:, :, width : 2 * width].reshape(groups, members, HEADS, head_dim)
    values = qkv[:, :, 2 * width :].reshape(groups, members, HEADS, head_dim)
    scores = (
        jnp.einsum("gihd,gjhd->ghij", query, keys, preferred_element_type=jnp.float32)
        * head_dim ** (-0.5)
        + pos_bias[None]
    )
    top = jnp.max(scores, axis=-1, keepdims=True)
    expo = jnp.exp(scores - top)
    probs = (expo / jnp.sum(expo, axis=-1, keepdims=True)).astype(jnp.bfloat16)
    mixed = jnp.einsum("ghij,gjhd->gihd", probs, values, preferred_element_type=jnp.float32)
    return mixed.astype(jnp.bfloat16).reshape(groups, members, width)


def owner_kernel(mid_ref, gain_ref, bias_ref, wqkv_ref, pos_ref, wout_ref, bout_ref, out_ref, qkv_ref, att_ref):
    rows_all, width = mid_ref.shape
    lanes = qkv_ref.shape[-1]
    members = pos_ref.shape[-1]
    groups = rows_all // members
    head_dim = width // HEADS
    values = mid_ref[...].astype(jnp.float32)
    mean = jnp.mean(values, axis=-1, keepdims=True)
    centred = values - mean
    var = jnp.mean(jnp.square(centred), axis=-1, keepdims=True)
    normed = (centred * lax.rsqrt(var + 1e-05) * gain_ref[...] + bias_ref[...]).astype(jnp.bfloat16)
    qkv = jnp.dot(normed, wqkv_ref[...], preferred_element_type=jnp.float32)
    qkv = qkv.astype(jnp.bfloat16).astype(jnp.float32)
    for t in range(qkv_ref.shape[0]):
        qkv_ref[t] = qkv[:, t * lanes : (t + 1) * lanes]
    tiles = width // lanes
    per_tile = lanes // head_dim
    head_of = lax.broadcasted_iota(jnp.int32, (1, lanes), 1) // head_dim
    for g in range(groups):
        rows = pl.ds(g, members, stride=groups)
        for k in range(tiles):
            query = qkv_ref[k, rows, :].astype(jnp.bfloat16)
            keys = qkv_ref[tiles + k, rows, :].astype(jnp.bfloat16)
            vals = qkv_ref[2 * tiles + k, rows, :].astype(jnp.bfloat16)
            masked = jnp.concatenate(
                [jnp.where(head_of == t, query, jnp.zeros_like(query)) for t in range(per_tile)], axis=0
            )
            scores = lax.dot_general(
                masked, keys, (((1,), (1,)), ((), ())), preferred_element_type=jnp.float32
            ) * head_dim ** (-0.5) + pos_ref[k]
            top = jnp.max(scores, axis=-1, keepdims=True)
            expo = jnp.exp(scores - top)
            probs = (expo / jnp.sum(expo, axis=-1, keepdims=True)).astype(jnp.bfloat16)
            mixed = jnp.dot(probs, vals, preferred_element_type=jnp.float32)
            picked = jnp.where(head_of == 0, mixed[:members], 0.0)
            for t in range(1, per_tile):
                picked = picked + jnp.where(head_of == t, mixed[t * members : (t + 1) * members], 0.0)
            att_ref[k, rows, :] = picked.astype(jnp.bfloat16).astype(jnp.float32)
    attended = jnp.concatenate([att_ref[k] for k in range(tiles)], axis=1).astype(jnp.bfloat16)
    result = values + jnp.dot(attended, wout_ref[...], preferred_element_type=jnp.float32) + bout_ref[...]
    out_ref[...] = result.astype(jnp.bfloat16)


def owner_block(arrived, ln_gain, ln_bias, w_qkv, pos_bias, w_out, b_out):
    rows_all, width = arrived.shape
    members = pos_bias.shape[-1]
    lanes = 128
    whole = lambda shape: pl.BlockSpec(shape, lambda: (0,) * len(shape))
    return pl.pallas_call(
        owner_kernel,
        out_shape=jax.ShapeDtypeStruct(arrived.shape, jnp.bfloat16),
        in_specs=[
            whole(arrived.shape),
            whole((1, width)),
            whole((1, width)),
            whole(w_qkv.shape),
            whole((width // lanes, lanes // (width // HEADS) * members, members)),
            whole(w_out.shape),
            whole((1, width)),
        ],
        out_specs=whole(arrived.shape),
        scratch_shapes=[
            pltpu.VMEM((3 * width // lanes, rows_all, lanes), jnp.float32),
            pltpu.VMEM((width // lanes, rows_all, lanes), jnp.float32),
        ],
    )(
        arrived,
        ln_gain.reshape(1, width),
        ln_bias.reshape(1, width),
        w_qkv,
        pos_bias.reshape(width // lanes, -1, members),
        w_out,
        b_out.reshape(1, width),
    )


def send_to_owner(tile, sizes):
    tile_h, tile_w, feats = tile.shape
    outgoing = tile.reshape(
        sizes["pr"], sizes["n_row"], sizes["kr"], sizes["pc"], sizes["n_col"], sizes["kc"], feats
    ).transpose(1, 4, 0, 2, 3, 5, 6)
    arrived = lax.all_to_all(
        outgoing.reshape(sizes["n_row"] * sizes["n_col"], -1, feats),
        ("row", "col"),
        split_axis=0,
        concat_axis=0,
        tiled=True,
    )
    return arrived.reshape(-1, feats)


def back_home(rows, sizes, tile_h, tile_w):
    feats = rows.shape[-1]
    back = lax.all_to_all(
        rows.reshape(sizes["n_row"] * sizes["n_col"], -1, feats),
        ("row", "col"),
        split_axis=0,
        concat_axis=0,
        tiled=True,
    )
    back = back.reshape(
        sizes["n_row"], sizes["n_col"], sizes["pr"], sizes["kr"], sizes["pc"], sizes["kc"], feats
    ).transpose(2, 0, 3, 4, 1, 5, 6)
    return back.reshape(tile_h, tile_w, feats)


def runs_plan(tile_h, tile_w):
    n_row = lax.axis_size("row")
    n_col = lax.axis_size("col")
    stride_h = tile_h * n_row // GRID
    stride_w = tile_w * n_col // GRID
    n_dev = n_row * n_col
    per_owner = stride_h * stride_w // n_dev
    if tile_w != stride_w or tile_h % stride_h or stride_w % per_owner or per_owner % 16:
        return None
    return dict(parts=tile_h // stride_h, stride_h=stride_h, blocks=stride_w // per_owner, run=per_owner)


def send_runs(tile, plan):
    feats = tile.shape[-1]
    outgoing = tile.reshape(
        plan["parts"], plan["stride_h"], plan["blocks"], plan["run"], feats
    ).transpose(1, 2, 0, 3, 4)
    arrived = lax.all_to_all(
        outgoing.reshape(plan["stride_h"] * plan["blocks"], -1, feats),
        ("row", "col"),
        split_axis=0,
        concat_axis=0,
        tiled=True,
    )
    return arrived.reshape(-1, feats)


def back_runs(rows, plan, tile_h, tile_w):
    feats = rows.shape[-1]
    back = lax.all_to_all(
        rows.reshape(plan["stride_h"] * plan["blocks"], -1, feats),
        ("row", "col"),
        split_axis=0,
        concat_axis=0,
        tiled=True,
    )
    back = back.reshape(
        plan["stride_h"], plan["blocks"], plan["parts"], plan["run"], feats
    ).transpose(2, 0, 1, 3, 4)
    return back.reshape(tile_h, tile_w, feats)


def arrived_bias(pos_bias, a, b, c, d):
    heads, members, _ = pos_bias.shape
    order = np.arange(members).reshape(a, c, b, d).transpose(0, 2, 1, 3).reshape(-1)
    pick = jnp.asarray(np.eye(members, dtype=np.float32)[order])
    picked = jnp.einsum("hij,bj->hib", pos_bias, pick, precision=lax.Precision.HIGHEST)
    return jnp.einsum("ai,hib->hab", pick, picked, precision=lax.Precision.HIGHEST)

def on_device(
    latent,
    bn_scale,
    bn_shift,
    w_expand,
    b_expand,
    dw_kernel,
    dw_bias,
    w_project,
    b_project,
    ln_gain,
    ln_bias,
    w_qkv,
    pos_bias,
    w_out,
    b_out,
):
    tile_h, tile_w, width = latent.shape
    hidden_width = w_expand.shape[1]
    rows_here = latent.shape[0]
    cols_here = latent.shape[1]
    wide_in = extended(latent, (("row", 0), ("col", 1)), 1)
    row_at = lax.axis_index("row") * rows_here - 1 + jnp.arange(rows_here + 2)
    col_at = lax.axis_index("col") * cols_here - 1 + jnp.arange(cols_here + 2)
    inside = ((row_at >= 0) & (row_at < lax.axis_size("row") * rows_here))[:, None] & (
        (col_at >= 0) & (col_at < lax.axis_size("col") * cols_here)
    )[None, :]

    def expand(pixels, keep):
        normed_in = (pixels.astype(jnp.float32) * bn_scale + bn_shift).astype(jnp.bfloat16)
        hidden = (
            jnp.einsum("yxc,cd->yxd", normed_in, w_expand, preferred_element_type=jnp.float32)
            + b_expand
        )
        hidden = gelu_tanh(hidden).astype(jnp.bfloat16)
        return jnp.where(keep[:, :, None], hidden, jnp.zeros_like(hidden))

    middle = expand(wide_in[:, 1:-1], inside[:, 1:-1])
    edges = expand(
        jnp.concatenate([wide_in[:, :1], wide_in[:, -1:]], axis=1),
        jnp.concatenate([inside[:, :1], inside[:, -1:]], axis=1),
    )
    padded = jnp.concatenate([edges[:, :1], middle, edges[:, 1:]], axis=1)
    total = jnp.zeros((tile_h, tile_w, hidden_width), jnp.float32)
    for down in range(3):
        for across in range(3):
            total = total + padded[down : down + tile_h, across : across + tile_w].astype(
                jnp.float32
            ) * dw_kernel[down, across].astype(jnp.float32)
    depth = gelu_tanh(total + dw_bias).astype(jnp.bfloat16)
    proj = jnp.dot(depth.reshape(-1, hidden_width), w_project, preferred_element_type=jnp.float32)
    mid = (latent.reshape(-1, width).astype(jnp.float32) + proj + b_project).astype(jnp.bfloat16)
    sizes = layout_sizes(tile_h, tile_w)
    plan = runs_plan(tile_h, tile_w)
    if plan is not None:
        arrived = send_runs(mid.reshape(tile_h, tile_w, width), plan)
        order = (lax.axis_size("row"), lax.axis_size("col"), plan["parts"], 1)
    else:
        arrived = send_to_owner(mid.reshape(tile_h, tile_w, width), sizes)
        order = (
            sizes["n_row"] // sizes["qr"], sizes["n_col"] // sizes["qc"], sizes["pr"], sizes["pc"]
        )
        assert sizes["qr"] == 1 or order[1] * order[2] * order[3] == 1
        assert sizes["qc"] == 1 or order[2] * order[3] == 1
        assert sizes["kr"] == 1 or order[3] == 1
    result = owner_block(arrived, ln_gain, ln_bias, w_qkv, arrived_bias(pos_bias, *order), w_out, b_out)
    if plan is not None:
        return back_runs(result, plan, tile_h, tile_w)
    return back_home(result, sizes, tile_h, tile_w)

def solution(mesh):
    return jax.shard_map(
        on_device,
        mesh=mesh,
        in_specs=(
            P("row", "col", None),
            P(),
            P(),
            P(),
            P(),
            P(),
            P(),
            P(),
            P(),
            P(),
            P(),
            P(),
            P(),
            P(),
            P(),
        ),
        out_specs=P("row", "col", None),
        check_vma=False,
    )
```

```python
import math

import numpy as np

import jax
import jax.numpy as jnp
from jax import lax
from jax.sharding import PartitionSpec as P
from jax.experimental import pallas as pl
from jax.experimental.pallas import tpu as pltpu

HEADS = 16
GRID = 8


def extended(block, sides, width):
    for axis, dim in sides:
        count = lax.axis_size(axis)
        forward = [(i, i + 1) for i in range(count - 1)]
        backward = [(target, source) for source, target in forward]
        low = lax.ppermute(
            lax.slice_in_dim(block, block.shape[dim] - width, None, axis=dim), axis, forward
        )
        high = lax.ppermute(lax.slice_in_dim(block, 0, width, axis=dim), axis, backward)
        block = jnp.concatenate([low, block, high], axis=dim)
    return block


def gelu_tanh(v):
    return jax.nn.gelu(v, approximate=True)


def layout_sizes(tile_h, tile_w):
    n_row = lax.axis_size("row")
    n_col = lax.axis_size("col")
    stride_h = tile_h * n_row // GRID
    stride_w = tile_w * n_col // GRID
    part_h = min(tile_h, stride_h)
    part_w = min(tile_w, stride_w)
    return dict(
        n_row=n_row,
        n_col=n_col,
        pr=tile_h // part_h,
        kr=part_h // n_row,
        qr=stride_h // part_h,
        pc=tile_w // part_w,
        kc=part_w // n_col,
        qc=stride_w // part_w,
    )


def to_owner(tile, sizes):
    tile_h, tile_w, feats = tile.shape
    message = sizes["pr"] * sizes["kr"] * sizes["pc"] * sizes["kc"]
    outgoing = tile.reshape(
        sizes["pr"], sizes["n_row"], sizes["kr"], sizes["pc"], sizes["n_col"], sizes["kc"], feats
    ).transpose(1, 4, 0, 2, 3, 5, 6)
    arrived = lax.all_to_all(
        outgoing.reshape(sizes["n_row"] * sizes["n_col"], message, feats),
        ("row", "col"),
        split_axis=0,
        concat_axis=0,
        tiled=True,
    )
    arrived = arrived.reshape(
        sizes["n_row"] // sizes["qr"],
        sizes["qr"],
        sizes["n_col"] // sizes["qc"],
        sizes["qc"],
        sizes["pr"],
        sizes["kr"],
        sizes["pc"],
        sizes["kc"],
        feats,
    )
    arrived = arrived.transpose(1, 5, 3, 7, 0, 4, 2, 6, 8)
    return arrived.reshape(
        sizes["qr"] * sizes["kr"] * sizes["qc"] * sizes["kc"], GRID * GRID, feats
    )


def to_home(grouped, sizes, tile_h, tile_w):
    feats = grouped.shape[-1]
    message = sizes["pr"] * sizes["kr"] * sizes["pc"] * sizes["kc"]
    outgoing = grouped.reshape(
        sizes["qr"],
        sizes["kr"],
        sizes["qc"],
        sizes["kc"],
        sizes["n_row"] // sizes["qr"],
        sizes["pr"],
        sizes["n_col"] // sizes["qc"],
        sizes["pc"],
        feats,
    )
    outgoing = outgoing.transpose(4, 0, 6, 2, 5, 1, 7, 3, 8)
    back = lax.all_to_all(
        outgoing.reshape(sizes["n_row"] * sizes["n_col"], message, feats),
        ("row", "col"),
        split_axis=0,
        concat_axis=0,
        tiled=True,
    )
    back = back.reshape(
        sizes["n_row"], sizes["n_col"], sizes["pr"], sizes["kr"], sizes["pc"], sizes["kc"], feats
    ).transpose(2, 0, 3, 4, 1, 5, 6)
    return back.reshape(tile_h, tile_w, feats)


def attend(qkv, pos_bias):
    groups, members, three = qkv.shape
    width = three // 3
    head_dim = width // HEADS
    query = qkv[:, :, :width].reshape(groups, members, HEADS, head_dim)
    keys = qkv[:, :, width : 2 * width].reshape(groups, members, HEADS, head_dim)
    values = qkv[:, :, 2 * width :].reshape(groups, members, HEADS, head_dim)
    scores = (
        jnp.einsum("gihd,gjhd->ghij", query, keys, preferred_element_type=jnp.float32)
        * head_dim ** (-0.5)
        + pos_bias[None]
    )
    top = jnp.max(scores, axis=-1, keepdims=True)
    expo = jnp.exp(scores - top)
    probs = (expo / jnp.sum(expo, axis=-1, keepdims=True)).astype(jnp.bfloat16)
    mixed = jnp.einsum("ghij,gjhd->gihd", probs, values, preferred_element_type=jnp.float32)
    return mixed.astype(jnp.bfloat16).reshape(groups, members, width)


def owner_kernel(mid_ref, gain_ref, bias_ref, wqkv_ref, pos_ref, wout_ref, bout_ref, out_ref, qkv_ref, att_ref):
    rows_all, width = mid_ref.shape
    lanes = qkv_ref.shape[-1]
    members = pos_ref.shape[-1]
    groups = rows_all // members
    head_dim = width // HEADS
    values = mid_ref[...].astype(jnp.float32)
    mean = jnp.mean(values, axis=-1, keepdims=True)
    centred = values - mean
    var = jnp.mean(jnp.square(centred), axis=-1, keepdims=True)
    normed = (centred * lax.rsqrt(var + 1e-05) * gain_ref[...] + bias_ref[...]).astype(jnp.bfloat16)
    qkv = jnp.dot(normed, wqkv_ref[...], preferred_element_type=jnp.float32)
    qkv = qkv.astype(jnp.bfloat16).astype(jnp.float32)
    for t in range(qkv_ref.shape[0]):
        qkv_ref[t] = qkv[:, t * lanes : (t + 1) * lanes]
    tiles = width // lanes
    per_tile = lanes // head_dim
    head_of = lax.broadcasted_iota(jnp.int32, (1, lanes), 1) // head_dim
    for g in range(groups):
        rows = pl.ds(g, members, stride=groups)
        for k in range(tiles):
            query = qkv_ref[k, rows, :].astype(jnp.bfloat16)
            keys = qkv_ref[tiles + k, rows, :].astype(jnp.bfloat16)
            vals = qkv_ref[2 * tiles + k, rows, :].astype(jnp.bfloat16)
            masked = jnp.concatenate(
                [jnp.where(head_of == t, query, jnp.zeros_like(query)) for t in range(per_tile)], axis=0
            )
            scores = lax.dot_general(
                masked, keys, (((1,), (1,)), ((), ())), preferred_element_type=jnp.float32
            ) * head_dim ** (-0.5) + pos_ref[k]
            top = jnp.max(scores, axis=-1, keepdims=True)
            expo = jnp.exp(scores - top)
            probs = (expo / jnp.sum(expo, axis=-1, keepdims=True)).astype(jnp.bfloat16)
            mixed = jnp.dot(probs, vals, preferred_element_type=jnp.float32)
            picked = jnp.where(head_of == 0, mixed[:members], 0.0)
            for t in range(1, per_tile):
                picked = picked + jnp.where(head_of == t, mixed[t * members : (t + 1) * members], 0.0)
            att_ref[k, rows, :] = picked.astype(jnp.bfloat16).astype(jnp.float32)
    attended = jnp.concatenate([att_ref[k] for k in range(tiles)], axis=1).astype(jnp.bfloat16)
    result = values + jnp.dot(attended, wout_ref[...], preferred_element_type=jnp.float32) + bout_ref[...]
    out_ref[...] = result.astype(jnp.bfloat16)


def owner_block(arrived, ln_gain, ln_bias, w_qkv, pos_bias, w_out, b_out):
    rows_all, width = arrived.shape
    members = pos_bias.shape[-1]
    lanes = 128
    whole = lambda shape: pl.BlockSpec(shape, lambda: (0,) * len(shape))
    return pl.pallas_call(
        owner_kernel,
        out_shape=jax.ShapeDtypeStruct(arrived.shape, jnp.bfloat16),
        in_specs=[
            whole(arrived.shape),
            whole((1, width)),
            whole((1, width)),
            whole(w_qkv.shape),
            whole((width // lanes, lanes // (width // HEADS) * members, members)),
            whole(w_out.shape),
            whole((1, width)),
        ],
        out_specs=whole(arrived.shape),
        scratch_shapes=[
            pltpu.VMEM((3 * width // lanes, rows_all, lanes), jnp.float32),
            pltpu.VMEM((width // lanes, rows_all, lanes), jnp.float32),
        ],
    )(
        arrived,
        ln_gain.reshape(1, width),
        ln_bias.reshape(1, width),
        w_qkv,
        pos_bias.reshape(width // lanes, -1, members),
        w_out,
        b_out.reshape(1, width),
    )


def send_to_owner(tile, sizes):
    tile_h, tile_w, feats = tile.shape
    outgoing = tile.reshape(
        sizes["pr"], sizes["n_row"], sizes["kr"], sizes["pc"], sizes["n_col"], sizes["kc"], feats
    ).transpose(1, 4, 0, 2, 3, 5, 6)
    arrived = lax.all_to_all(
        outgoing.reshape(sizes["n_row"] * sizes["n_col"], -1, feats),
        ("row", "col"),
        split_axis=0,
        concat_axis=0,
        tiled=True,
    )
    return arrived.reshape(-1, feats)


def back_home(rows, sizes, tile_h, tile_w):
    feats = rows.shape[-1]
    back = lax.all_to_all(
        rows.reshape(sizes["n_row"] * sizes["n_col"], -1, feats),
        ("row", "col"),
        split_axis=0,
        concat_axis=0,
        tiled=True,
    )
    back = back.reshape(
        sizes["n_row"], sizes["n_col"], sizes["pr"], sizes["kr"], sizes["pc"], sizes["kc"], feats
    ).transpose(2, 0, 3, 4, 1, 5, 6)
    return back.reshape(tile_h, tile_w, feats)


def runs_plan(tile_h, tile_w):
    n_row = lax.axis_size("row")
    n_col = lax.axis_size("col")
    stride_h = tile_h * n_row // GRID
    stride_w = tile_w * n_col // GRID
    n_dev = n_row * n_col
    per_owner = stride_h * stride_w // n_dev
    if tile_w != stride_w or tile_h % stride_h or stride_w % per_owner or per_owner % 16:
        return None
    return dict(parts=tile_h // stride_h, stride_h=stride_h, blocks=stride_w // per_owner, run=per_owner)


def send_runs(tile, plan):
    feats = tile.shape[-1]
    outgoing = tile.reshape(
        plan["parts"], plan["stride_h"], plan["blocks"], plan["run"], feats
    ).transpose(1, 2, 0, 3, 4)
    arrived = lax.all_to_all(
        outgoing.reshape(plan["stride_h"] * plan["blocks"], -1, feats),
        ("row", "col"),
        split_axis=0,
        concat_axis=0,
        tiled=True,
    )
    return arrived.reshape(-1, feats)


def back_runs(rows, plan, tile_h, tile_w):
    feats = rows.shape[-1]
    back = lax.all_to_all(
        rows.reshape(plan["stride_h"] * plan["blocks"], -1, feats),
        ("row", "col"),
        split_axis=0,
        concat_axis=0,
        tiled=True,
    )
    back = back.reshape(
        plan["stride_h"], plan["blocks"], plan["parts"], plan["run"], feats
    ).transpose(2, 0, 1, 3, 4)
    return back.reshape(tile_h, tile_w, feats)


def arrived_bias(pos_bias, a, b, c, d):
    heads, members, _ = pos_bias.shape
    order = np.arange(members).reshape(a, c, b, d).transpose(0, 2, 1, 3).reshape(-1)
    pick = jnp.asarray(np.eye(members, dtype=np.float32)[order])
    picked = jnp.einsum("hij,bj->hib", pos_bias, pick, precision=lax.Precision.HIGHEST)
    return jnp.einsum("ai,hib->hab", pick, picked, precision=lax.Precision.HIGHEST)

def on_device(
    latent,
    bn_scale,
    bn_shift,
    w_expand,
    b_expand,
    dw_kernel,
    dw_bias,
    w_project,
    b_project,
    ln_gain,
    ln_bias,
    w_qkv,
    pos_bias,
    w_out,
    b_out,
):
    tile_h, tile_w, width = latent.shape
    hidden_width = w_expand.shape[1]
    rows_here = latent.shape[0]
    cols_here = latent.shape[1]
    wide_in = extended(latent, (("row", 0), ("col", 1)), 1)
    row_at = lax.axis_index("row") * rows_here - 1 + jnp.arange(rows_here + 2)
    col_at = lax.axis_index("col") * cols_here - 1 + jnp.arange(cols_here + 2)
    inside = ((row_at >= 0) & (row_at < lax.axis_size("row") * rows_here))[:, None] & (
        (col_at >= 0) & (col_at < lax.axis_size("col") * cols_here)
    )[None, :]

    def expand(pixels, keep):
        normed_in = (pixels.astype(jnp.float32) * bn_scale + bn_shift).astype(jnp.bfloat16)
        hidden = (
            jnp.einsum("yxc,cd->yxd", normed_in, w_expand, preferred_element_type=jnp.float32)
            + b_expand
        )
        hidden = gelu_tanh(hidden).astype(jnp.bfloat16)
        return jnp.where(keep[:, :, None], hidden, jnp.zeros_like(hidden))

    middle = expand(wide_in[:, 1:-1], inside[:, 1:-1])
    edges = expand(
        jnp.concatenate([wide_in[:, :1], wide_in[:, -1:]], axis=1),
        jnp.concatenate([inside[:, :1], inside[:, -1:]], axis=1),
    )
    padded = lax.optimization_barrier(jnp.concatenate([edges[:, :1], middle, edges[:, 1:]], axis=1))
    total = jnp.zeros((tile_h, tile_w, hidden_width), jnp.float32)
    for down in range(3):
        for across in range(3):
            total = total + padded[down : down + tile_h, across : across + tile_w].astype(
                jnp.float32
            ) * dw_kernel[down, across].astype(jnp.float32)
    depth = gelu_tanh(total + dw_bias).astype(jnp.bfloat16)
    proj = jnp.dot(depth.reshape(-1, hidden_width), w_project, preferred_element_type=jnp.float32)
    mid = (latent.reshape(-1, width).astype(jnp.float32) + proj + b_project).astype(jnp.bfloat16)
    sizes = layout_sizes(tile_h, tile_w)
    plan = runs_plan(tile_h, tile_w)
    if plan is not None:
        arrived = send_runs(mid.reshape(tile_h, tile_w, width), plan)
        order = (lax.axis_size("row"), lax.axis_size("col"), plan["parts"], 1)
    else:
        arrived = send_to_owner(mid.reshape(tile_h, tile_w, width), sizes)
        order = (
            sizes["n_row"] // sizes["qr"], sizes["n_col"] // sizes["qc"], sizes["pr"], sizes["pc"]
        )
        assert sizes["qr"] == 1 or order[1] * order[2] * order[3] == 1
        assert sizes["qc"] == 1 or order[2] * order[3] == 1
        assert sizes["kr"] == 1 or order[3] == 1
    result = owner_block(arrived, ln_gain, ln_bias, w_qkv, arrived_bias(pos_bias, *order), w_out, b_out)
    if plan is not None:
        return back_runs(result, plan, tile_h, tile_w)
    return back_home(result, sizes, tile_h, tile_w)

def solution(mesh):
    return jax.shard_map(
        on_device,
        mesh=mesh,
        in_specs=(
            P("row", "col", None),
            P(),
            P(),
            P(),
            P(),
            P(),
            P(),
            P(),
            P(),
            P(),
            P(),
            P(),
            P(),
            P(),
            P(),
        ),
        out_specs=P("row", "col", None),
        check_vma=False,
    )
```

```python
import math

import numpy as np

import jax
import jax.numpy as jnp
from jax import lax
from jax.sharding import PartitionSpec as P
from jax.experimental import pallas as pl
from jax.experimental.pallas import tpu as pltpu

HEADS = 16
GRID = 8


def extended(block, sides, width):
    for axis, dim in sides:
        count = lax.axis_size(axis)
        forward = [(i, i + 1) for i in range(count - 1)]
        backward = [(target, source) for source, target in forward]
        low = lax.ppermute(
            lax.slice_in_dim(block, block.shape[dim] - width, None, axis=dim), axis, forward
        )
        high = lax.ppermute(lax.slice_in_dim(block, 0, width, axis=dim), axis, backward)
        block = jnp.concatenate([low, block, high], axis=dim)
    return block


def gelu_tanh(v):
    return jax.nn.gelu(v, approximate=True)


def layout_sizes(tile_h, tile_w):
    n_row = lax.axis_size("row")
    n_col = lax.axis_size("col")
    stride_h = tile_h * n_row // GRID
    stride_w = tile_w * n_col // GRID
    part_h = min(tile_h, stride_h)
    part_w = min(tile_w, stride_w)
    return dict(
        n_row=n_row,
        n_col=n_col,
        pr=tile_h // part_h,
        kr=part_h // n_row,
        qr=stride_h // part_h,
        pc=tile_w // part_w,
        kc=part_w // n_col,
        qc=stride_w // part_w,
    )


def to_owner(tile, sizes):
    tile_h, tile_w, feats = tile.shape
    message = sizes["pr"] * sizes["kr"] * sizes["pc"] * sizes["kc"]
    outgoing = tile.reshape(
        sizes["pr"], sizes["n_row"], sizes["kr"], sizes["pc"], sizes["n_col"], sizes["kc"], feats
    ).transpose(1, 4, 0, 2, 3, 5, 6)
    arrived = lax.all_to_all(
        outgoing.reshape(sizes["n_row"] * sizes["n_col"], message, feats),
        ("row", "col"),
        split_axis=0,
        concat_axis=0,
        tiled=True,
    )
    arrived = arrived.reshape(
        sizes["n_row"] // sizes["qr"],
        sizes["qr"],
        sizes["n_col"] // sizes["qc"],
        sizes["qc"],
        sizes["pr"],
        sizes["kr"],
        sizes["pc"],
        sizes["kc"],
        feats,
    )
    arrived = arrived.transpose(1, 5, 3, 7, 0, 4, 2, 6, 8)
    return arrived.reshape(
        sizes["qr"] * sizes["kr"] * sizes["qc"] * sizes["kc"], GRID * GRID, feats
    )


def to_home(grouped, sizes, tile_h, tile_w):
    feats = grouped.shape[-1]
    message = sizes["pr"] * sizes["kr"] * sizes["pc"] * sizes["kc"]
    outgoing = grouped.reshape(
        sizes["qr"],
        sizes["kr"],
        sizes["qc"],
        sizes["kc"],
        sizes["n_row"] // sizes["qr"],
        sizes["pr"],
        sizes["n_col"] // sizes["qc"],
        sizes["pc"],
        feats,
    )
    outgoing = outgoing.transpose(4, 0, 6, 2, 5, 1, 7, 3, 8)
    back = lax.all_to_all(
        outgoing.reshape(sizes["n_row"] * sizes["n_col"], message, feats),
        ("row", "col"),
        split_axis=0,
        concat_axis=0,
        tiled=True,
    )
    back = back.reshape(
        sizes["n_row"], sizes["n_col"], sizes["pr"], sizes["kr"], sizes["pc"], sizes["kc"], feats
    ).transpose(2, 0, 3, 4, 1, 5, 6)
    return back.reshape(tile_h, tile_w, feats)


def attend(qkv, pos_bias):
    groups, members, three = qkv.shape
    width = three // 3
    head_dim = width // HEADS
    query = qkv[:, :, :width].reshape(groups, members, HEADS, head_dim)
    keys = qkv[:, :, width : 2 * width].reshape(groups, members, HEADS, head_dim)
    values = qkv[:, :, 2 * width :].reshape(groups, members, HEADS, head_dim)
    scores = (
        jnp.einsum("gihd,gjhd->ghij", query, keys, preferred_element_type=jnp.float32)
        * head_dim ** (-0.5)
        + pos_bias[None]
    )
    top = jnp.max(scores, axis=-1, keepdims=True)
    expo = jnp.exp(scores - top)
    probs = (expo / jnp.sum(expo, axis=-1, keepdims=True)).astype(jnp.bfloat16)
    mixed = jnp.einsum("ghij,gjhd->gihd", probs, values, preferred_element_type=jnp.float32)
    return mixed.astype(jnp.bfloat16).reshape(groups, members, width)


def owner_kernel(mid_ref, gain_ref, bias_ref, wqkv_ref, pos_ref, wout_ref, bout_ref, out_ref, qkv_ref, att_ref):
    rows_all, width = mid_ref.shape
    lanes = qkv_ref.shape[-1]
    members = pos_ref.shape[-1]
    groups = rows_all // members
    head_dim = width // HEADS
    values = mid_ref[...].astype(jnp.float32)
    mean = jnp.mean(values, axis=-1, keepdims=True)
    centred = values - mean
    var = jnp.mean(jnp.square(centred), axis=-1, keepdims=True)
    normed = (centred * lax.rsqrt(var + 1e-05) * gain_ref[...] + bias_ref[...]).astype(jnp.bfloat16)
    qkv = jnp.dot(normed, wqkv_ref[...], preferred_element_type=jnp.float32)
    qkv = qkv.astype(jnp.bfloat16).astype(jnp.float32)
    for t in range(qkv_ref.shape[0]):
        qkv_ref[t] = qkv[:, t * lanes : (t + 1) * lanes]
    tiles = width // lanes
    per_tile = lanes // head_dim
    head_of = lax.broadcasted_iota(jnp.int32, (1, lanes), 1) // head_dim
    for g in range(groups):
        rows = pl.ds(g, members, stride=groups)
        for k in range(tiles):
            query = qkv_ref[k, rows, :].astype(jnp.bfloat16)
            keys = qkv_ref[tiles + k, rows, :].astype(jnp.bfloat16)
            vals = qkv_ref[2 * tiles + k, rows, :].astype(jnp.bfloat16)
            masked = jnp.concatenate(
                [jnp.where(head_of == t, query, jnp.zeros_like(query)) for t in range(per_tile)], axis=0
            )
            scores = lax.dot_general(
                masked, keys, (((1,), (1,)), ((), ())), preferred_element_type=jnp.float32
            ) * head_dim ** (-0.5) + pos_ref[k]
            top = jnp.max(scores, axis=-1, keepdims=True)
            expo = jnp.exp(scores - top)
            probs = (expo / jnp.sum(expo, axis=-1, keepdims=True)).astype(jnp.bfloat16)
            mixed = jnp.dot(probs, vals, preferred_element_type=jnp.float32)
            picked = jnp.where(head_of == 0, mixed[:members], 0.0)
            for t in range(1, per_tile):
                picked = picked + jnp.where(head_of == t, mixed[t * members : (t + 1) * members], 0.0)
            att_ref[k, rows, :] = picked.astype(jnp.bfloat16).astype(jnp.float32)
    attended = jnp.concatenate([att_ref[k] for k in range(tiles)], axis=1).astype(jnp.bfloat16)
    result = values + jnp.dot(attended, wout_ref[...], preferred_element_type=jnp.float32) + bout_ref[...]
    out_ref[...] = result.astype(jnp.bfloat16)


def owner_block(arrived, ln_gain, ln_bias, w_qkv, pos_bias, w_out, b_out):
    rows_all, width = arrived.shape
    members = pos_bias.shape[-1]
    lanes = 128
    whole = lambda shape: pl.BlockSpec(shape, lambda: (0,) * len(shape))
    return pl.pallas_call(
        owner_kernel,
        out_shape=jax.ShapeDtypeStruct(arrived.shape, jnp.bfloat16),
        in_specs=[
            whole(arrived.shape),
            whole((1, width)),
            whole((1, width)),
            whole(w_qkv.shape),
            whole((width // lanes, lanes // (width // HEADS) * members, members)),
            whole(w_out.shape),
            whole((1, width)),
        ],
        out_specs=whole(arrived.shape),
        scratch_shapes=[
            pltpu.VMEM((3 * width // lanes, rows_all, lanes), jnp.float32),
            pltpu.VMEM((width // lanes, rows_all, lanes), jnp.float32),
        ],
    )(
        arrived,
        ln_gain.reshape(1, width),
        ln_bias.reshape(1, width),
        w_qkv,
        pos_bias.reshape(width // lanes, -1, members),
        w_out,
        b_out.reshape(1, width),
    )


def send_to_owner(tile, sizes):
    tile_h, tile_w, feats = tile.shape
    outgoing = tile.reshape(
        sizes["pr"], sizes["n_row"], sizes["kr"], sizes["pc"], sizes["n_col"], sizes["kc"], feats
    ).transpose(1, 4, 0, 2, 3, 5, 6)
    arrived = lax.all_to_all(
        outgoing.reshape(sizes["n_row"] * sizes["n_col"], -1, feats),
        ("row", "col"),
        split_axis=0,
        concat_axis=0,
        tiled=True,
    )
    return arrived.reshape(-1, feats)


def back_home(rows, sizes, tile_h, tile_w):
    feats = rows.shape[-1]
    back = lax.all_to_all(
        rows.reshape(sizes["n_row"] * sizes["n_col"], -1, feats),
        ("row", "col"),
        split_axis=0,
        concat_axis=0,
        tiled=True,
    )
    back = back.reshape(
        sizes["n_row"], sizes["n_col"], sizes["pr"], sizes["kr"], sizes["pc"], sizes["kc"], feats
    ).transpose(2, 0, 3, 4, 1, 5, 6)
    return back.reshape(tile_h, tile_w, feats)


def runs_plan(tile_h, tile_w):
    n_row = lax.axis_size("row")
    n_col = lax.axis_size("col")
    stride_h = tile_h * n_row // GRID
    stride_w = tile_w * n_col // GRID
    n_dev = n_row * n_col
    per_owner = stride_h * stride_w // n_dev
    if tile_w != stride_w or tile_h % stride_h or stride_w % per_owner or per_owner % 16:
        return None
    return dict(parts=tile_h // stride_h, stride_h=stride_h, blocks=stride_w // per_owner, run=per_owner)


def send_runs(tile, plan):
    feats = tile.shape[-1]
    outgoing = tile.reshape(
        plan["parts"], plan["stride_h"], plan["blocks"], plan["run"], feats
    ).transpose(1, 2, 0, 3, 4)
    arrived = lax.all_to_all(
        outgoing.reshape(plan["stride_h"] * plan["blocks"], -1, feats),
        ("row", "col"),
        split_axis=0,
        concat_axis=0,
        tiled=True,
    )
    return arrived.reshape(-1, feats)


def back_runs(rows, plan, tile_h, tile_w):
    feats = rows.shape[-1]
    back = lax.all_to_all(
        rows.reshape(plan["stride_h"] * plan["blocks"], -1, feats),
        ("row", "col"),
        split_axis=0,
        concat_axis=0,
        tiled=True,
    )
    back = back.reshape(
        plan["stride_h"], plan["blocks"], plan["parts"], plan["run"], feats
    ).transpose(2, 0, 1, 3, 4)
    return back.reshape(tile_h, tile_w, feats)


def arrived_bias(pos_bias, a, b, c, d):
    heads, members, _ = pos_bias.shape
    order = np.arange(members).reshape(a, c, b, d).transpose(0, 2, 1, 3).reshape(-1)
    pick = jnp.asarray(np.eye(members, dtype=np.float32)[order])
    picked = jnp.einsum("hij,bj->hib", pos_bias, pick, precision=lax.Precision.HIGHEST)
    return jnp.einsum("ai,hib->hab", pick, picked, precision=lax.Precision.HIGHEST)

def on_device(
    latent,
    bn_scale,
    bn_shift,
    w_expand,
    b_expand,
    dw_kernel,
    dw_bias,
    w_project,
    b_project,
    ln_gain,
    ln_bias,
    w_qkv,
    pos_bias,
    w_out,
    b_out,
):
    tile_h, tile_w, width = latent.shape
    hidden_width = w_expand.shape[1]
    rows_here = latent.shape[0]
    cols_here = latent.shape[1]
    wide_in = extended(latent, (("row", 0), ("col", 1)), 1)
    row_at = lax.axis_index("row") * rows_here - 1 + jnp.arange(rows_here + 2)
    col_at = lax.axis_index("col") * cols_here - 1 + jnp.arange(cols_here + 2)
    inside = ((row_at >= 0) & (row_at < lax.axis_size("row") * rows_here))[:, None] & (
        (col_at >= 0) & (col_at < lax.axis_size("col") * cols_here)
    )[None, :]

    def expand(pixels, keep):
        normed_in = (pixels.astype(jnp.float32) * bn_scale + bn_shift).astype(jnp.bfloat16)
        hidden = (
            jnp.einsum("yxc,cd->yxd", normed_in, w_expand, preferred_element_type=jnp.float32)
            + b_expand
        )
        hidden = gelu_tanh(hidden).astype(jnp.bfloat16)
        return jnp.where(keep[:, :, None], hidden, jnp.zeros_like(hidden))

    middle = expand(wide_in[:, 1:-1], inside[:, 1:-1])
    edges = expand(
        jnp.concatenate([wide_in[:, :1], wide_in[:, -1:]], axis=1),
        jnp.concatenate([inside[:, :1], inside[:, -1:]], axis=1),
    )
    padded = jnp.pad(middle, ((0, 0), (1, 1), (0, 0)))
    padded = lax.optimization_barrier(padded.at[:, :1].set(edges[:, :1]).at[:, -1:].set(edges[:, 1:]))
    total = jnp.zeros((tile_h, tile_w, hidden_width), jnp.float32)
    for down in range(3):
        for across in range(3):
            total = total + padded[down : down + tile_h, across : across + tile_w].astype(
                jnp.float32
            ) * dw_kernel[down, across].astype(jnp.float32)
    depth = gelu_tanh(total + dw_bias).astype(jnp.bfloat16)
    proj = jnp.dot(depth.reshape(-1, hidden_width), w_project, preferred_element_type=jnp.float32)
    mid = (latent.reshape(-1, width).astype(jnp.float32) + proj + b_project).astype(jnp.bfloat16)
    sizes = layout_sizes(tile_h, tile_w)
    plan = runs_plan(tile_h, tile_w)
    if plan is not None:
        arrived = send_runs(mid.reshape(tile_h, tile_w, width), plan)
        order = (lax.axis_size("row"), lax.axis_size("col"), plan["parts"], 1)
    else:
        arrived = send_to_owner(mid.reshape(tile_h, tile_w, width), sizes)
        order = (
            sizes["n_row"] // sizes["qr"], sizes["n_col"] // sizes["qc"], sizes["pr"], sizes["pc"]
        )
        assert sizes["qr"] == 1 or order[1] * order[2] * order[3] == 1
        assert sizes["qc"] == 1 or order[2] * order[3] == 1
        assert sizes["kr"] == 1 or order[3] == 1
    result = owner_block(arrived, ln_gain, ln_bias, w_qkv, arrived_bias(pos_bias, *order), w_out, b_out)
    if plan is not None:
        return back_runs(result, plan, tile_h, tile_w)
    return back_home(result, sizes, tile_h, tile_w)

def solution(mesh):
    return jax.shard_map(
        on_device,
        mesh=mesh,
        in_specs=(
            P("row", "col", None),
            P(),
            P(),
            P(),
            P(),
            P(),
            P(),
            P(),
            P(),
            P(),
            P(),
            P(),
            P(),
            P(),
            P(),
        ),
        out_specs=P("row", "col", None),
        check_vma=False,
    )
```
